32 devices in a mesh: home: 4 (over z), pair: 8 (over y, x, core).
Axes of the slice: x: 2, y: 2, z: 4, core: 2. Of those that a mesh axis runs over, the one named last changes fastest.
Arguments:
- orbitals: bfloat16 [64, 32768], P('home'), may hold values from -4 to 4
- offsets: int32 [64, 3], P('home'), may hold values from 0 to 16
- sends: int32 [4, 4, 1], P('home'), may hold values from 0 to 15
- pair_home: int32 [4, 8, 4], P('home', 'pair'), may hold values from 0 to 15
- pair_visit: int32 [4, 8, 4], P('home', 'pair'), may hold values from 0 to 3
- pair_count: int32 [4, 8], P('home', 'pair'), may hold values from 1 to 4, as said below
Outputs:
- fields: float32 [64, 32768], P('home', 'pair')
The draws below stay inside these ranges and needn't reach their ends.
Inputs may be any that keep to these rules, and one draw needn't show every extreme that they name: `pair_count`: slots from this number on hold no pair; some device holds 4 live pairs.
All inputs are finite; a program needn't handle non-finite values.
Results may differ from the reference program's by a relative error of at most 0.0003.
Values may be sent and summed in bfloat16 or wider, within the bound.
No kernel may reach another device: no remote copies, remote signals or barrier semaphores. Data moves between devices by JAX's collectives and lax.ppermute only.
A program may use at most 64 MiB of HBM per device.

```python
import jax
import jax.numpy as jnp
from jax import lax

B = 32
CELLS = 32768
HS = 16
C = 1
PD = 4
ORB = 64
VS = 4
N_HOME = 4
N_PAIR = 8


def draw_orbitals(key, part):
    noise_part = jnp.clip(jax.random.normal(key, (ORB, B ** 3), jnp.float32), -4.0, 4.0)
    return noise_part.astype(jnp.bfloat16)


def draw_pair_count(key, part):
    counts_low = jax.random.randint(jax.random.fold_in(key, 3), (N_HOME * N_PAIR,), 1, PD // 2 + 1)
    heavy = jax.random.randint(jax.random.fold_in(key, 5), (N_HOME * N_PAIR,), 0, 8) == 0
    flattened = jnp.where(heavy, PD, counts_low)
    busiest = jax.random.randint(jax.random.fold_in(key, 9), (), 0, N_HOME * N_PAIR)
    flattened = flattened.at[busiest].set(PD)
    return flattened.reshape(N_HOME, N_PAIR).astype(jnp.int32)


def with_ends(values, own_key, low, largest):
    extent = values.shape
    spot = [jax.random.randint(jax.random.fold_in(own_key, axis), (), 0, extent[axis]) for axis in range(len(extent))]
    values = values.at[tuple(spot)].set(low)
    longest = extent.index(max(extent))
    spot[longest] = (spot[longest] + 1) % extent[longest]
    return values.at[tuple(spot)].set(largest)


def setup_inputs(seed: int = 0) -> dict:
    arg_keys = jax.random.split(jax.random.key(seed), 7)
    return {
        "orbitals": draw_orbitals(jax.random.fold_in(arg_keys[6], 71), 0),
        "offsets": with_ends(jax.random.randint(arg_keys[1], (ORB, 3), 0, B // 2 + 1), jax.random.fold_in(arg_keys[1], 1), 0, (B // 2 + 1) - 1).astype(jnp.int32),
        "sends": with_ends(jax.random.randint(arg_keys[2], (N_HOME, N_HOME, C), 0, HS), jax.random.fold_in(arg_keys[2], 1), 0, HS - 1).astype(jnp.int32),
        "pair_home": with_ends(jax.random.randint(arg_keys[3], (N_HOME, N_PAIR, PD), 0, HS), jax.random.fold_in(arg_keys[3], 1), 0, HS - 1).astype(jnp.int32),
        "pair_visit": with_ends(jax.random.randint(arg_keys[4], (N_HOME, N_PAIR, PD), 0, VS), jax.random.fold_in(arg_keys[4], 1), 0, VS - 1).astype(jnp.int32),
        "pair_count": draw_pair_count(jax.random.fold_in(arg_keys[6], 71), 0),
    }


PRECISE = lax.Precision.HIGHEST

def sine_table():
    grid = jnp.arange(B, dtype=jnp.float32) + 1.0
    return jnp.sqrt(2.0 / (B + 1.0)) * jnp.sin(jnp.pi * grid[:, None] * grid[None, :] / (B + 1.0))

def eigen_sum():
    grid = jnp.arange(B, dtype=jnp.float32) + 1.0
    single = 2.0 - 2.0 * jnp.cos(jnp.pi * grid / (B + 1.0))
    return (single[:, None, None] + single[None, :, None] + single[None, None, :]).reshape(-1)

def shift_matrices(delta):
    rows = jnp.arange(B, dtype=jnp.int32)
    return [(rows[None, :] == rows[:, None] + delta[axis_pos]).astype(jnp.float32) for axis_pos in range(3)]

def apply_axes(values, matrices):
    for matrix in matrices:
        values = jnp.dot(matrix, values.reshape(B, B * B), precision=PRECISE)
        values = values.reshape(B, B, B).transpose(1, 2, 0).reshape(-1)
    return values

def pair_fields(home_orb, part_orb, delta, table, eigen):
    matrices = shift_matrices(delta)
    shifted = apply_axes(part_orb, matrices)
    density = home_orb * shifted
    potential = apply_axes(apply_axes(density, [table, table, table]) / eigen, [table, table, table])
    to_home = potential * shifted
    to_partner = apply_axes(potential * home_orb, [matrix.T for matrix in matrices])
    return (to_home, to_partner)

def reference(orbitals, offsets, sends, pair_home, pair_visit, pair_count):
    sections = jnp.arange(N_HOME, dtype=jnp.int32)[:, None, None]
    home_ids = (sections * HS + pair_home).reshape(-1)
    source = pair_visit // C
    slot_index = pair_visit % C
    sections_full = jnp.broadcast_to(sections, pair_visit.shape)
    part_local = sends[source, sections_full, slot_index]
    part_ids = (source * HS + part_local).reshape(-1)
    active = (jnp.arange(PD, dtype=jnp.int32)[None, None, :] < pair_count[:, :, None]).reshape(-1)
    table = sine_table()
    eigen = eigen_sum()

    def visit_pair(totals, record):
        home_id, part_id, live_flag = record
        home_orb = orbitals[home_id].astype(jnp.float32)
        part_orb = orbitals[part_id].astype(jnp.float32)
        delta = offsets[home_id] - offsets[part_id]
        to_home, to_partner = pair_fields(home_orb, part_orb, delta, table, eigen)
        weight_on = live_flag.astype(jnp.float32)
        totals = totals.at[home_id].add(weight_on * to_home)
        totals = totals.at[part_id].add(weight_on * to_partner)
        return (totals, None)
    start_totals = jnp.zeros((ORB, CELLS), jnp.float32)
    fields, _ = lax.scan(visit_pair, start_totals, (home_ids, part_ids, active))
    return fields
```

```python
import jax
import jax.numpy as jnp
from jax import lax
from jax.sharding import PartitionSpec as P

B = 32


PRECISE = lax.Precision.HIGHEST
TRANSFORM = lax.Precision.HIGHEST


def sine_table():
    grid = jnp.arange(B, dtype=jnp.float32) + 1.0
    return jnp.sqrt(2.0 / (B + 1.0)) * jnp.sin(jnp.pi * grid[:, None] * grid[None, :] / (B + 1.0))


def eigen_sum():
    grid = jnp.arange(B, dtype=jnp.float32) + 1.0
    single = 2.0 - 2.0 * jnp.cos(jnp.pi * grid / (B + 1.0))
    return single[:, None, None] + single[None, :, None] + single[None, None, :]


def shift_mats(delta):
    rows = jnp.arange(B, dtype=jnp.int32)
    target = rows[None, None, :, None] + delta[:, :, None, None]
    return (rows[None, None, None, :] == target).astype(jnp.float32)


def shift_batch(values, mats, precision):
    values = jnp.einsum("pka,pabc->pkbc", mats[:, 0], values, precision=precision)
    values = jnp.einsum("pkb,pabc->pakc", mats[:, 1], values, precision=precision)
    values = jnp.einsum("pkc,pabc->pabk", mats[:, 2], values, precision=precision)
    return values


def sine_batch(values, table):
    values = jnp.einsum("ka,pabc->pkbc", table, values, precision=TRANSFORM)
    values = jnp.einsum("kb,pabc->pakc", table, values, precision=TRANSFORM)
    values = jnp.einsum("kc,pabc->pabk", table, values, precision=TRANSFORM)
    return values


def per_device(orbitals, offsets, sends, pair_home, pair_visit, pair_count):
    home_count = orbitals.shape[0]
    cell_count = orbitals.shape[1]
    chosen = sends[0].reshape(-1)
    slot_total = chosen.shape[0]
    slots = pair_home.shape[2]
    extra = 128
    outgoing = jnp.concatenate(
        [
            orbitals[chosen],
            jnp.pad(offsets[chosen].astype(jnp.bfloat16), ((0, 0), (0, extra - 3))),
        ],
        axis=1,
    )
    arrived = lax.all_to_all(outgoing, "home", split_axis=0, concat_axis=0, tiled=True)
    visitors = arrived[:, :cell_count]
    visit_offsets = arrived[:, cell_count : cell_count + 3].astype(jnp.int32)
    table = sine_table()
    eigen = eigen_sum()

    home_slot = pair_home[0, 0]
    visit_slot = pair_visit[0, 0]
    live = (jnp.arange(slots, dtype=jnp.int32) < pair_count[0, 0]).astype(jnp.float32)
    home_orb = orbitals[home_slot].reshape(slots, B, B, B)
    part_orb = visitors[visit_slot].reshape(slots, B, B, B)
    delta = offsets[home_slot] - visit_offsets[visit_slot]
    mats = shift_mats(delta)
    shifted = shift_batch(
        part_orb.astype(jnp.float32), mats, lax.Precision.DEFAULT
    )
    home_box = home_orb.astype(jnp.float32)
    density = home_box * shifted
    potential = sine_batch(sine_batch(density, table) / eigen, table)
    to_home = potential * shifted
    to_partner = shift_batch(
        potential * home_box, jnp.swapaxes(mats, 2, 3), PRECISE
    )
    fields = jnp.concatenate([to_home, to_partner], axis=0).reshape(2 * slots, cell_count)
    rows = jnp.arange(home_count + slot_total, dtype=jnp.int32)
    targets = jnp.concatenate([home_slot, home_count + visit_slot])
    weights = jnp.concatenate([live, live])
    picker = (targets[:, None] == rows[None, :]).astype(jnp.float32) * weights[:, None]
    totals = jnp.dot(picker.T, fields, precision=PRECISE)
    totals = lax.psum_scatter(totals, "pair", scatter_dimension=1, tiled=True)
    home_totals = totals[:home_count]
    visit_totals = totals[home_count:]
    chooser = (chosen[:, None] == jnp.arange(home_count, dtype=jnp.int32)[None, :]).astype(
        jnp.float32
    )
    returned = lax.all_to_all(visit_totals, "home", split_axis=0, concat_axis=0, tiled=True)
    return home_totals + jnp.dot(chooser.T, returned, precision=PRECISE)


def solution(mesh):
    in_specs = (
        P("home", None),
        P("home", None),
        P("home", None, None),
        P("home", "pair", None),
        P("home", "pair", None),
        P("home", "pair"),
    )
    out_specs = P("home", "pair")
    return jax.shard_map(
        per_device, mesh=mesh, in_specs=in_specs, out_specs=out_specs, check_vma=False
    )
```

```python
import functools

import jax
import jax.numpy as jnp
from jax import lax
from jax.experimental import pallas as pl
from jax.experimental.pallas import tpu as pltpu
from jax.sharding import PartitionSpec as P

B = 32
PLANE = B * B


PRECISE = lax.Precision.HIGHEST


def sine_table():
    grid = jnp.arange(B, dtype=jnp.float32) + 1.0
    return jnp.sqrt(2.0 / (B + 1.0)) * jnp.sin(jnp.pi * grid[:, None] * grid[None, :] / (B + 1.0))


def eigen_sum():
    grid = jnp.arange(B, dtype=jnp.float32) + 1.0
    single = 2.0 - 2.0 * jnp.cos(jnp.pi * grid / (B + 1.0))
    return single[:, None, None] + single[None, :, None] + single[None, None, :]


def split(values):
    high = values.astype(jnp.bfloat16)
    low = (values - high.astype(jnp.float32)).astype(jnp.bfloat16)
    return high, low


def split_outside(values):
    high = lax.reduce_precision(values, exponent_bits=8, mantissa_bits=7)
    return high.astype(jnp.bfloat16), (values - high).astype(jnp.bfloat16)


def dot3(left, right_high, right_low):
    high, low = split(left)
    out = jnp.dot(high, right_high, preferred_element_type=jnp.float32)
    out = out + jnp.dot(low, right_high, preferred_element_type=jnp.float32)
    return out + jnp.dot(high, right_low, preferred_element_type=jnp.float32)


def dot3_left(left_high, left_low, right):
    high, low = split(right)
    out = jnp.dot(left_high, high, preferred_element_type=jnp.float32)
    out = out + jnp.dot(left_low, high, preferred_element_type=jnp.float32)
    return out + jnp.dot(left_high, low, preferred_element_type=jnp.float32)


def exact_rows(matrix, values):
    first = values.astype(jnp.bfloat16)
    rest = values - first.astype(jnp.float32)
    second = rest.astype(jnp.bfloat16)
    third = (rest - second.astype(jnp.float32)).astype(jnp.bfloat16)
    out = jnp.dot(matrix, first, preferred_element_type=jnp.float32)
    out = out + jnp.dot(matrix, second, preferred_element_type=jnp.float32)
    return out + jnp.dot(matrix, third, preferred_element_type=jnp.float32)


def pair_kernel(
    delta_ref,
    live_ref,
    home_ref,
    part_ref,
    kron_high_ref,
    kron_low_ref,
    rows_high_ref,
    rows_low_ref,
    eigen_ref,
    to_home_ref,
    to_partner_ref,
    shifted_ref,
    work_ref,
):
    slots = home_ref.shape[0]
    lane = lax.broadcasted_iota(jnp.int32, (B, PLANE), 1)
    lane_b = lane // B
    lane_c = lane % B
    row = lax.broadcasted_iota(jnp.int32, (B, B), 0)
    col = lax.broadcasted_iota(jnp.int32, (B, B), 1)
    for slot in range(slots):
        d_a = delta_ref[slot, 0]
        d_b = delta_ref[slot, 1]
        d_c = delta_ref[slot, 2]
        pick = (col == row + d_a).astype(jnp.bfloat16)
        moved = jnp.dot(pick, part_ref[slot], preferred_element_type=jnp.float32)
        step = d_b * B + d_c
        moved = pltpu.roll(moved, (PLANE - step) % PLANE, 1)
        inside = (
            (lane_b + d_b >= 0) & (lane_b + d_b < B) & (lane_c + d_c >= 0) & (lane_c + d_c < B)
        )
        moved = jnp.where(inside, moved, 0.0)
        shifted_ref[slot] = moved
        work_ref[slot * B : (slot + 1) * B, :] = home_ref[slot].astype(jnp.float32) * moved

    kron_high = kron_high_ref[...]
    kron_low = kron_low_ref[...]
    rows_high = rows_high_ref[...]
    rows_low = rows_low_ref[...]
    coef = dot3_left(rows_high, rows_low, dot3(work_ref[...], kron_high, kron_low))
    eigen = eigen_ref[...]
    for slot in range(slots):
        work_ref[slot * B : (slot + 1) * B, :] = coef[slot * B : (slot + 1) * B, :] / eigen
    potential = dot3_left(rows_high, rows_low, dot3(work_ref[...], kron_high, kron_low))

    for slot in range(slots):
        d_a = delta_ref[slot, 0]
        d_b = delta_ref[slot, 1]
        d_c = delta_ref[slot, 2]
        live = live_ref[slot] > 0
        here = potential[slot * B : (slot + 1) * B, :]
        to_home_ref[slot] = jnp.where(live, here * shifted_ref[slot], 0.0)
        product = here * home_ref[slot].astype(jnp.float32)
        pick = (col == row - d_a).astype(jnp.bfloat16)
        moved = exact_rows(pick, product)
        step = d_b * B + d_c
        moved = pltpu.roll(moved, (PLANE + step) % PLANE, 1)
        inside = (
            (lane_b - d_b >= 0) & (lane_b - d_b < B) & (lane_c - d_c >= 0) & (lane_c - d_c < B)
        )
        to_partner_ref[slot] = jnp.where(live & inside, moved, 0.0)


def pair_fields(delta, live, home, part):
    slots = home.shape[0]
    table = sine_table()
    kron_high, kron_low = split_outside(jnp.kron(table, table))
    rows_high, rows_low = split_outside(jnp.kron(jnp.eye(slots, dtype=jnp.float32), table))
    eigen = eigen_sum().reshape(B, PLANE)
    smem = pl.BlockSpec(memory_space=pltpu.SMEM)
    vmem = pl.BlockSpec(memory_space=pltpu.VMEM)
    box = jax.ShapeDtypeStruct((slots, B, PLANE), jnp.float32)
    return pl.pallas_call(
        pair_kernel,
        out_shape=(box, box),
        in_specs=[smem, smem] + [vmem] * 7,
        out_specs=(vmem, vmem),
        scratch_shapes=[
            pltpu.VMEM((slots, B, PLANE), jnp.float32),
            pltpu.VMEM((slots * B, PLANE), jnp.float32),
        ],
    )(delta, live, home, part, kron_high, kron_low, rows_high, rows_low, eigen)


def per_device(orbitals, offsets, sends, pair_home, pair_visit, pair_count):
    home_count = orbitals.shape[0]
    cell_count = orbitals.shape[1]
    chosen = sends[0].reshape(-1)
    slot_total = chosen.shape[0]
    slots = pair_home.shape[2]
    extra = 128
    outgoing = jnp.concatenate(
        [
            orbitals[chosen],
            jnp.pad(offsets[chosen].astype(jnp.bfloat16), ((0, 0), (0, extra - 3))),
        ],
        axis=1,
    )
    arrived = lax.all_to_all(outgoing, "home", split_axis=0, concat_axis=0, tiled=True)
    visitors = arrived[:, :cell_count]
    visit_offsets = arrived[:, cell_count : cell_count + 3].astype(jnp.int32)

    home_slot = pair_home[0, 0]
    visit_slot = pair_visit[0, 0]
    live = (jnp.arange(slots, dtype=jnp.int32) < pair_count[0, 0]).astype(jnp.int32)
    home_orb = orbitals[home_slot].reshape(slots, B, PLANE)
    part_orb = visitors[visit_slot].reshape(slots, B, PLANE)
    delta = offsets[home_slot] - visit_offsets[visit_slot]
    to_home, to_partner = pair_fields(delta, live, home_orb, part_orb)

    fields = jnp.concatenate([to_home, to_partner], axis=0).reshape(2 * slots, cell_count)
    rows = jnp.arange(home_count + slot_total, dtype=jnp.int32)
    targets = jnp.concatenate([home_slot, home_count + visit_slot])
    picker = (targets[:, None] == rows[None, :]).astype(jnp.float32)
    totals = jnp.dot(picker.T, fields, precision=PRECISE)
    totals = lax.psum_scatter(totals, "pair", scatter_dimension=1, tiled=True)
    home_totals = totals[:home_count]
    visit_totals = totals[home_count:]
    chooser = (chosen[:, None] == jnp.arange(home_count, dtype=jnp.int32)[None, :]).astype(
        jnp.float32
    )
    returned = lax.all_to_all(visit_totals, "home", split_axis=0, concat_axis=0, tiled=True)
    return home_totals + jnp.dot(chooser.T, returned, precision=PRECISE)


def solution(mesh):
    in_specs = (
        P("home", None),
        P("home", None),
        P("home", None, None),
        P("home", "pair", None),
        P("home", "pair", None),
        P("home", "pair"),
    )
    out_specs = P("home", "pair")
    return jax.shard_map(
        per_device, mesh=mesh, in_specs=in_specs, out_specs=out_specs, check_vma=False
    )
```

```python
import functools

import jax
import jax.numpy as jnp
import ml_dtypes
import numpy as np
from jax import lax
from jax.experimental import pallas as pl
from jax.experimental.pallas import tpu as pltpu
from jax.sharding import PartitionSpec as P

B = 32
PLANE = B * B


PRECISE = lax.Precision.HIGHEST


def sine_table():
    grid = jnp.arange(B, dtype=jnp.float32) + 1.0
    return jnp.sqrt(2.0 / (B + 1.0)) * jnp.sin(jnp.pi * grid[:, None] * grid[None, :] / (B + 1.0))


def eigen_sum():
    grid = jnp.arange(B, dtype=jnp.float32) + 1.0
    single = 2.0 - 2.0 * jnp.cos(jnp.pi * grid / (B + 1.0))
    return single[:, None, None] + single[None, :, None] + single[None, None, :]


def host_tables(slots):
    grid = np.arange(B, dtype=np.float32) + np.float32(1.0)
    angle = np.float32(np.pi) * grid[:, None] * grid[None, :] / np.float32(B + 1.0)
    table = (np.sqrt(np.float32(2.0 / (B + 1.0))) * np.sin(angle)).astype(np.float32)
    tiled = np.tile(table, (1, B))
    spread = np.repeat(table, B, axis=1)
    rows = np.kron(np.eye(slots, dtype=np.float32), table).astype(np.float32)
    rows_high = rows.astype(ml_dtypes.bfloat16)
    rows_low = (rows - rows_high.astype(np.float32)).astype(ml_dtypes.bfloat16)
    single = (np.float32(2.0) - np.float32(2.0) * np.cos(np.float32(np.pi) * grid / np.float32(B + 1.0))).astype(np.float32)
    eigen = (single[:, None, None] + single[None, :, None] + single[None, None, :]).reshape(B, PLANE)
    return tiled, spread, rows_high, rows_low, eigen.astype(np.float32)


def split(values):
    high = values.astype(jnp.bfloat16)
    low = (values - high.astype(jnp.float32)).astype(jnp.bfloat16)
    return high, low


def split_outside(values):
    high = lax.reduce_precision(values, exponent_bits=8, mantissa_bits=7)
    return high.astype(jnp.bfloat16), (values - high).astype(jnp.bfloat16)


def dot3(left, right_high, right_low):
    high, low = split(left)
    out = jnp.dot(high, right_high, preferred_element_type=jnp.float32)
    out = out + jnp.dot(low, right_high, preferred_element_type=jnp.float32)
    return out + jnp.dot(high, right_low, preferred_element_type=jnp.float32)


def dot3_left(left_high, left_low, right):
    high, low = split(right)
    out = jnp.dot(left_high, high, preferred_element_type=jnp.float32)
    out = out + jnp.dot(left_low, high, preferred_element_type=jnp.float32)
    return out + jnp.dot(left_high, low, preferred_element_type=jnp.float32)


def exact_rows(matrix, values):
    first = values.astype(jnp.bfloat16)
    rest = values - first.astype(jnp.float32)
    second = rest.astype(jnp.bfloat16)
    third = (rest - second.astype(jnp.float32)).astype(jnp.bfloat16)
    out = jnp.dot(matrix, first, preferred_element_type=jnp.float32)
    out = out + jnp.dot(matrix, second, preferred_element_type=jnp.float32)
    return out + jnp.dot(matrix, third, preferred_element_type=jnp.float32)


def pair_kernel(
    delta_ref,
    live_ref,
    home_ref,
    part_ref,
    tiled_ref,
    spread_ref,
    rows_high_ref,
    rows_low_ref,
    eigen_ref,
    to_home_ref,
    to_partner_ref,
    shifted_ref,
    work_ref,
    kron_high_ref,
    kron_low_ref,
):
    slots = home_ref.shape[0]
    tiled = tiled_ref[...]
    for block in range(B):
        values = tiled * spread_ref[block : block + 1, :]
        high = values.astype(jnp.bfloat16)
        kron_high_ref[block * B : (block + 1) * B, :] = high
        kron_low_ref[block * B : (block + 1) * B, :] = (
            values - high.astype(jnp.float32)
        ).astype(jnp.bfloat16)
    lane = lax.broadcasted_iota(jnp.int32, (B, PLANE), 1)
    lane_b = lane // B
    lane_c = lane % B
    row = lax.broadcasted_iota(jnp.int32, (B, B), 0)
    col = lax.broadcasted_iota(jnp.int32, (B, B), 1)
    for slot in range(slots):
        d_a = delta_ref[slot, 0]
        d_b = delta_ref[slot, 1]
        d_c = delta_ref[slot, 2]
        pick = (col == row + d_a).astype(jnp.bfloat16)
        moved = jnp.dot(pick, part_ref[slot], preferred_element_type=jnp.float32)
        step = d_b * B + d_c
        moved = pltpu.roll(moved, (PLANE - step) % PLANE, 1)
        inside = (
            (lane_b + d_b >= 0) & (lane_b + d_b < B) & (lane_c + d_c >= 0) & (lane_c + d_c < B)
        )
        moved = jnp.where(inside, moved, 0.0)
        shifted_ref[slot] = moved
        work_ref[slot * B : (slot + 1) * B, :] = home_ref[slot].astype(jnp.float32) * moved

    kron_high = kron_high_ref[...]
    kron_low = kron_low_ref[...]
    rows_high = rows_high_ref[...]
    rows_low = rows_low_ref[...]
    coef = dot3_left(rows_high, rows_low, dot3(work_ref[...], kron_high, kron_low))
    eigen = eigen_ref[...]
    for slot in range(slots):
        work_ref[slot * B : (slot + 1) * B, :] = coef[slot * B : (slot + 1) * B, :] / eigen
    potential = dot3_left(rows_high, rows_low, dot3(work_ref[...], kron_high, kron_low))

    for slot in range(slots):
        d_a = delta_ref[slot, 0]
        d_b = delta_ref[slot, 1]
        d_c = delta_ref[slot, 2]
        live = live_ref[slot] > 0
        here = potential[slot * B : (slot + 1) * B, :]
        to_home_ref[slot] = jnp.where(live, here * shifted_ref[slot], 0.0)
        product = here * home_ref[slot].astype(jnp.float32)
        pick = (col == row - d_a).astype(jnp.bfloat16)
        moved = exact_rows(pick, product)
        step = d_b * B + d_c
        moved = pltpu.roll(moved, (PLANE + step) % PLANE, 1)
        inside = (
            (lane_b - d_b >= 0) & (lane_b - d_b < B) & (lane_c - d_c >= 0) & (lane_c - d_c < B)
        )
        to_partner_ref[slot] = jnp.where(live & inside, moved, 0.0)


def pair_fields(delta, live, home, part):
    slots = home.shape[0]
    tiled, spread, rows_high, rows_low, eigen = host_tables(slots)
    smem = pl.BlockSpec(memory_space=pltpu.SMEM)
    vmem = pl.BlockSpec(memory_space=pltpu.VMEM)
    box = jax.ShapeDtypeStruct((slots, B, PLANE), jnp.float32)
    return pl.pallas_call(
        pair_kernel,
        out_shape=(box, box),
        in_specs=[smem, smem] + [vmem] * 7,
        out_specs=(vmem, vmem),
        scratch_shapes=[
            pltpu.VMEM((slots, B, PLANE), jnp.float32),
            pltpu.VMEM((slots * B, PLANE), jnp.float32),
            pltpu.VMEM((PLANE, PLANE), jnp.bfloat16),
            pltpu.VMEM((PLANE, PLANE), jnp.bfloat16),
        ],
    )(delta, live, home, part, tiled, spread, rows_high, rows_low, eigen)


def per_device(orbitals, offsets, sends, pair_home, pair_visit, pair_count):
    home_count = orbitals.shape[0]
    cell_count = orbitals.shape[1]
    chosen = sends[0].reshape(-1)
    slot_total = chosen.shape[0]
    slots = pair_home.shape[2]
    extra = 128
    outgoing = jnp.concatenate(
        [
            orbitals[chosen],
            jnp.pad(offsets[chosen].astype(jnp.bfloat16), ((0, 0), (0, extra - 3))),
        ],
        axis=1,
    )
    arrived = lax.all_to_all(outgoing, "home", split_axis=0, concat_axis=0, tiled=True)
    visitors = arrived[:, :cell_count]
    visit_offsets = arrived[:, cell_count : cell_count + 3].astype(jnp.int32)

    home_slot = pair_home[0, 0]
    visit_slot = pair_visit[0, 0]
    live = (jnp.arange(slots, dtype=jnp.int32) < pair_count[0, 0]).astype(jnp.int32)
    home_orb = orbitals[home_slot].reshape(slots, B, PLANE)
    part_orb = visitors[visit_slot].reshape(slots, B, PLANE)
    delta = offsets[home_slot] - visit_offsets[visit_slot]
    to_home, to_partner = pair_fields(delta, live, home_orb, part_orb)

    fields = jnp.concatenate([to_home, to_partner], axis=0).reshape(2 * slots, cell_count)
    rows = jnp.arange(home_count + slot_total, dtype=jnp.int32)
    targets = jnp.concatenate([home_slot, home_count + visit_slot])
    picker = (targets[:, None] == rows[None, :]).astype(jnp.float32)
    totals = jnp.dot(picker.T, fields, precision=PRECISE)
    totals = lax.psum_scatter(totals, "pair", scatter_dimension=1, tiled=True)
    home_totals = totals[:home_count]
    visit_totals = totals[home_count:]
    chooser = (chosen[:, None] == jnp.arange(home_count, dtype=jnp.int32)[None, :]).astype(
        jnp.float32
    )
    returned = lax.all_to_all(visit_totals, "home", split_axis=0, concat_axis=0, tiled=True)
    return home_totals + jnp.dot(chooser.T, returned, precision=PRECISE)


def solution(mesh):
    in_specs = (
        P("home", None),
        P("home", None),
        P("home", None, None),
        P("home", "pair", None),
        P("home", "pair", None),
        P("home", "pair"),
    )
    out_specs = P("home", "pair")
    return jax.shard_map(
        per_device, mesh=mesh, in_specs=in_specs, out_specs=out_specs, check_vma=False
    )
```

```python
import functools

import jax
import jax.numpy as jnp
import ml_dtypes
import numpy as np
from jax import lax
from jax.experimental import pallas as pl
from jax.experimental.pallas import tpu as pltpu
from jax.sharding import PartitionSpec as P

B = 32
PLANE = B * B


PRECISE = lax.Precision.HIGHEST


def sine_table():
    grid = jnp.arange(B, dtype=jnp.float32) + 1.0
    return jnp.sqrt(2.0 / (B + 1.0)) * jnp.sin(jnp.pi * grid[:, None] * grid[None, :] / (B + 1.0))


def eigen_sum():
    grid = jnp.arange(B, dtype=jnp.float32) + 1.0
    single = 2.0 - 2.0 * jnp.cos(jnp.pi * grid / (B + 1.0))
    return single[:, None, None] + single[None, :, None] + single[None, None, :]


def host_tables(slots):
    grid = np.arange(B, dtype=np.float32) + np.float32(1.0)
    angle = np.float32(np.pi) * grid[:, None] * grid[None, :] / np.float32(B + 1.0)
    table = (np.sqrt(np.float32(2.0 / (B + 1.0))) * np.sin(angle)).astype(np.float32)
    tiled = np.tile(table, (1, B))
    spread = np.repeat(table, B, axis=1)
    rows = np.kron(np.eye(slots, dtype=np.float32), table).astype(np.float32)
    rows_high = rows.astype(ml_dtypes.bfloat16)
    rows_low = (rows - rows_high.astype(np.float32)).astype(ml_dtypes.bfloat16)
    single = (np.float32(2.0) - np.float32(2.0) * np.cos(np.float32(np.pi) * grid / np.float32(B + 1.0))).astype(np.float32)
    eigen = (single[:, None, None] + single[None, :, None] + single[None, None, :]).reshape(B, PLANE)
    return tiled, spread, rows_high, rows_low, eigen.astype(np.float32)


def split(values):
    high = values.astype(jnp.bfloat16)
    low = (values - high.astype(jnp.float32)).astype(jnp.bfloat16)
    return high, low


def split_outside(values):
    high = lax.reduce_precision(values, exponent_bits=8, mantissa_bits=7)
    return high.astype(jnp.bfloat16), (values - high).astype(jnp.bfloat16)


def dot3(left, right_high, right_low):
    high, low = split(left)
    out = jnp.dot(high, right_high, preferred_element_type=jnp.float32)
    out = out + jnp.dot(low, right_high, preferred_element_type=jnp.float32)
    return out + jnp.dot(high, right_low, preferred_element_type=jnp.float32)


def dot3_left(left_high, left_low, right):
    high, low = split(right)
    out = jnp.dot(left_high, high, preferred_element_type=jnp.float32)
    out = out + jnp.dot(left_low, high, preferred_element_type=jnp.float32)
    return out + jnp.dot(left_high, low, preferred_element_type=jnp.float32)


def exact_rows(matrix, values):
    first = values.astype(jnp.bfloat16)
    rest = values - first.astype(jnp.float32)
    second = rest.astype(jnp.bfloat16)
    third = (rest - second.astype(jnp.float32)).astype(jnp.bfloat16)
    out = jnp.dot(matrix, first, preferred_element_type=jnp.float32)
    out = out + jnp.dot(matrix, second, preferred_element_type=jnp.float32)
    return out + jnp.dot(matrix, third, preferred_element_type=jnp.float32)


def pair_kernel(
    delta_ref,
    live_ref,
    home_ref,
    part_ref,
    tiled_ref,
    spread_ref,
    rows_high_ref,
    rows_low_ref,
    eigen_ref,
    to_home_ref,
    to_partner_ref,
    shifted_ref,
    work_ref,
    kron_high_ref,
    kron_low_ref,
):
    slots = home_ref.shape[0]
    tiled = tiled_ref[...]
    for block in range(B):
        values = tiled * spread_ref[block : block + 1, :]
        high = values.astype(jnp.bfloat16)
        kron_high_ref[block * B : (block + 1) * B, :] = high
        kron_low_ref[block * B : (block + 1) * B, :] = (
            values - high.astype(jnp.float32)
        ).astype(jnp.bfloat16)
    lane = lax.broadcasted_iota(jnp.int32, (B, PLANE), 1)
    lane_b = lane // B
    lane_c = lane % B
    row = lax.broadcasted_iota(jnp.int32, (B, B), 0)
    col = lax.broadcasted_iota(jnp.int32, (B, B), 1)
    for slot in range(slots):
        d_a = delta_ref[slot, 0]
        d_b = delta_ref[slot, 1]
        d_c = delta_ref[slot, 2]
        pick = (col == row + d_a).astype(jnp.bfloat16)
        moved = jnp.dot(pick, part_ref[slot], preferred_element_type=jnp.float32)
        step = d_b * B + d_c
        moved = pltpu.roll(moved, (PLANE - step) % PLANE, 1)
        inside = (
            (lane_b + d_b >= 0) & (lane_b + d_b < B) & (lane_c + d_c >= 0) & (lane_c + d_c < B)
        )
        moved = jnp.where(inside, moved, 0.0)
        shifted_ref[slot] = moved
        work_ref[slot * B : (slot + 1) * B, :] = home_ref[slot].astype(jnp.float32) * moved

    kron_high = kron_high_ref[...]
    kron_low = kron_low_ref[...]
    rows_high = rows_high_ref[...]
    rows_low = rows_low_ref[...]
    coef = dot3_left(rows_high, rows_low, dot3(work_ref[...], kron_high, kron_low))
    eigen = eigen_ref[...]
    for slot in range(slots):
        work_ref[slot * B : (slot + 1) * B, :] = coef[slot * B : (slot + 1) * B, :] / eigen
    potential = dot3_left(rows_high, rows_low, dot3(work_ref[...], kron_high, kron_low))

    for slot in range(slots):
        d_a = delta_ref[slot, 0]
        d_b = delta_ref[slot, 1]
        d_c = delta_ref[slot, 2]
        live = live_ref[slot] > 0
        here = potential[slot * B : (slot + 1) * B, :]
        to_home_ref[slot] = jnp.where(live, here * shifted_ref[slot], 0.0)
        product = here * home_ref[slot].astype(jnp.float32)
        pick = (col == row - d_a).astype(jnp.bfloat16)
        moved = exact_rows(pick, product)
        step = d_b * B + d_c
        moved = pltpu.roll(moved, (PLANE + step) % PLANE, 1)
        inside = (
            (lane_b - d_b >= 0) & (lane_b - d_b < B) & (lane_c - d_c >= 0) & (lane_c - d_c < B)
        )
        to_partner_ref[slot] = jnp.where(live & inside, moved, 0.0)


def pair_fields(delta, live, home, part):
    slots = home.shape[0]
    tiled, spread, rows_high, rows_low, eigen = host_tables(slots)
    smem = pl.BlockSpec(memory_space=pltpu.SMEM)
    vmem = pl.BlockSpec(memory_space=pltpu.VMEM)
    box = jax.ShapeDtypeStruct((slots, B, PLANE), jnp.float32)
    return pl.pallas_call(
        pair_kernel,
        out_shape=(box, box),
        in_specs=[smem, smem] + [vmem] * 7,
        out_specs=(vmem, vmem),
        scratch_shapes=[
            pltpu.VMEM((slots, B, PLANE), jnp.float32),
            pltpu.VMEM((slots * B, PLANE), jnp.float32),
            pltpu.VMEM((PLANE, PLANE), jnp.bfloat16),
            pltpu.VMEM((PLANE, PLANE), jnp.bfloat16),
        ],
    )(delta, live, home, part, tiled, spread, rows_high, rows_low, eigen)


def per_device(orbitals, offsets, sends, pair_home, pair_visit, pair_count):
    home_count = orbitals.shape[0]
    cell_count = orbitals.shape[1]
    chosen = sends[0].reshape(-1)
    slot_total = chosen.shape[0]
    slots = pair_home.shape[2]
    extra = 128
    outgoing = jnp.concatenate(
        [
            orbitals[chosen],
            jnp.pad(offsets[chosen].astype(jnp.bfloat16), ((0, 0), (0, extra - 3))),
        ],
        axis=1,
    )
    arrived = lax.all_to_all(outgoing, "home", split_axis=0, concat_axis=0, tiled=True)
    visitors = arrived[:, :cell_count]
    visit_offsets = arrived[:, cell_count : cell_count + 3].astype(jnp.int32)

    home_slot = pair_home[0, 0]
    visit_slot = pair_visit[0, 0]
    live = (jnp.arange(slots, dtype=jnp.int32) < pair_count[0, 0]).astype(jnp.int32)
    home_orb = orbitals[home_slot].reshape(slots, B, PLANE)
    part_orb = visitors[visit_slot].reshape(slots, B, PLANE)
    delta = offsets[home_slot] - visit_offsets[visit_slot]
    to_home, to_partner = pair_fields(delta, live, home_orb, part_orb)

    rows_out = 2 * slots
    fields = jnp.concatenate([to_home, to_partner], axis=0).reshape(rows_out, cell_count)
    pair_total = lax.psum(1, "pair")
    chunk = cell_count // pair_total
    targets = jnp.concatenate([home_slot, home_count + visit_slot]).astype(jnp.float32)
    body = fields.reshape(rows_out, pair_total, chunk).transpose(1, 0, 2)
    tags = jnp.broadcast_to(targets[None, :, None], (pair_total, rows_out, extra))
    payload = jnp.concatenate([body, tags], axis=2)
    got = lax.all_to_all(payload, "pair", split_axis=0, concat_axis=0, tiled=True)
    got_ids = got[:, :, chunk].astype(jnp.int32)
    all_rows = jnp.arange(home_count + slot_total, dtype=jnp.int32)
    picker = (got_ids[:, :, None] == all_rows[None, None, :]).astype(jnp.float32)
    totals = jnp.einsum("srk,srl->kl", picker, got[:, :, :chunk], precision=PRECISE)
    home_totals = totals[:home_count]
    visit_totals = totals[home_count:]
    chooser = (chosen[:, None] == jnp.arange(home_count, dtype=jnp.int32)[None, :]).astype(
        jnp.float32
    )
    returned = lax.all_to_all(visit_totals, "home", split_axis=0, concat_axis=0, tiled=True)
    return home_totals + jnp.dot(chooser.T, returned, precision=PRECISE)


def solution(mesh):
    in_specs = (
        P("home", None),
        P("home", None),
        P("home", None, None),
        P("home", "pair", None),
        P("home", "pair", None),
        P("home", "pair"),
    )
    out_specs = P("home", "pair")
    return jax.shard_map(
        per_device, mesh=mesh, in_specs=in_specs, out_specs=out_specs, check_vma=False
    )
```

```python
import functools

import jax
import jax.numpy as jnp
import ml_dtypes
import numpy as np
from jax import lax
from jax.experimental import pallas as pl
from jax.experimental.pallas import tpu as pltpu
from jax.sharding import PartitionSpec as P

B = 32
PLANE = B * B


PRECISE = lax.Precision.HIGHEST


def sine_table():
    grid = jnp.arange(B, dtype=jnp.float32) + 1.0
    return jnp.sqrt(2.0 / (B + 1.0)) * jnp.sin(jnp.pi * grid[:, None] * grid[None, :] / (B + 1.0))


def eigen_sum():
    grid = jnp.arange(B, dtype=jnp.float32) + 1.0
    single = 2.0 - 2.0 * jnp.cos(jnp.pi * grid / (B + 1.0))
    return single[:, None, None] + single[None, :, None] + single[None, None, :]


def host_tables(slots):
    grid = np.arange(B, dtype=np.float32) + np.float32(1.0)
    angle = np.float32(np.pi) * grid[:, None] * grid[None, :] / np.float32(B + 1.0)
    table = (np.sqrt(np.float32(2.0 / (B + 1.0))) * np.sin(angle)).astype(np.float32)
    tiled = np.tile(table, (1, B))
    spread = np.repeat(table, B, axis=1)
    rows = np.kron(np.eye(slots, dtype=np.float32), table).astype(np.float32)
    rows_high = rows.astype(ml_dtypes.bfloat16)
    rows_low = (rows - rows_high.astype(np.float32)).astype(ml_dtypes.bfloat16)
    single = (np.float32(2.0) - np.float32(2.0) * np.cos(np.float32(np.pi) * grid / np.float32(B + 1.0))).astype(np.float32)
    eigen = (single[:, None, None] + single[None, :, None] + single[None, None, :]).reshape(B, PLANE)
    return tiled, spread, rows_high, rows_low, eigen.astype(np.float32)


def split(values):
    high = values.astype(jnp.bfloat16)
    low = (values - high.astype(jnp.float32)).astype(jnp.bfloat16)
    return high, low


def split_outside(values):
    high = lax.reduce_precision(values, exponent_bits=8, mantissa_bits=7)
    return high.astype(jnp.bfloat16), (values - high).astype(jnp.bfloat16)


def dot3(left, right_high, right_low):
    high, low = split(left)
    out = jnp.dot(high, right_high, preferred_element_type=jnp.float32)
    out = out + jnp.dot(low, right_high, preferred_element_type=jnp.float32)
    return out + jnp.dot(high, right_low, preferred_element_type=jnp.float32)


def dot3_left(left_high, left_low, right):
    high, low = split(right)
    out = jnp.dot(left_high, high, preferred_element_type=jnp.float32)
    out = out + jnp.dot(left_low, high, preferred_element_type=jnp.float32)
    return out + jnp.dot(left_high, low, preferred_element_type=jnp.float32)


def exact_rows(matrix, values):
    first = values.astype(jnp.bfloat16)
    rest = values - first.astype(jnp.float32)
    second = rest.astype(jnp.bfloat16)
    third = (rest - second.astype(jnp.float32)).astype(jnp.bfloat16)
    out = jnp.dot(matrix, first, preferred_element_type=jnp.float32)
    out = out + jnp.dot(matrix, second, preferred_element_type=jnp.float32)
    return out + jnp.dot(matrix, third, preferred_element_type=jnp.float32)


def pair_kernel(
    delta_ref,
    live_ref,
    home_ref,
    part_ref,
    tiled_ref,
    spread_ref,
    rows_high_ref,
    rows_low_ref,
    eigen_ref,
    to_home_ref,
    to_partner_ref,
    shifted_ref,
    work_ref,
    kron_high_ref,
    kron_low_ref,
):
    slots = home_ref.shape[0]
    tiled = tiled_ref[...]
    for block in range(B):
        values = tiled * spread_ref[block : block + 1, :]
        high = values.astype(jnp.bfloat16)
        kron_high_ref[block * B : (block + 1) * B, :] = high
        kron_low_ref[block * B : (block + 1) * B, :] = (
            values - high.astype(jnp.float32)
        ).astype(jnp.bfloat16)
    lane = lax.broadcasted_iota(jnp.int32, (B, PLANE), 1)
    lane_b = lane // B
    lane_c = lane % B
    row = lax.broadcasted_iota(jnp.int32, (B, B), 0)
    col = lax.broadcasted_iota(jnp.int32, (B, B), 1)
    for slot in range(slots):
        d_a = delta_ref[slot, 0]
        d_b = delta_ref[slot, 1]
        d_c = delta_ref[slot, 2]
        pick = (col == row + d_a).astype(jnp.bfloat16)
        moved = jnp.dot(pick, part_ref[slot], preferred_element_type=jnp.float32)
        step = d_b * B + d_c
        moved = pltpu.roll(moved, (PLANE - step) % PLANE, 1)
        inside = (
            (lane_b + d_b >= 0) & (lane_b + d_b < B) & (lane_c + d_c >= 0) & (lane_c + d_c < B)
        )
        moved = jnp.where(inside, moved, 0.0)
        shifted_ref[slot] = moved
        work_ref[slot * B : (slot + 1) * B, :] = home_ref[slot].astype(jnp.float32) * moved

    kron_high = kron_high_ref[...]
    kron_low = kron_low_ref[...]
    rows_high = rows_high_ref[...]
    rows_low = rows_low_ref[...]
    coef = dot3_left(rows_high, rows_low, dot3(work_ref[...], kron_high, kron_low))
    eigen = eigen_ref[...]
    for slot in range(slots):
        work_ref[slot * B : (slot + 1) * B, :] = coef[slot * B : (slot + 1) * B, :] / eigen
    potential = dot3_left(rows_high, rows_low, dot3(work_ref[...], kron_high, kron_low))

    for slot in range(slots):
        d_a = delta_ref[slot, 0]
        d_b = delta_ref[slot, 1]
        d_c = delta_ref[slot, 2]
        live = live_ref[slot] > 0
        here = potential[slot * B : (slot + 1) * B, :]
        to_home_ref[slot] = jnp.where(live, here * shifted_ref[slot], 0.0)
        product = here * home_ref[slot].astype(jnp.float32)
        pick = (col == row - d_a).astype(jnp.bfloat16)
        moved = exact_rows(pick, product)
        step = d_b * B + d_c
        moved = pltpu.roll(moved, (PLANE + step) % PLANE, 1)
        inside = (
            (lane_b - d_b >= 0) & (lane_b - d_b < B) & (lane_c - d_c >= 0) & (lane_c - d_c < B)
        )
        to_partner_ref[slot] = jnp.where(live & inside, moved, 0.0)


def pair_fields(delta, live, home, part):
    slots = home.shape[0]
    tiled, spread, rows_high, rows_low, eigen = host_tables(slots)
    smem = pl.BlockSpec(memory_space=pltpu.SMEM)
    vmem = pl.BlockSpec(memory_space=pltpu.VMEM)
    box = jax.ShapeDtypeStruct((slots, B, PLANE), jnp.float32)
    return pl.pallas_call(
        pair_kernel,
        out_shape=(box, box),
        in_specs=[smem, smem] + [vmem] * 7,
        out_specs=(vmem, vmem),
        scratch_shapes=[
            pltpu.VMEM((slots, B, PLANE), jnp.float32),
            pltpu.VMEM((slots * B, PLANE), jnp.float32),
            pltpu.VMEM((PLANE, PLANE), jnp.bfloat16),
            pltpu.VMEM((PLANE, PLANE), jnp.bfloat16),
        ],
    )(delta, live, home, part, tiled, spread, rows_high, rows_low, eigen)


def exchange(blocks, axis):
    count = blocks.shape[0]
    received = [blocks[0]]
    for step in range(1, count):
        pairs = [(source, (source + step) % count) for source in range(count)]
        received.append(lax.ppermute(blocks[step], axis, pairs))
    return jnp.stack(received)


def per_device(orbitals, offsets, sends, pair_home, pair_visit, pair_count):
    home_count = orbitals.shape[0]
    cell_count = orbitals.shape[1]
    section_total = sends.shape[1]
    per_target = sends.shape[2]
    slot_total = section_total * per_target
    slots = pair_home.shape[2]
    extra = 128
    me = lax.axis_index("home")
    ahead = (me + jnp.arange(section_total, dtype=jnp.int32)) % section_total
    chosen = sends[0][ahead]
    flat_chosen = chosen.reshape(-1)
    outgoing = jnp.concatenate(
        [
            orbitals[flat_chosen],
            jnp.pad(offsets[flat_chosen].astype(jnp.bfloat16), ((0, 0), (0, extra - 3))),
        ],
        axis=1,
    ).reshape(section_total, per_target, cell_count + extra)
    arrived = exchange(outgoing, "home").reshape(slot_total, cell_count + extra)
    visitors = arrived[:, :cell_count]
    visit_offsets = arrived[:, cell_count : cell_count + 3].astype(jnp.int32)

    home_slot = pair_home[0, 0]
    visit_code = pair_visit[0, 0]
    source = visit_code // per_target
    visit_slot = ((me - source) % section_total) * per_target + visit_code % per_target
    live = (jnp.arange(slots, dtype=jnp.int32) < pair_count[0, 0]).astype(jnp.int32)
    home_orb = orbitals[home_slot].reshape(slots, B, PLANE)
    part_orb = visitors[visit_slot].reshape(slots, B, PLANE)
    delta = offsets[home_slot] - visit_offsets[visit_slot]
    to_home, to_partner = pair_fields(delta, live, home_orb, part_orb)

    rows_out = 2 * slots
    fields = jnp.concatenate([to_home, to_partner], axis=0).reshape(rows_out, cell_count)
    pair_total = lax.psum(1, "pair")
    chunk = cell_count // pair_total
    pair_me = lax.axis_index("pair")
    targets = jnp.concatenate([home_slot, home_count + visit_slot]).astype(jnp.float32)
    body = fields.reshape(rows_out, pair_total, chunk).transpose(1, 0, 2)
    body = body[(pair_me + jnp.arange(pair_total, dtype=jnp.int32)) % pair_total]
    tags = jnp.broadcast_to(targets[None, :, None], (pair_total, rows_out, extra))
    payload = jnp.concatenate([body, tags], axis=2)
    got = exchange(payload, "pair")
    got_ids = got[:, :, chunk].astype(jnp.int32)
    all_rows = jnp.arange(home_count + slot_total, dtype=jnp.int32)
    picker = (got_ids[:, :, None] == all_rows[None, None, :]).astype(jnp.float32)
    totals = jnp.einsum("srk,srl->kl", picker, got[:, :, :chunk], precision=PRECISE)
    home_totals = totals[:home_count]
    back = (-jnp.arange(section_total, dtype=jnp.int32)) % section_total
    back_rows = (back[:, None] * per_target + jnp.arange(per_target)[None, :]).reshape(-1)
    visit_totals = totals[home_count:][back_rows].reshape(section_total, per_target, chunk)
    returned = exchange(visit_totals, "home").reshape(slot_total, chunk)
    owners = chosen[back].reshape(-1)
    chooser = (owners[:, None] == jnp.arange(home_count, dtype=jnp.int32)[None, :]).astype(
        jnp.float32
    )
    return home_totals + jnp.dot(chooser.T, returned, precision=PRECISE)


def solution(mesh):
    in_specs = (
        P("home", None),
        P("home", None),
        P("home", None, None),
        P("home", "pair", None),
        P("home", "pair", None),
        P("home", "pair"),
    )
    out_specs = P("home", "pair")
    return jax.shard_map(
        per_device, mesh=mesh, in_specs=in_specs, out_specs=out_specs, check_vma=False
    )
```

```python
import functools

import jax
import jax.numpy as jnp
import ml_dtypes
import numpy as np
from jax import lax
from jax.experimental import pallas as pl
from jax.experimental.pallas import tpu as pltpu
from jax.sharding import PartitionSpec as P

B = 32
PLANE = B * B


PRECISE = lax.Precision.HIGHEST


def sine_table():
    grid = jnp.arange(B, dtype=jnp.float32) + 1.0
    return jnp.sqrt(2.0 / (B + 1.0)) * jnp.sin(jnp.pi * grid[:, None] * grid[None, :] / (B + 1.0))


def eigen_sum():
    grid = jnp.arange(B, dtype=jnp.float32) + 1.0
    single = 2.0 - 2.0 * jnp.cos(jnp.pi * grid / (B + 1.0))
    return single[:, None, None] + single[None, :, None] + single[None, None, :]


def host_tables(slots):
    grid = np.arange(B, dtype=np.float32) + np.float32(1.0)
    angle = np.float32(np.pi) * grid[:, None] * grid[None, :] / np.float32(B + 1.0)
    table = (np.sqrt(np.float32(2.0 / (B + 1.0))) * np.sin(angle)).astype(np.float32)
    tiled = np.tile(table, (1, B))
    spread = np.repeat(table, B, axis=1)
    rows = np.kron(np.eye(slots, dtype=np.float32), table).astype(np.float32)
    rows_high = rows.astype(ml_dtypes.bfloat16)
    rows_low = (rows - rows_high.astype(np.float32)).astype(ml_dtypes.bfloat16)
    single = (np.float32(2.0) - np.float32(2.0) * np.cos(np.float32(np.pi) * grid / np.float32(B + 1.0))).astype(np.float32)
    eigen = (single[:, None, None] + single[None, :, None] + single[None, None, :]).reshape(B, PLANE)
    return tiled, spread, rows_high, rows_low, eigen.astype(np.float32)


def split(values):
    high = values.astype(jnp.bfloat16)
    low = (values - high.astype(jnp.float32)).astype(jnp.bfloat16)
    return high, low


def split_outside(values):
    high = lax.reduce_precision(values, exponent_bits=8, mantissa_bits=7)
    return high.astype(jnp.bfloat16), (values - high).astype(jnp.bfloat16)


def dot3(left, right_high, right_low):
    high, low = split(left)
    out = jnp.dot(high, right_high, preferred_element_type=jnp.float32)
    out = out + jnp.dot(low, right_high, preferred_element_type=jnp.float32)
    return out + jnp.dot(high, right_low, preferred_element_type=jnp.float32)


def dot3_left(left_high, left_low, right):
    high, low = split(right)
    out = jnp.dot(left_high, high, preferred_element_type=jnp.float32)
    out = out + jnp.dot(left_low, high, preferred_element_type=jnp.float32)
    return out + jnp.dot(left_high, low, preferred_element_type=jnp.float32)


def exact_rows(matrix, values):
    first = values.astype(jnp.bfloat16)
    rest = values - first.astype(jnp.float32)
    second = rest.astype(jnp.bfloat16)
    third = (rest - second.astype(jnp.float32)).astype(jnp.bfloat16)
    out = jnp.dot(matrix, first, preferred_element_type=jnp.float32)
    out = out + jnp.dot(matrix, second, preferred_element_type=jnp.float32)
    return out + jnp.dot(matrix, third, preferred_element_type=jnp.float32)


def pair_kernel(
    delta_ref,
    live_ref,
    home_ref,
    part_ref,
    tiled_ref,
    spread_ref,
    rows_high_ref,
    rows_low_ref,
    eigen_ref,
    to_home_ref,
    to_partner_ref,
    shifted_ref,
    work_ref,
    kron_high_ref,
    kron_low_ref,
):
    slots = home_ref.shape[0]
    tiled = tiled_ref[...]
    for block in range(B):
        values = tiled * spread_ref[block : block + 1, :]
        high = values.astype(jnp.bfloat16)
        kron_high_ref[block * B : (block + 1) * B, :] = high
        kron_low_ref[block * B : (block + 1) * B, :] = (
            values - high.astype(jnp.float32)
        ).astype(jnp.bfloat16)
    lane = lax.broadcasted_iota(jnp.int32, (B, PLANE), 1)
    lane_b = lane // B
    lane_c = lane % B
    row = lax.broadcasted_iota(jnp.int32, (B, B), 0)
    col = lax.broadcasted_iota(jnp.int32, (B, B), 1)
    for slot in range(slots):
        d_a = delta_ref[slot, 0]
        d_b = delta_ref[slot, 1]
        d_c = delta_ref[slot, 2]
        pick = (col == row + d_a).astype(jnp.bfloat16)
        moved = jnp.dot(pick, part_ref[slot], preferred_element_type=jnp.float32)
        step = d_b * B + d_c
        moved = pltpu.roll(moved, (PLANE - step) % PLANE, 1)
        inside = (
            (lane_b + d_b >= 0) & (lane_b + d_b < B) & (lane_c + d_c >= 0) & (lane_c + d_c < B)
        )
        moved = jnp.where(inside, moved, 0.0)
        shifted_ref[slot] = moved
        work_ref[slot * B : (slot + 1) * B, :] = home_ref[slot].astype(jnp.float32) * moved

    kron_high = kron_high_ref[...]
    kron_low = kron_low_ref[...]
    rows_high = rows_high_ref[...]
    rows_low = rows_low_ref[...]
    coef = dot3_left(rows_high, rows_low, dot3(work_ref[...], kron_high, kron_low))
    eigen = eigen_ref[...]
    for slot in range(slots):
        work_ref[slot * B : (slot + 1) * B, :] = coef[slot * B : (slot + 1) * B, :] / eigen
    potential = dot3_left(rows_high, rows_low, dot3(work_ref[...], kron_high, kron_low))

    for slot in range(slots):
        d_a = delta_ref[slot, 0]
        d_b = delta_ref[slot, 1]
        d_c = delta_ref[slot, 2]
        live = live_ref[slot] > 0
        here = potential[slot * B : (slot + 1) * B, :]
        to_home_ref[slot] = jnp.where(live, here * shifted_ref[slot], 0.0)
        product = here * home_ref[slot].astype(jnp.float32)
        pick = (col == row - d_a).astype(jnp.bfloat16)
        moved = exact_rows(pick, product)
        step = d_b * B + d_c
        moved = pltpu.roll(moved, (PLANE + step) % PLANE, 1)
        inside = (
            (lane_b - d_b >= 0) & (lane_b - d_b < B) & (lane_c - d_c >= 0) & (lane_c - d_c < B)
        )
        to_partner_ref[slot] = jnp.where(live & inside, moved, 0.0)


def pair_fields(delta, live, home, part):
    slots = home.shape[0]
    tiled, spread, rows_high, rows_low, eigen = host_tables(slots)
    smem = pl.BlockSpec(memory_space=pltpu.SMEM)
    vmem = pl.BlockSpec(memory_space=pltpu.VMEM)
    box = jax.ShapeDtypeStruct((slots, B, PLANE), jnp.float32)
    return pl.pallas_call(
        pair_kernel,
        out_shape=(box, box),
        in_specs=[smem, smem] + [vmem] * 7,
        out_specs=(vmem, vmem),
        scratch_shapes=[
            pltpu.VMEM((slots, B, PLANE), jnp.float32),
            pltpu.VMEM((slots * B, PLANE), jnp.float32),
            pltpu.VMEM((PLANE, PLANE), jnp.bfloat16),
            pltpu.VMEM((PLANE, PLANE), jnp.bfloat16),
        ],
    )(delta, live, home, part, tiled, spread, rows_high, rows_low, eigen)


def exchange(blocks, axis):
    count = blocks.shape[0]
    received = [blocks[0]]
    for step in range(1, count):
        pairs = [(source, (source + step) % count) for source in range(count)]
        received.append(lax.ppermute(blocks[step], axis, pairs))
    return jnp.stack(received)


def pair_exchange(blocks, axis):
    chips = blocks.shape[0]
    count = 2 * chips
    partner = [(source, source ^ 1) for source in range(count)]
    mine = [blocks[0, 0], lax.ppermute(blocks[0, 1], axis, partner)]
    forward = []
    for step in range(1, chips):
        pairs = [
            (source, ((source // 2 + step) % chips) * 2 + source % 2) for source in range(count)
        ]
        got = lax.ppermute(blocks[step], axis, pairs)
        mine.append(got[0])
        forward.append(got[1])
    if forward:
        passed = lax.ppermute(jnp.stack(forward), axis, partner)
        mine.extend(passed[index] for index in range(chips - 1))
    return jnp.stack(mine)


def per_device(orbitals, offsets, sends, pair_home, pair_visit, pair_count):
    home_count = orbitals.shape[0]
    cell_count = orbitals.shape[1]
    section_total = sends.shape[1]
    per_target = sends.shape[2]
    slot_total = section_total * per_target
    slots = pair_home.shape[2]
    extra = 128
    me = lax.axis_index("home")
    ahead = (me + jnp.arange(section_total, dtype=jnp.int32)) % section_total
    chosen = sends[0][ahead]
    flat_chosen = chosen.reshape(-1)
    outgoing = jnp.concatenate(
        [
            orbitals[flat_chosen],
            jnp.pad(offsets[flat_chosen].astype(jnp.bfloat16), ((0, 0), (0, extra - 3))),
        ],
        axis=1,
    ).reshape(section_total, per_target, cell_count + extra)
    arrived = exchange(outgoing, "home").reshape(slot_total, cell_count + extra)
    visitors = arrived[:, :cell_count]
    visit_offsets = arrived[:, cell_count : cell_count + 3].astype(jnp.int32)

    home_slot = pair_home[0, 0]
    visit_code = pair_visit[0, 0]
    source = visit_code // per_target
    visit_slot = ((me - source) % section_total) * per_target + visit_code % per_target
    live = (jnp.arange(slots, dtype=jnp.int32) < pair_count[0, 0]).astype(jnp.int32)
    home_orb = orbitals[home_slot].reshape(slots, B, PLANE)
    part_orb = visitors[visit_slot].reshape(slots, B, PLANE)
    delta = offsets[home_slot] - visit_offsets[visit_slot]
    to_home, to_partner = pair_fields(delta, live, home_orb, part_orb)

    rows_out = 2 * slots
    fields = jnp.concatenate([to_home, to_partner], axis=0).reshape(rows_out, cell_count)
    pair_total = lax.psum(1, "pair")
    chunk = cell_count // pair_total
    pair_me = lax.axis_index("pair")
    targets = jnp.concatenate([home_slot, home_count + visit_slot]).astype(jnp.float32)
    body = fields.reshape(rows_out, pair_total, chunk).transpose(1, 0, 2)
    chips = pair_total // 2
    chip_me = pair_me // 2
    ahead_chip = (chip_me + jnp.arange(chips, dtype=jnp.int32)) % chips
    ahead_core = (pair_me + jnp.arange(2, dtype=jnp.int32)) % 2
    body = body[(ahead_chip[:, None] * 2 + ahead_core[None, :]).reshape(-1)]
    tags = jnp.broadcast_to(targets[None, :, None], (pair_total, rows_out, extra))
    payload = jnp.concatenate([body, tags], axis=2).reshape(chips, 2, rows_out, chunk + extra)
    got = pair_exchange(payload, "pair")
    got_ids = got[:, :, chunk].astype(jnp.int32)
    all_rows = jnp.arange(home_count + slot_total, dtype=jnp.int32)
    picker = (got_ids[:, :, None] == all_rows[None, None, :]).astype(jnp.float32)
    totals = jnp.einsum("srk,srl->kl", picker, got[:, :, :chunk], precision=PRECISE)
    home_totals = totals[:home_count]
    back = (-jnp.arange(section_total, dtype=jnp.int32)) % section_total
    back_rows = (back[:, None] * per_target + jnp.arange(per_target)[None, :]).reshape(-1)
    visit_totals = totals[home_count:][back_rows].reshape(section_total, per_target, chunk)
    returned = exchange(visit_totals, "home").reshape(slot_total, chunk)
    owners = chosen[back].reshape(-1)
    chooser = (owners[:, None] == jnp.arange(home_count, dtype=jnp.int32)[None, :]).astype(
        jnp.float32
    )
    return home_totals + jnp.dot(chooser.T, returned, precision=PRECISE)


def solution(mesh):
    in_specs = (
        P("home", None),
        P("home", None),
        P("home", None, None),
        P("home", "pair", None),
        P("home", "pair", None),
        P("home", "pair"),
    )
    out_specs = P("home", "pair")
    return jax.shard_map(
        per_device, mesh=mesh, in_specs=in_specs, out_specs=out_specs, check_vma=False
    )
```

```python
import functools

import jax
import jax.numpy as jnp
import ml_dtypes
import numpy as np
from jax import lax
from jax.experimental import pallas as pl
from jax.experimental.pallas import tpu as pltpu
from jax.sharding import PartitionSpec as P

B = 32
PLANE = B * B


PRECISE = lax.Precision.HIGHEST


def sine_table():
    grid = jnp.arange(B, dtype=jnp.float32) + 1.0
    return jnp.sqrt(2.0 / (B + 1.0)) * jnp.sin(jnp.pi * grid[:, None] * grid[None, :] / (B + 1.0))


def eigen_sum():
    grid = jnp.arange(B, dtype=jnp.float32) + 1.0
    single = 2.0 - 2.0 * jnp.cos(jnp.pi * grid / (B + 1.0))
    return single[:, None, None] + single[None, :, None] + single[None, None, :]


def host_tables(slots):
    grid = np.arange(B, dtype=np.float32) + np.float32(1.0)
    angle = np.float32(np.pi) * grid[:, None] * grid[None, :] / np.float32(B + 1.0)
    table = (np.sqrt(np.float32(2.0 / (B + 1.0))) * np.sin(angle)).astype(np.float32)
    tiled = np.tile(table, (1, B))
    spread = np.repeat(table, B, axis=1)
    rows = np.kron(np.eye(slots, dtype=np.float32), table).astype(np.float32)
    rows_high = rows.astype(ml_dtypes.bfloat16)
    rows_low = (rows - rows_high.astype(np.float32)).astype(ml_dtypes.bfloat16)
    single = (np.float32(2.0) - np.float32(2.0) * np.cos(np.float32(np.pi) * grid / np.float32(B + 1.0))).astype(np.float32)
    eigen = (single[:, None, None] + single[None, :, None] + single[None, None, :]).reshape(B, PLANE)
    return tiled, spread, rows_high, rows_low, eigen.astype(np.float32)


def split(values):
    high = values.astype(jnp.bfloat16)
    low = (values - high.astype(jnp.float32)).astype(jnp.bfloat16)
    return high, low


def split_outside(values):
    high = lax.reduce_precision(values, exponent_bits=8, mantissa_bits=7)
    return high.astype(jnp.bfloat16), (values - high).astype(jnp.bfloat16)


def dot3(left, right_high, right_low):
    high, low = split(left)
    out = jnp.dot(high, right_high, preferred_element_type=jnp.float32)
    out = out + jnp.dot(low, right_high, preferred_element_type=jnp.float32)
    return out + jnp.dot(high, right_low, preferred_element_type=jnp.float32)


def dot3_left(left_high, left_low, right):
    high, low = split(right)
    out = jnp.dot(left_high, high, preferred_element_type=jnp.float32)
    out = out + jnp.dot(left_low, high, preferred_element_type=jnp.float32)
    return out + jnp.dot(left_high, low, preferred_element_type=jnp.float32)


def exact_rows(matrix, values):
    first = values.astype(jnp.bfloat16)
    rest = values - first.astype(jnp.float32)
    second = rest.astype(jnp.bfloat16)
    third = (rest - second.astype(jnp.float32)).astype(jnp.bfloat16)
    out = jnp.dot(matrix, first, preferred_element_type=jnp.float32)
    out = out + jnp.dot(matrix, second, preferred_element_type=jnp.float32)
    return out + jnp.dot(matrix, third, preferred_element_type=jnp.float32)


def emit(payload_ref, row, values, tag, me):
    count, _, width = payload_ref.shape
    chunk = width - 128
    for index in range(count):
        place = lax.rem(index - me + count, count)
        if chunk >= PLANE:
            per = chunk // PLANE
            for part in range(per):
                payload_ref[place, pl.ds(row, 1), pl.ds(part * PLANE, PLANE)] = values[
                    index * per + part : index * per + part + 1, :
                ]
        else:
            per = PLANE // chunk
            line, piece = divmod(index, per)
            payload_ref[place, pl.ds(row, 1), pl.ds(0, chunk)] = values[
                line : line + 1, piece * chunk : (piece + 1) * chunk
            ]
        payload_ref[place, pl.ds(row, 1), pl.ds(chunk, 128)] = tag


def pair_kernel(
    meta_ref,
    home_ref,
    part_ref,
    tiled_ref,
    spread_ref,
    rows_high_ref,
    rows_low_ref,
    eigen_ref,
    payload_ref,
    shifted_ref,
    work_ref,
    kron_high_ref,
    kron_low_ref,
):
    slots = home_ref.shape[0]
    me = meta_ref[6 * slots]
    tiled = tiled_ref[...]
    for block in range(B):
        values = tiled * spread_ref[block : block + 1, :]
        high = values.astype(jnp.bfloat16)
        kron_high_ref[block * B : (block + 1) * B, :] = high
        kron_low_ref[block * B : (block + 1) * B, :] = (
            values - high.astype(jnp.float32)
        ).astype(jnp.bfloat16)
    lane = lax.broadcasted_iota(jnp.int32, (B, PLANE), 1)
    lane_b = lane // B
    lane_c = lane % B
    row = lax.broadcasted_iota(jnp.int32, (B, B), 0)
    col = lax.broadcasted_iota(jnp.int32, (B, B), 1)
    for slot in range(slots):
        d_a = meta_ref[3 * slot]
        d_b = meta_ref[3 * slot + 1]
        d_c = meta_ref[3 * slot + 2]
        pick = (col == row + d_a).astype(jnp.bfloat16)
        moved = jnp.dot(pick, part_ref[slot], preferred_element_type=jnp.float32)
        step = d_b * B + d_c
        moved = pltpu.roll(moved, (PLANE - step) % PLANE, 1)
        inside = (
            (lane_b + d_b >= 0) & (lane_b + d_b < B) & (lane_c + d_c >= 0) & (lane_c + d_c < B)
        )
        moved = jnp.where(inside, moved, 0.0)
        shifted_ref[slot] = moved
        work_ref[slot * B : (slot + 1) * B, :] = home_ref[slot].astype(jnp.float32) * moved

    kron_high = kron_high_ref[...]
    kron_low = kron_low_ref[...]
    rows_high = rows_high_ref[...]
    rows_low = rows_low_ref[...]
    coef = dot3_left(rows_high, rows_low, dot3(work_ref[...], kron_high, kron_low))
    eigen = eigen_ref[...]
    for slot in range(slots):
        work_ref[slot * B : (slot + 1) * B, :] = coef[slot * B : (slot + 1) * B, :] / eigen
    potential = dot3_left(rows_high, rows_low, dot3(work_ref[...], kron_high, kron_low))

    for slot in range(slots):
        d_a = meta_ref[3 * slot]
        d_b = meta_ref[3 * slot + 1]
        d_c = meta_ref[3 * slot + 2]
        live = meta_ref[3 * slots + slot] > 0
        here = potential[slot * B : (slot + 1) * B, :]
        tag_home = jnp.full((1, 128), meta_ref[4 * slots + slot].astype(jnp.float32))
        tag_part = jnp.full((1, 128), meta_ref[5 * slots + slot].astype(jnp.float32))
        emit(payload_ref, slot, jnp.where(live, here * shifted_ref[slot], 0.0), tag_home, me)
        product = here * home_ref[slot].astype(jnp.float32)
        pick = (col == row - d_a).astype(jnp.bfloat16)
        moved = exact_rows(pick, product)
        step = d_b * B + d_c
        moved = pltpu.roll(moved, (PLANE + step) % PLANE, 1)
        inside = (
            (lane_b - d_b >= 0) & (lane_b - d_b < B) & (lane_c - d_c >= 0) & (lane_c - d_c < B)
        )
        emit(payload_ref, slots + slot, jnp.where(live & inside, moved, 0.0), tag_part, me)


def pair_fields(meta, home, part, count, chunk):
    slots = home.shape[0]
    tiled, spread, rows_high, rows_low, eigen = host_tables(slots)
    smem = pl.BlockSpec(memory_space=pltpu.SMEM)
    vmem = pl.BlockSpec(memory_space=pltpu.VMEM)
    box = jax.ShapeDtypeStruct((count, 2 * slots, chunk + 128), jnp.float32)
    return pl.pallas_call(
        pair_kernel,
        out_shape=box,
        in_specs=[smem] + [vmem] * 7,
        out_specs=vmem,
        scratch_shapes=[
            pltpu.VMEM((slots, B, PLANE), jnp.float32),
            pltpu.VMEM((slots * B, PLANE), jnp.float32),
            pltpu.VMEM((PLANE, PLANE), jnp.bfloat16),
            pltpu.VMEM((PLANE, PLANE), jnp.bfloat16),
        ],
    )(meta, home, part, tiled, spread, rows_high, rows_low, eigen)


def exchange(blocks, axis):
    count = blocks.shape[0]
    received = [blocks[0]]
    for step in range(1, count):
        pairs = [(source, (source + step) % count) for source in range(count)]
        received.append(lax.ppermute(blocks[step], axis, pairs))
    return jnp.stack(received)


def per_device(orbitals, offsets, sends, pair_home, pair_visit, pair_count):
    home_count = orbitals.shape[0]
    cell_count = orbitals.shape[1]
    section_total = sends.shape[1]
    per_target = sends.shape[2]
    slot_total = section_total * per_target
    slots = pair_home.shape[2]
    extra = 128
    me = lax.axis_index("home")
    ahead = (me + jnp.arange(section_total, dtype=jnp.int32)) % section_total
    chosen = sends[0][ahead]
    flat_chosen = chosen.reshape(-1)
    outgoing = jnp.concatenate(
        [
            orbitals[flat_chosen],
            jnp.pad(offsets[flat_chosen].astype(jnp.bfloat16), ((0, 0), (0, extra - 3))),
        ],
        axis=1,
    ).reshape(section_total, per_target, cell_count + extra)
    arrived = exchange(outgoing, "home").reshape(slot_total, cell_count + extra)
    visitors = arrived[:, :cell_count]
    visit_offsets = arrived[:, cell_count : cell_count + 3].astype(jnp.int32)

    home_slot = pair_home[0, 0]
    visit_code = pair_visit[0, 0]
    source = visit_code // per_target
    visit_slot = ((me - source) % section_total) * per_target + visit_code % per_target
    live = (jnp.arange(slots, dtype=jnp.int32) < pair_count[0, 0]).astype(jnp.int32)
    home_orb = orbitals[home_slot].reshape(slots, B, PLANE)
    part_orb = visitors[visit_slot].reshape(slots, B, PLANE)
    delta = offsets[home_slot] - visit_offsets[visit_slot]
    pair_total = lax.psum(1, "pair")
    chunk = cell_count // pair_total
    pair_me = lax.axis_index("pair")
    meta = jnp.concatenate(
        [
            delta.reshape(-1),
            live,
            home_slot,
            home_count + visit_slot,
            jnp.reshape(pair_me, (1,)).astype(jnp.int32),
        ]
    )
    payload = pair_fields(meta, home_orb, part_orb, pair_total, chunk)
    got = exchange(payload, "pair")
    got_ids = got[:, :, chunk].astype(jnp.int32)
    all_rows = jnp.arange(home_count + slot_total, dtype=jnp.int32)
    picker = (got_ids[:, :, None] == all_rows[None, None, :]).astype(jnp.float32)
    totals = jnp.einsum("srk,srl->kl", picker, got[:, :, :chunk], precision=PRECISE)
    home_totals = totals[:home_count]
    back = (-jnp.arange(section_total, dtype=jnp.int32)) % section_total
    back_rows = (back[:, None] * per_target + jnp.arange(per_target)[None, :]).reshape(-1)
    visit_totals = totals[home_count:][back_rows].reshape(section_total, per_target, chunk)
    returned = exchange(visit_totals, "home").reshape(slot_total, chunk)
    owners = chosen[back].reshape(-1)
    chooser = (owners[:, None] == jnp.arange(home_count, dtype=jnp.int32)[None, :]).astype(
        jnp.float32
    )
    return home_totals + jnp.dot(chooser.T, returned, precision=PRECISE)


def solution(mesh):
    in_specs = (
        P("home", None),
        P("home", None),
        P("home", None, None),
        P("home", "pair", None),
        P("home", "pair", None),
        P("home", "pair"),
    )
    out_specs = P("home", "pair")
    return jax.shard_map(
        per_device, mesh=mesh, in_specs=in_specs, out_specs=out_specs, check_vma=False
    )
```

```python
import functools

import jax
import jax.numpy as jnp
import ml_dtypes
import numpy as np
from jax import lax
from jax.experimental import pallas as pl
from jax.experimental.pallas import tpu as pltpu
from jax.sharding import PartitionSpec as P

B = 32
PLANE = B * B


PRECISE = lax.Precision.HIGHEST


def sine_table():
    grid = jnp.arange(B, dtype=jnp.float32) + 1.0
    return jnp.sqrt(2.0 / (B + 1.0)) * jnp.sin(jnp.pi * grid[:, None] * grid[None, :] / (B + 1.0))


def eigen_sum():
    grid = jnp.arange(B, dtype=jnp.float32) + 1.0
    single = 2.0 - 2.0 * jnp.cos(jnp.pi * grid / (B + 1.0))
    return single[:, None, None] + single[None, :, None] + single[None, None, :]


def host_tables(slots):
    grid = np.arange(B, dtype=np.float32) + np.float32(1.0)
    angle = np.float32(np.pi) * grid[:, None] * grid[None, :] / np.float32(B + 1.0)
    table = (np.sqrt(np.float32(2.0 / (B + 1.0))) * np.sin(angle)).astype(np.float32)
    tiled = np.tile(table, (1, B))
    spread = np.repeat(table, B, axis=1)
    rows = np.kron(np.eye(slots, dtype=np.float32), table).astype(np.float32)
    rows_high = rows.astype(ml_dtypes.bfloat16)
    rows_low = (rows - rows_high.astype(np.float32)).astype(ml_dtypes.bfloat16)
    single = (np.float32(2.0) - np.float32(2.0) * np.cos(np.float32(np.pi) * grid / np.float32(B + 1.0))).astype(np.float32)
    eigen = (single[:, None, None] + single[None, :, None] + single[None, None, :]).reshape(B, PLANE)
    return tiled, spread, rows_high, rows_low, eigen.astype(np.float32)


def split(values):
    high = values.astype(jnp.bfloat16)
    low = (values - high.astype(jnp.float32)).astype(jnp.bfloat16)
    return high, low


def split_outside(values):
    high = lax.reduce_precision(values, exponent_bits=8, mantissa_bits=7)
    return high.astype(jnp.bfloat16), (values - high).astype(jnp.bfloat16)


def dot3(left, right_high, right_low):
    high, low = split(left)
    out = jnp.dot(high, right_high, preferred_element_type=jnp.float32)
    out = out + jnp.dot(low, right_high, preferred_element_type=jnp.float32)
    return out + jnp.dot(high, right_low, preferred_element_type=jnp.float32)


def dot3_left(left_high, left_low, right):
    high, low = split(right)
    out = jnp.dot(left_high, high, preferred_element_type=jnp.float32)
    out = out + jnp.dot(left_low, high, preferred_element_type=jnp.float32)
    return out + jnp.dot(left_high, low, preferred_element_type=jnp.float32)


def exact_rows(matrix, values):
    first = values.astype(jnp.bfloat16)
    rest = values - first.astype(jnp.float32)
    second = rest.astype(jnp.bfloat16)
    third = (rest - second.astype(jnp.float32)).astype(jnp.bfloat16)
    out = jnp.dot(matrix, first, preferred_element_type=jnp.float32)
    out = out + jnp.dot(matrix, second, preferred_element_type=jnp.float32)
    return out + jnp.dot(matrix, third, preferred_element_type=jnp.float32)


def emit(payload_ref, row, values, tag, me):
    count, _, width = payload_ref.shape
    chunk = width - 128
    for index in range(count):
        if flips(count):
            place = lax.bitwise_xor(me, jnp.int32(index))
        else:
            place = lax.rem(index - me + count, count)
        if chunk >= PLANE:
            per = chunk // PLANE
            for part in range(per):
                payload_ref[place, pl.ds(row, 1), pl.ds(part * PLANE, PLANE)] = values[
                    index * per + part : index * per + part + 1, :
                ]
        else:
            per = PLANE // chunk
            line, piece = divmod(index, per)
            payload_ref[place, pl.ds(row, 1), pl.ds(0, chunk)] = values[
                line : line + 1, piece * chunk : (piece + 1) * chunk
            ]
        payload_ref[place, pl.ds(row, 1), pl.ds(chunk, 128)] = tag


def pair_kernel(
    meta_ref,
    home_ref,
    part_ref,
    tiled_ref,
    spread_ref,
    rows_high_ref,
    rows_low_ref,
    eigen_ref,
    payload_ref,
    shifted_ref,
    work_ref,
    kron_high_ref,
    kron_low_ref,
):
    slots = home_ref.shape[0]
    me = meta_ref[6 * slots]
    tiled = tiled_ref[...]
    for block in range(B):
        values = tiled * spread_ref[block : block + 1, :]
        high = values.astype(jnp.bfloat16)
        kron_high_ref[block * B : (block + 1) * B, :] = high
        kron_low_ref[block * B : (block + 1) * B, :] = (
            values - high.astype(jnp.float32)
        ).astype(jnp.bfloat16)
    lane = lax.broadcasted_iota(jnp.int32, (B, PLANE), 1)
    lane_b = lane // B
    lane_c = lane % B
    row = lax.broadcasted_iota(jnp.int32, (B, B), 0)
    col = lax.broadcasted_iota(jnp.int32, (B, B), 1)
    for slot in range(slots):
        d_a = meta_ref[3 * slot]
        d_b = meta_ref[3 * slot + 1]
        d_c = meta_ref[3 * slot + 2]
        pick = (col == row + d_a).astype(jnp.bfloat16)
        moved = jnp.dot(pick, part_ref[slot], preferred_element_type=jnp.float32)
        step = d_b * B + d_c
        moved = pltpu.roll(moved, (PLANE - step) % PLANE, 1)
        inside = (
            (lane_b + d_b >= 0) & (lane_b + d_b < B) & (lane_c + d_c >= 0) & (lane_c + d_c < B)
        )
        moved = jnp.where(inside, moved, 0.0)
        shifted_ref[slot] = moved
        work_ref[slot * B : (slot + 1) * B, :] = home_ref[slot].astype(jnp.float32) * moved

    kron_high = kron_high_ref[...]
    kron_low = kron_low_ref[...]
    rows_high = rows_high_ref[...]
    rows_low = rows_low_ref[...]
    coef = dot3_left(rows_high, rows_low, dot3(work_ref[...], kron_high, kron_low))
    eigen = eigen_ref[...]
    for slot in range(slots):
        work_ref[slot * B : (slot + 1) * B, :] = coef[slot * B : (slot + 1) * B, :] / eigen
    potential = dot3_left(rows_high, rows_low, dot3(work_ref[...], kron_high, kron_low))

    for slot in range(slots):
        d_a = meta_ref[3 * slot]
        d_b = meta_ref[3 * slot + 1]
        d_c = meta_ref[3 * slot + 2]
        live = meta_ref[3 * slots + slot] > 0
        here = potential[slot * B : (slot + 1) * B, :]
        tag_home = jnp.full((1, 128), meta_ref[4 * slots + slot].astype(jnp.float32))
        tag_part = jnp.full((1, 128), meta_ref[5 * slots + slot].astype(jnp.float32))
        emit(payload_ref, slot, jnp.where(live, here * shifted_ref[slot], 0.0), tag_home, me)
        product = here * home_ref[slot].astype(jnp.float32)
        pick = (col == row - d_a).astype(jnp.bfloat16)
        moved = exact_rows(pick, product)
        step = d_b * B + d_c
        moved = pltpu.roll(moved, (PLANE + step) % PLANE, 1)
        inside = (
            (lane_b - d_b >= 0) & (lane_b - d_b < B) & (lane_c - d_c >= 0) & (lane_c - d_c < B)
        )
        emit(payload_ref, slots + slot, jnp.where(live & inside, moved, 0.0), tag_part, me)


def pair_fields(meta, home, part, count, chunk):
    slots = home.shape[0]
    tiled, spread, rows_high, rows_low, eigen = host_tables(slots)
    smem = pl.BlockSpec(memory_space=pltpu.SMEM)
    vmem = pl.BlockSpec(memory_space=pltpu.VMEM)
    box = jax.ShapeDtypeStruct((count, 2 * slots, chunk + 128), jnp.float32)
    return pl.pallas_call(
        pair_kernel,
        out_shape=box,
        in_specs=[smem] + [vmem] * 7,
        out_specs=vmem,
        scratch_shapes=[
            pltpu.VMEM((slots, B, PLANE), jnp.float32),
            pltpu.VMEM((slots * B, PLANE), jnp.float32),
            pltpu.VMEM((PLANE, PLANE), jnp.bfloat16),
            pltpu.VMEM((PLANE, PLANE), jnp.bfloat16),
        ],
    )(meta, home, part, tiled, spread, rows_high, rows_low, eigen)


def flips(count):
    return count & (count - 1) == 0


def toward(index, step, count):
    if flips(count):
        return index ^ step
    return (index + step) % count


def exchange(blocks, axis):
    count = blocks.shape[0]
    received = [blocks[0]]
    for step in range(1, count):
        pairs = [(source, toward(source, step, count)) for source in range(count)]
        received.append(lax.ppermute(blocks[step], axis, pairs))
    return jnp.stack(received)


def per_device(orbitals, offsets, sends, pair_home, pair_visit, pair_count):
    home_count = orbitals.shape[0]
    cell_count = orbitals.shape[1]
    section_total = sends.shape[1]
    per_target = sends.shape[2]
    slot_total = section_total * per_target
    slots = pair_home.shape[2]
    extra = 128
    me = lax.axis_index("home")
    steps = jnp.arange(section_total, dtype=jnp.int32)
    if flips(section_total):
        ahead = me ^ steps
    else:
        ahead = (me + steps) % section_total
    chosen = sends[0][ahead]
    flat_chosen = chosen.reshape(-1)
    outgoing = jnp.concatenate(
        [
            orbitals[flat_chosen],
            jnp.pad(offsets[flat_chosen].astype(jnp.bfloat16), ((0, 0), (0, extra - 3))),
        ],
        axis=1,
    ).reshape(section_total, per_target, cell_count + extra)
    arrived = exchange(outgoing, "home").reshape(slot_total, cell_count + extra)
    visitors = arrived[:, :cell_count]
    visit_offsets = arrived[:, cell_count : cell_count + 3].astype(jnp.int32)

    home_slot = pair_home[0, 0]
    visit_code = pair_visit[0, 0]
    source = visit_code // per_target
    if flips(section_total):
        arrival = me ^ source
    else:
        arrival = (me - source) % section_total
    visit_slot = arrival * per_target + visit_code % per_target
    live = (jnp.arange(slots, dtype=jnp.int32) < pair_count[0, 0]).astype(jnp.int32)
    home_orb = orbitals[home_slot].reshape(slots, B, PLANE)
    part_orb = visitors[visit_slot].reshape(slots, B, PLANE)
    delta = offsets[home_slot] - visit_offsets[visit_slot]
    pair_total = lax.psum(1, "pair")
    chunk = cell_count // pair_total
    pair_me = lax.axis_index("pair")
    meta = jnp.concatenate(
        [
            delta.reshape(-1),
            live,
            home_slot,
            home_count + visit_slot,
            jnp.reshape(pair_me, (1,)).astype(jnp.int32),
        ]
    )
    payload = pair_fields(meta, home_orb, part_orb, pair_total, chunk)
    got = exchange(payload, "pair")
    got_ids = got[:, :, chunk].astype(jnp.int32)
    all_rows = jnp.arange(home_count + slot_total, dtype=jnp.int32)
    picker = (got_ids[:, :, None] == all_rows[None, None, :]).astype(jnp.float32)
    totals = jnp.einsum("srk,srl->kl", picker, got[:, :, :chunk], precision=PRECISE)
    home_totals = totals[:home_count]
    if flips(section_total):
        back = steps
    else:
        back = (-steps) % section_total
    back_rows = (back[:, None] * per_target + jnp.arange(per_target)[None, :]).reshape(-1)
    visit_totals = totals[home_count:]
    if not flips(section_total):
        visit_totals = visit_totals[back_rows]
    visit_totals = visit_totals.reshape(section_total, per_target, chunk)
    returned = exchange(visit_totals, "home").reshape(slot_total, chunk)
    owners = chosen[back].reshape(-1)
    chooser = (owners[:, None] == jnp.arange(home_count, dtype=jnp.int32)[None, :]).astype(
        jnp.float32
    )
    return home_totals + jnp.dot(chooser.T, returned, precision=PRECISE)


def solution(mesh):
    in_specs = (
        P("home", None),
        P("home", None),
        P("home", None, None),
        P("home", "pair", None),
        P("home", "pair", None),
        P("home", "pair"),
    )
    out_specs = P("home", "pair")
    return jax.shard_map(
        per_device, mesh=mesh, in_specs=in_specs, out_specs=out_specs, check_vma=False
    )
```

```python
import functools

import jax
import jax.numpy as jnp
import ml_dtypes
import numpy as np
from jax import lax
from jax.experimental import pallas as pl
from jax.experimental.pallas import tpu as pltpu
from jax.sharding import PartitionSpec as P

B = 32
PLANE = B * B


PRECISE = lax.Precision.HIGHEST


def sine_table():
    grid = jnp.arange(B, dtype=jnp.float32) + 1.0
    return jnp.sqrt(2.0 / (B + 1.0)) * jnp.sin(jnp.pi * grid[:, None] * grid[None, :] / (B + 1.0))


def eigen_sum():
    grid = jnp.arange(B, dtype=jnp.float32) + 1.0
    single = 2.0 - 2.0 * jnp.cos(jnp.pi * grid / (B + 1.0))
    return single[:, None, None] + single[None, :, None] + single[None, None, :]


def host_tables(slots):
    grid = np.arange(B, dtype=np.float32) + np.float32(1.0)
    angle = np.float32(np.pi) * grid[:, None] * grid[None, :] / np.float32(B + 1.0)
    table = (np.sqrt(np.float32(2.0 / (B + 1.0))) * np.sin(angle)).astype(np.float32)
    tiled = np.tile(table, (1, B))
    spread = np.repeat(table, B, axis=1)
    rows = np.kron(np.eye(slots, dtype=np.float32), table).astype(np.float32)
    rows_high = rows.astype(ml_dtypes.bfloat16)
    rows_low = (rows - rows_high.astype(np.float32)).astype(ml_dtypes.bfloat16)
    single = (np.float32(2.0) - np.float32(2.0) * np.cos(np.float32(np.pi) * grid / np.float32(B + 1.0))).astype(np.float32)
    eigen = (single[:, None, None] + single[None, :, None] + single[None, None, :]).reshape(B, PLANE)
    return tiled, spread, rows_high, rows_low, eigen.astype(np.float32)


def split(values):
    high = values.astype(jnp.bfloat16)
    low = (values - high.astype(jnp.float32)).astype(jnp.bfloat16)
    return high, low


def split_outside(values):
    high = lax.reduce_precision(values, exponent_bits=8, mantissa_bits=7)
    return high.astype(jnp.bfloat16), (values - high).astype(jnp.bfloat16)


def dot3(left, right_high, right_low):
    high, low = split(left)
    out = jnp.dot(high, right_high, preferred_element_type=jnp.float32)
    out = out + jnp.dot(low, right_high, preferred_element_type=jnp.float32)
    return out + jnp.dot(high, right_low, preferred_element_type=jnp.float32)


def dot3_left(left_high, left_low, right):
    high, low = split(right)
    out = jnp.dot(left_high, high, preferred_element_type=jnp.float32)
    out = out + jnp.dot(left_low, high, preferred_element_type=jnp.float32)
    return out + jnp.dot(left_high, low, preferred_element_type=jnp.float32)


def exact_rows(matrix, values):
    first = values.astype(jnp.bfloat16)
    rest = values - first.astype(jnp.float32)
    second = rest.astype(jnp.bfloat16)
    third = (rest - second.astype(jnp.float32)).astype(jnp.bfloat16)
    out = jnp.dot(matrix, first, preferred_element_type=jnp.float32)
    out = out + jnp.dot(matrix, second, preferred_element_type=jnp.float32)
    return out + jnp.dot(matrix, third, preferred_element_type=jnp.float32)


def emit(payload_refs, stage_ref, row, values, tag, me):
    count = len(payload_refs)
    chunk = payload_refs[0].shape[1] - 128
    stage_ref[...] = values
    for step in range(count):
        index = lax.rem(me + step, count)
        out = payload_refs[step]
        if chunk >= PLANE:
            per = chunk // PLANE
            for part in range(per):
                out[pl.ds(row, 1), pl.ds(part * PLANE, PLANE)] = stage_ref[
                    pl.ds(index * per + part, 1), :
                ]
        else:
            per = PLANE // chunk
            full = stage_ref[pl.ds(index // per, 1), :]
            piece = index % per
            pick = full[:, 0:chunk]
            for other in range(1, per):
                pick = jnp.where(piece == other, full[:, other * chunk : (other + 1) * chunk], pick)
            out[pl.ds(row, 1), pl.ds(0, chunk)] = pick
        out[pl.ds(row, 1), pl.ds(chunk, 128)] = tag


def pair_kernel(
    count,
    meta_ref,
    home_ref,
    part_ref,
    tiled_ref,
    spread_ref,
    rows_high_ref,
    rows_low_ref,
    eigen_ref,
    *rest,
):
    payload_ref = rest[:count]
    shifted_ref, work_ref, kron_high_ref, kron_low_ref, stage_ref = rest[count:]
    slots = home_ref.shape[0]
    me = meta_ref[6 * slots]
    tiled = tiled_ref[...]
    for block in range(B):
        values = tiled * spread_ref[block : block + 1, :]
        high = values.astype(jnp.bfloat16)
        kron_high_ref[block * B : (block + 1) * B, :] = high
        kron_low_ref[block * B : (block + 1) * B, :] = (
            values - high.astype(jnp.float32)
        ).astype(jnp.bfloat16)
    lane = lax.broadcasted_iota(jnp.int32, (B, PLANE), 1)
    lane_b = lane // B
    lane_c = lane % B
    row = lax.broadcasted_iota(jnp.int32, (B, B), 0)
    col = lax.broadcasted_iota(jnp.int32, (B, B), 1)
    for slot in range(slots):
        d_a = meta_ref[3 * slot]
        d_b = meta_ref[3 * slot + 1]
        d_c = meta_ref[3 * slot + 2]
        pick = (col == row + d_a).astype(jnp.bfloat16)
        moved = jnp.dot(pick, part_ref[slot], preferred_element_type=jnp.float32)
        step = d_b * B + d_c
        moved = pltpu.roll(moved, (PLANE - step) % PLANE, 1)
        inside = (
            (lane_b + d_b >= 0) & (lane_b + d_b < B) & (lane_c + d_c >= 0) & (lane_c + d_c < B)
        )
        moved = jnp.where(inside, moved, 0.0)
        shifted_ref[slot] = moved
        work_ref[slot * B : (slot + 1) * B, :] = home_ref[slot].astype(jnp.float32) * moved

    kron_high = kron_high_ref[...]
    kron_low = kron_low_ref[...]
    rows_high = rows_high_ref[...]
    rows_low = rows_low_ref[...]
    coef = dot3_left(rows_high, rows_low, dot3(work_ref[...], kron_high, kron_low))
    eigen = eigen_ref[...]
    for slot in range(slots):
        work_ref[slot * B : (slot + 1) * B, :] = coef[slot * B : (slot + 1) * B, :] / eigen
    potential = dot3_left(rows_high, rows_low, dot3(work_ref[...], kron_high, kron_low))

    for slot in range(slots):
        d_a = meta_ref[3 * slot]
        d_b = meta_ref[3 * slot + 1]
        d_c = meta_ref[3 * slot + 2]
        live = meta_ref[3 * slots + slot] > 0
        here = potential[slot * B : (slot + 1) * B, :]
        tag_home = jnp.full((1, 128), meta_ref[4 * slots + slot].astype(jnp.float32))
        tag_part = jnp.full((1, 128), meta_ref[5 * slots + slot].astype(jnp.float32))
        emit(payload_ref, stage_ref, slot, jnp.where(live, here * shifted_ref[slot], 0.0), tag_home, me)
        product = here * home_ref[slot].astype(jnp.float32)
        pick = (col == row - d_a).astype(jnp.bfloat16)
        moved = exact_rows(pick, product)
        step = d_b * B + d_c
        moved = pltpu.roll(moved, (PLANE + step) % PLANE, 1)
        inside = (
            (lane_b - d_b >= 0) & (lane_b - d_b < B) & (lane_c - d_c >= 0) & (lane_c - d_c < B)
        )
        emit(
            payload_ref, stage_ref, slots + slot, jnp.where(live & inside, moved, 0.0), tag_part, me
        )


def pair_fields(meta, home, part, count, chunk):
    slots = home.shape[0]
    tiled, spread, rows_high, rows_low, eigen = host_tables(slots)
    smem = pl.BlockSpec(memory_space=pltpu.SMEM)
    vmem = pl.BlockSpec(memory_space=pltpu.VMEM)
    box = jax.ShapeDtypeStruct((2 * slots, chunk + 128), jnp.float32)
    return pl.pallas_call(
        functools.partial(pair_kernel, count),
        out_shape=tuple([box] * count),
        in_specs=[smem] + [vmem] * 7,
        out_specs=tuple([vmem] * count),
        scratch_shapes=[
            pltpu.VMEM((slots, B, PLANE), jnp.float32),
            pltpu.VMEM((slots * B, PLANE), jnp.float32),
            pltpu.VMEM((PLANE, PLANE), jnp.bfloat16),
            pltpu.VMEM((PLANE, PLANE), jnp.bfloat16),
            pltpu.VMEM((B, PLANE), jnp.float32),
        ],
    )(meta, home, part, tiled, spread, rows_high, rows_low, eigen)


def exchange(blocks, axis):
    count = len(blocks)
    received = [blocks[0]]
    for step in range(1, count):
        pairs = [(source, (source + step) % count) for source in range(count)]
        received.append(lax.ppermute(blocks[step], axis, pairs))
    return jnp.stack(received)


def per_device(orbitals, offsets, sends, pair_home, pair_visit, pair_count):
    home_count = orbitals.shape[0]
    cell_count = orbitals.shape[1]
    section_total = sends.shape[1]
    per_target = sends.shape[2]
    slot_total = section_total * per_target
    slots = pair_home.shape[2]
    extra = 128
    me = lax.axis_index("home")
    ahead = (me + jnp.arange(section_total, dtype=jnp.int32)) % section_total
    chosen = sends[0][ahead]
    flat_chosen = chosen.reshape(-1)
    outgoing = jnp.concatenate(
        [
            orbitals[flat_chosen],
            jnp.pad(offsets[flat_chosen].astype(jnp.bfloat16), ((0, 0), (0, extra - 3))),
        ],
        axis=1,
    ).reshape(section_total, per_target, cell_count + extra)
    arrived = exchange(outgoing, "home").reshape(slot_total, cell_count + extra)
    visitors = arrived[:, :cell_count]
    visit_offsets = arrived[:, cell_count : cell_count + 3].astype(jnp.int32)

    home_slot = pair_home[0, 0]
    visit_code = pair_visit[0, 0]
    source = visit_code // per_target
    visit_slot = ((me - source) % section_total) * per_target + visit_code % per_target
    live = (jnp.arange(slots, dtype=jnp.int32) < pair_count[0, 0]).astype(jnp.int32)
    home_orb = orbitals[home_slot].reshape(slots, B, PLANE)
    part_orb = visitors[visit_slot].reshape(slots, B, PLANE)
    delta = offsets[home_slot] - visit_offsets[visit_slot]
    pair_total = lax.psum(1, "pair")
    chunk = cell_count // pair_total
    pair_me = lax.axis_index("pair")
    meta = jnp.concatenate(
        [
            delta.reshape(-1),
            live,
            home_slot,
            home_count + visit_slot,
            jnp.reshape(pair_me, (1,)).astype(jnp.int32),
        ]
    )
    payload = pair_fields(meta, home_orb, part_orb, pair_total, chunk)
    got = exchange(payload, "pair")
    got_ids = got[:, :, chunk].astype(jnp.int32)
    all_rows = jnp.arange(home_count + slot_total, dtype=jnp.int32)
    picker = (got_ids[:, :, None] == all_rows[None, None, :]).astype(jnp.float32)
    totals = jnp.einsum("srk,srl->kl", picker, got[:, :, :chunk], precision=PRECISE)
    home_totals = totals[:home_count]
    back = (-jnp.arange(section_total, dtype=jnp.int32)) % section_total
    back_rows = (back[:, None] * per_target + jnp.arange(per_target)[None, :]).reshape(-1)
    visit_totals = totals[home_count:][back_rows].reshape(section_total, per_target, chunk)
    returned = exchange(visit_totals, "home").reshape(slot_total, chunk)
    owners = chosen[back].reshape(-1)
    chooser = (owners[:, None] == jnp.arange(home_count, dtype=jnp.int32)[None, :]).astype(
        jnp.float32
    )
    return home_totals + jnp.dot(chooser.T, returned, precision=PRECISE)


def solution(mesh):
    in_specs = (
        P("home", None),
        P("home", None),
        P("home", None, None),
        P("home", "pair", None),
        P("home", "pair", None),
        P("home", "pair"),
    )
    out_specs = P("home", "pair")
    return jax.shard_map(
        per_device, mesh=mesh, in_specs=in_specs, out_specs=out_specs, check_vma=False
    )
```

```python
import functools

import jax
import jax.numpy as jnp
import ml_dtypes
import numpy as np
from jax import lax
from jax.experimental import pallas as pl
from jax.experimental.pallas import tpu as pltpu
from jax.sharding import PartitionSpec as P

B = 32
PLANE = B * B


PRECISE = lax.Precision.HIGHEST


def sine_table():
    grid = jnp.arange(B, dtype=jnp.float32) + 1.0
    return jnp.sqrt(2.0 / (B + 1.0)) * jnp.sin(jnp.pi * grid[:, None] * grid[None, :] / (B + 1.0))


def eigen_sum():
    grid = jnp.arange(B, dtype=jnp.float32) + 1.0
    single = 2.0 - 2.0 * jnp.cos(jnp.pi * grid / (B + 1.0))
    return single[:, None, None] + single[None, :, None] + single[None, None, :]


def host_tables(slots):
    grid = np.arange(B, dtype=np.float32) + np.float32(1.0)
    angle = np.float32(np.pi) * grid[:, None] * grid[None, :] / np.float32(B + 1.0)
    table = (np.sqrt(np.float32(2.0 / (B + 1.0))) * np.sin(angle)).astype(np.float32)
    tiled = np.tile(table, (1, B))
    spread = np.repeat(table, B, axis=1)
    rows = np.kron(np.eye(slots, dtype=np.float32), table).astype(np.float32)
    rows_high = rows.astype(ml_dtypes.bfloat16)
    rows_low = (rows - rows_high.astype(np.float32)).astype(ml_dtypes.bfloat16)
    single = (np.float32(2.0) - np.float32(2.0) * np.cos(np.float32(np.pi) * grid / np.float32(B + 1.0))).astype(np.float32)
    eigen = (single[:, None, None] + single[None, :, None] + single[None, None, :]).reshape(B, PLANE)
    return tiled, spread, rows_high, rows_low, eigen.astype(np.float32)


def split(values):
    high = values.astype(jnp.bfloat16)
    low = (values - high.astype(jnp.float32)).astype(jnp.bfloat16)
    return high, low


def split_outside(values):
    high = lax.reduce_precision(values, exponent_bits=8, mantissa_bits=7)
    return high.astype(jnp.bfloat16), (values - high).astype(jnp.bfloat16)


def dot3(left, right_high, right_low):
    high, low = split(left)
    out = jnp.dot(high, right_high, preferred_element_type=jnp.float32)
    out = out + jnp.dot(low, right_high, preferred_element_type=jnp.float32)
    return out + jnp.dot(high, right_low, preferred_element_type=jnp.float32)


def dot3_left(left_high, left_low, right):
    high, low = split(right)
    out = jnp.dot(left_high, high, preferred_element_type=jnp.float32)
    out = out + jnp.dot(left_low, high, preferred_element_type=jnp.float32)
    return out + jnp.dot(left_high, low, preferred_element_type=jnp.float32)


def exact_rows(matrix, values):
    first = values.astype(jnp.bfloat16)
    rest = values - first.astype(jnp.float32)
    second = rest.astype(jnp.bfloat16)
    third = (rest - second.astype(jnp.float32)).astype(jnp.bfloat16)
    out = jnp.dot(matrix, first, preferred_element_type=jnp.float32)
    out = out + jnp.dot(matrix, second, preferred_element_type=jnp.float32)
    return out + jnp.dot(matrix, third, preferred_element_type=jnp.float32)


def emit(payload_refs, stage_ref, row, values, tag, me):
    count = len(payload_refs)
    chunk = payload_refs[0].shape[1] - 128
    stage_ref[...] = values
    for step in range(count):
        index = lax.rem(me + step, count)
        out = payload_refs[step]
        if chunk >= PLANE:
            per = chunk // PLANE
            for part in range(per):
                out[pl.ds(row, 1), pl.ds(part * PLANE, PLANE)] = stage_ref[
                    pl.ds(index * per + part, 1), :
                ]
        else:
            per = PLANE // chunk
            full = stage_ref[pl.ds(index // per, 1), :]
            piece = index % per
            pick = full[:, 0:chunk]
            for other in range(1, per):
                pick = jnp.where(piece == other, full[:, other * chunk : (other + 1) * chunk], pick)
            out[pl.ds(row, 1), pl.ds(0, chunk)] = pick
        out[pl.ds(row, 1), pl.ds(chunk, 128)] = tag


def kron_kernel(tiled_ref, spread_ref, kron_high_ref, kron_low_ref):
    tiled = tiled_ref[...]
    for block in range(B):
        values = tiled * spread_ref[block : block + 1, :]
        high = values.astype(jnp.bfloat16)
        kron_high_ref[block * B : (block + 1) * B, :] = high
        kron_low_ref[block * B : (block + 1) * B, :] = (
            values - high.astype(jnp.float32)
        ).astype(jnp.bfloat16)


def kron_tables():
    tiled, spread, _, _, _ = host_tables(1)
    vmem = pl.BlockSpec(memory_space=pltpu.VMEM)
    square = jax.ShapeDtypeStruct((PLANE, PLANE), jnp.bfloat16)
    return pl.pallas_call(
        kron_kernel,
        out_shape=(square, square),
        in_specs=[vmem, vmem],
        out_specs=(vmem, vmem),
    )(tiled, spread)


def pair_kernel(
    count,
    meta_ref,
    home_ref,
    part_ref,
    kron_high_ref,
    kron_low_ref,
    rows_high_ref,
    rows_low_ref,
    eigen_ref,
    *rest,
):
    payload_ref = rest[:count]
    shifted_ref, work_ref, stage_ref = rest[count:]
    slots = home_ref.shape[0]
    me = meta_ref[6 * slots]
    lane = lax.broadcasted_iota(jnp.int32, (B, PLANE), 1)
    lane_b = lane // B
    lane_c = lane % B
    row = lax.broadcasted_iota(jnp.int32, (B, B), 0)
    col = lax.broadcasted_iota(jnp.int32, (B, B), 1)
    for slot in range(slots):
        d_a = meta_ref[3 * slot]
        d_b = meta_ref[3 * slot + 1]
        d_c = meta_ref[3 * slot + 2]
        pick = (col == row + d_a).astype(jnp.bfloat16)
        moved = jnp.dot(pick, part_ref[slot], preferred_element_type=jnp.float32)
        step = d_b * B + d_c
        moved = pltpu.roll(moved, (PLANE - step) % PLANE, 1)
        inside = (
            (lane_b + d_b >= 0) & (lane_b + d_b < B) & (lane_c + d_c >= 0) & (lane_c + d_c < B)
        )
        moved = jnp.where(inside, moved, 0.0)
        shifted_ref[slot] = moved
        work_ref[slot * B : (slot + 1) * B, :] = home_ref[slot].astype(jnp.float32) * moved

    kron_high = kron_high_ref[...]
    kron_low = kron_low_ref[...]
    rows_high = rows_high_ref[...]
    rows_low = rows_low_ref[...]
    coef = dot3_left(rows_high, rows_low, dot3(work_ref[...], kron_high, kron_low))
    eigen = eigen_ref[...]
    for slot in range(slots):
        work_ref[slot * B : (slot + 1) * B, :] = coef[slot * B : (slot + 1) * B, :] / eigen
    potential = dot3_left(rows_high, rows_low, dot3(work_ref[...], kron_high, kron_low))

    for slot in range(slots):
        d_a = meta_ref[3 * slot]
        d_b = meta_ref[3 * slot + 1]
        d_c = meta_ref[3 * slot + 2]
        live = meta_ref[3 * slots + slot] > 0
        here = potential[slot * B : (slot + 1) * B, :]
        tag_home = jnp.full((1, 128), meta_ref[4 * slots + slot].astype(jnp.float32))
        tag_part = jnp.full((1, 128), meta_ref[5 * slots + slot].astype(jnp.float32))
        emit(payload_ref, stage_ref, slot, jnp.where(live, here * shifted_ref[slot], 0.0), tag_home, me)
        product = here * home_ref[slot].astype(jnp.float32)
        pick = (col == row - d_a).astype(jnp.bfloat16)
        moved = exact_rows(pick, product)
        step = d_b * B + d_c
        moved = pltpu.roll(moved, (PLANE + step) % PLANE, 1)
        inside = (
            (lane_b - d_b >= 0) & (lane_b - d_b < B) & (lane_c - d_c >= 0) & (lane_c - d_c < B)
        )
        emit(
            payload_ref, stage_ref, slots + slot, jnp.where(live & inside, moved, 0.0), tag_part, me
        )


def pair_fields(meta, home, part, count, chunk):
    slots = home.shape[0]
    _, _, rows_high, rows_low, eigen = host_tables(slots)
    kron_high, kron_low = kron_tables()
    smem = pl.BlockSpec(memory_space=pltpu.SMEM)
    vmem = pl.BlockSpec(memory_space=pltpu.VMEM)
    box = jax.ShapeDtypeStruct((2 * slots, chunk + 128), jnp.float32)
    return pl.pallas_call(
        functools.partial(pair_kernel, count),
        out_shape=tuple([box] * count),
        in_specs=[smem] + [vmem] * 7,
        out_specs=tuple([vmem] * count),
        scratch_shapes=[
            pltpu.VMEM((slots, B, PLANE), jnp.float32),
            pltpu.VMEM((slots * B, PLANE), jnp.float32),
            pltpu.VMEM((B, PLANE), jnp.float32),
        ],
    )(meta, home, part, kron_high, kron_low, rows_high, rows_low, eigen)


def exchange(blocks, axis):
    count = len(blocks)
    received = [blocks[0]]
    for step in range(1, count):
        pairs = [(source, (source + step) % count) for source in range(count)]
        received.append(lax.ppermute(blocks[step], axis, pairs))
    return jnp.stack(received)


def per_device(orbitals, offsets, sends, pair_home, pair_visit, pair_count):
    home_count = orbitals.shape[0]
    cell_count = orbitals.shape[1]
    section_total = sends.shape[1]
    per_target = sends.shape[2]
    slot_total = section_total * per_target
    slots = pair_home.shape[2]
    extra = 128
    me = lax.axis_index("home")
    ahead = (me + jnp.arange(section_total, dtype=jnp.int32)) % section_total
    chosen = sends[0][ahead]
    flat_chosen = chosen.reshape(-1)
    outgoing = jnp.concatenate(
        [
            orbitals[flat_chosen],
            jnp.pad(offsets[flat_chosen].astype(jnp.bfloat16), ((0, 0), (0, extra - 3))),
        ],
        axis=1,
    ).reshape(section_total, per_target, cell_count + extra)
    arrived = exchange(outgoing, "home").reshape(slot_total, cell_count + extra)
    visitors = arrived[:, :cell_count]
    visit_offsets = arrived[:, cell_count : cell_count + 3].astype(jnp.int32)

    home_slot = pair_home[0, 0]
    visit_code = pair_visit[0, 0]
    source = visit_code // per_target
    visit_slot = ((me - source) % section_total) * per_target + visit_code % per_target
    live = (jnp.arange(slots, dtype=jnp.int32) < pair_count[0, 0]).astype(jnp.int32)
    home_orb = orbitals[home_slot].reshape(slots, B, PLANE)
    part_orb = visitors[visit_slot].reshape(slots, B, PLANE)
    delta = offsets[home_slot] - visit_offsets[visit_slot]
    pair_total = lax.psum(1, "pair")
    chunk = cell_count // pair_total
    pair_me = lax.axis_index("pair")
    meta = jnp.concatenate(
        [
            delta.reshape(-1),
            live,
            home_slot,
            home_count + visit_slot,
            jnp.reshape(pair_me, (1,)).astype(jnp.int32),
        ]
    )
    payload = pair_fields(meta, home_orb, part_orb, pair_total, chunk)
    got = exchange(payload, "pair")
    got_ids = got[:, :, chunk].astype(jnp.int32)
    all_rows = jnp.arange(home_count + slot_total, dtype=jnp.int32)
    picker = (got_ids[:, :, None] == all_rows[None, None, :]).astype(jnp.float32)
    totals = jnp.einsum("srk,srl->kl", picker, got[:, :, :chunk], precision=PRECISE)
    home_totals = totals[:home_count]
    back = (-jnp.arange(section_total, dtype=jnp.int32)) % section_total
    back_rows = (back[:, None] * per_target + jnp.arange(per_target)[None, :]).reshape(-1)
    visit_totals = totals[home_count:][back_rows].reshape(section_total, per_target, chunk)
    returned = exchange(visit_totals, "home").reshape(slot_total, chunk)
    owners = chosen[back].reshape(-1)
    chooser = (owners[:, None] == jnp.arange(home_count, dtype=jnp.int32)[None, :]).astype(
        jnp.float32
    )
    return home_totals + jnp.dot(chooser.T, returned, precision=PRECISE)


def solution(mesh):
    in_specs = (
        P("home", None),
        P("home", None),
        P("home", None, None),
        P("home", "pair", None),
        P("home", "pair", None),
        P("home", "pair"),
    )
    out_specs = P("home", "pair")
    return jax.shard_map(
        per_device, mesh=mesh, in_specs=in_specs, out_specs=out_specs, check_vma=False
    )
```

```python
import functools

import jax
import jax.numpy as jnp
import ml_dtypes
import numpy as np
from jax import lax
from jax.experimental import pallas as pl
from jax.experimental.pallas import tpu as pltpu
from jax.sharding import PartitionSpec as P

B = 32
PLANE = B * B


PRECISE = lax.Precision.HIGHEST


def sine_table():
    grid = jnp.arange(B, dtype=jnp.float32) + 1.0
    return jnp.sqrt(2.0 / (B + 1.0)) * jnp.sin(jnp.pi * grid[:, None] * grid[None, :] / (B + 1.0))


def eigen_sum():
    grid = jnp.arange(B, dtype=jnp.float32) + 1.0
    single = 2.0 - 2.0 * jnp.cos(jnp.pi * grid / (B + 1.0))
    return single[:, None, None] + single[None, :, None] + single[None, None, :]


def host_tables(slots):
    grid = np.arange(B, dtype=np.float32) + np.float32(1.0)
    angle = np.float32(np.pi) * grid[:, None] * grid[None, :] / np.float32(B + 1.0)
    table = (np.sqrt(np.float32(2.0 / (B + 1.0))) * np.sin(angle)).astype(np.float32)
    tiled = np.tile(table, (1, B))
    spread = np.repeat(table, B, axis=1)
    rows = np.kron(np.eye(slots, dtype=np.float32), table).astype(np.float32)
    rows_high = rows.astype(ml_dtypes.bfloat16)
    rows_low = (rows - rows_high.astype(np.float32)).astype(ml_dtypes.bfloat16)
    single = (np.float32(2.0) - np.float32(2.0) * np.cos(np.float32(np.pi) * grid / np.float32(B + 1.0))).astype(np.float32)
    eigen = (single[:, None, None] + single[None, :, None] + single[None, None, :]).reshape(B, PLANE)
    return tiled, spread, rows_high, rows_low, eigen.astype(np.float32)


def split(values):
    high = values.astype(jnp.bfloat16)
    low = (values - high.astype(jnp.float32)).astype(jnp.bfloat16)
    return high, low


def split_outside(values):
    high = lax.reduce_precision(values, exponent_bits=8, mantissa_bits=7)
    return high.astype(jnp.bfloat16), (values - high).astype(jnp.bfloat16)


def dot3(left, right_high, right_low):
    high, low = split(left)
    out = jnp.dot(high, right_high, preferred_element_type=jnp.float32)
    out = out + jnp.dot(low, right_high, preferred_element_type=jnp.float32)
    return out + jnp.dot(high, right_low, preferred_element_type=jnp.float32)


def dot3_left(left_high, left_low, right):
    high, low = split(right)
    out = jnp.dot(left_high, high, preferred_element_type=jnp.float32)
    out = out + jnp.dot(left_low, high, preferred_element_type=jnp.float32)
    return out + jnp.dot(left_high, low, preferred_element_type=jnp.float32)


def exact_rows(matrix, values):
    first = values.astype(jnp.bfloat16)
    rest = values - first.astype(jnp.float32)
    second = rest.astype(jnp.bfloat16)
    third = (rest - second.astype(jnp.float32)).astype(jnp.bfloat16)
    out = jnp.dot(matrix, first, preferred_element_type=jnp.float32)
    out = out + jnp.dot(matrix, second, preferred_element_type=jnp.float32)
    return out + jnp.dot(matrix, third, preferred_element_type=jnp.float32)


def emit(payload_refs, stage_ref, row, values, tag, me):
    count = len(payload_refs)
    chunk = payload_refs[0].shape[1] - 128
    stage_ref[...] = values
    for step in range(count):
        index = lax.rem(me + step, count)
        out = payload_refs[step]
        if chunk >= PLANE:
            per = chunk // PLANE
            for part in range(per):
                out[pl.ds(row, 1), pl.ds(part * PLANE, PLANE)] = stage_ref[
                    pl.ds(index * per + part, 1), :
                ]
        else:
            per = PLANE // chunk
            full = stage_ref[pl.ds(index // per, 1), :]
            piece = index % per
            pick = full[:, 0:chunk]
            for other in range(1, per):
                pick = jnp.where(piece == other, full[:, other * chunk : (other + 1) * chunk], pick)
            out[pl.ds(row, 1), pl.ds(0, chunk)] = pick
        out[pl.ds(row, 1), pl.ds(chunk, 128)] = tag


def pair_kernel(
    count,
    meta_ref,
    home_ref,
    part_ref,
    tiled_ref,
    spread_ref,
    rows_high_ref,
    rows_low_ref,
    eigen_ref,
    *rest,
):
    payload_ref = rest[:count]
    shifted_ref, work_ref, kron_high_ref, kron_low_ref, stage_ref = rest[count:]
    slots = home_ref.shape[0]
    me = meta_ref[6 * slots]
    tiled = tiled_ref[...]
    for block in range(B):
        values = tiled * spread_ref[block : block + 1, :]
        high = values.astype(jnp.bfloat16)
        kron_high_ref[block * B : (block + 1) * B, :] = high
        kron_low_ref[block * B : (block + 1) * B, :] = (
            values - high.astype(jnp.float32)
        ).astype(jnp.bfloat16)
    lane = lax.broadcasted_iota(jnp.int32, (B, PLANE), 1)
    lane_b = lane // B
    lane_c = lane % B
    row = lax.broadcasted_iota(jnp.int32, (B, B), 0)
    col = lax.broadcasted_iota(jnp.int32, (B, B), 1)
    for slot in range(slots):
        d_a = meta_ref[3 * slot]
        d_b = meta_ref[3 * slot + 1]
        d_c = meta_ref[3 * slot + 2]
        pick = (col == row + d_a).astype(jnp.bfloat16)
        moved = jnp.dot(pick, part_ref[slot], preferred_element_type=jnp.float32)
        step = d_b * B + d_c
        moved = pltpu.roll(moved, (PLANE - step) % PLANE, 1)
        inside = (
            (lane_b + d_b >= 0) & (lane_b + d_b < B) & (lane_c + d_c >= 0) & (lane_c + d_c < B)
        )
        moved = jnp.where(inside, moved, 0.0)
        shifted_ref[slot] = moved
        work_ref[slot * B : (slot + 1) * B, :] = home_ref[slot].astype(jnp.float32) * moved

    kron_high = kron_high_ref[...]
    kron_low = kron_low_ref[...]
    rows_high = rows_high_ref[...]
    rows_low = rows_low_ref[...]
    coef = dot3_left(rows_high, rows_low, dot3(work_ref[...], kron_high, kron_low))
    eigen = eigen_ref[...]
    for slot in range(slots):
        work_ref[slot * B : (slot + 1) * B, :] = coef[slot * B : (slot + 1) * B, :] / eigen
    potential = dot3_left(rows_high, rows_low, dot3(work_ref[...], kron_high, kron_low))

    for slot in range(slots):
        d_a = meta_ref[3 * slot]
        d_b = meta_ref[3 * slot + 1]
        d_c = meta_ref[3 * slot + 2]
        live = meta_ref[3 * slots + slot] > 0
        here = potential[slot * B : (slot + 1) * B, :]
        tag_home = jnp.full((1, 128), meta_ref[4 * slots + slot].astype(jnp.float32))
        tag_part = jnp.full((1, 128), meta_ref[5 * slots + slot].astype(jnp.float32))
        emit(payload_ref, stage_ref, slot, jnp.where(live, here * shifted_ref[slot], 0.0), tag_home, me)
        product = here * home_ref[slot].astype(jnp.float32)
        pick = (col == row - d_a).astype(jnp.bfloat16)
        moved = exact_rows(pick, product)
        step = d_b * B + d_c
        moved = pltpu.roll(moved, (PLANE + step) % PLANE, 1)
        inside = (
            (lane_b - d_b >= 0) & (lane_b - d_b < B) & (lane_c - d_c >= 0) & (lane_c - d_c < B)
        )
        emit(
            payload_ref, stage_ref, slots + slot, jnp.where(live & inside, moved, 0.0), tag_part, me
        )


def pair_fields(meta, home, part, count, chunk):
    slots = home.shape[0]
    tiled, spread, rows_high, rows_low, eigen = host_tables(slots)
    smem = pl.BlockSpec(memory_space=pltpu.SMEM)
    vmem = pl.BlockSpec(memory_space=pltpu.VMEM)
    box = jax.ShapeDtypeStruct((2 * slots, chunk + 128), jnp.float32)
    return pl.pallas_call(
        functools.partial(pair_kernel, count),
        out_shape=tuple([box] * count),
        in_specs=[smem] + [vmem] * 7,
        out_specs=tuple([vmem] * count),
        scratch_shapes=[
            pltpu.VMEM((slots, B, PLANE), jnp.float32),
            pltpu.VMEM((slots * B, PLANE), jnp.float32),
            pltpu.VMEM((PLANE, PLANE), jnp.bfloat16),
            pltpu.VMEM((PLANE, PLANE), jnp.bfloat16),
            pltpu.VMEM((B, PLANE), jnp.float32),
        ],
    )(meta, home, part, tiled, spread, rows_high, rows_low, eigen)


def exchange(blocks, axis):
    count = len(blocks)
    received = [blocks[0]]
    for step in range(1, count):
        pairs = [(source, (source + step) % count) for source in range(count)]
        received.append(lax.ppermute(blocks[step], axis, pairs))
    return received


def per_device(orbitals, offsets, sends, pair_home, pair_visit, pair_count):
    home_count = orbitals.shape[0]
    cell_count = orbitals.shape[1]
    section_total = sends.shape[1]
    per_target = sends.shape[2]
    slot_total = section_total * per_target
    slots = pair_home.shape[2]
    extra = 128
    me = lax.axis_index("home")
    ahead = (me + jnp.arange(section_total, dtype=jnp.int32)) % section_total
    chosen = sends[0][ahead]
    flat_chosen = chosen.reshape(-1)
    outgoing = jnp.concatenate(
        [
            orbitals[flat_chosen],
            jnp.pad(offsets[flat_chosen].astype(jnp.bfloat16), ((0, 0), (0, extra - 3))),
        ],
        axis=1,
    ).reshape(section_total, per_target, cell_count + extra)
    arrived = exchange(outgoing, "home")
    visitors = jnp.stack(
        [block[:, :cell_count].reshape(per_target, B, PLANE) for block in arrived]
    ).reshape(slot_total, B, PLANE)
    visit_offsets = jnp.stack(
        [block[:, cell_count : cell_count + 3] for block in arrived]
    ).reshape(slot_total, 3).astype(jnp.int32)

    home_slot = pair_home[0, 0]
    visit_code = pair_visit[0, 0]
    source = visit_code // per_target
    visit_slot = ((me - source) % section_total) * per_target + visit_code % per_target
    return_slot = ((source - me) % section_total) * per_target + visit_code % per_target
    live = (jnp.arange(slots, dtype=jnp.int32) < pair_count[0, 0]).astype(jnp.int32)
    home_orb = orbitals[home_slot].reshape(slots, B, PLANE)
    part_orb = visitors[visit_slot]
    delta = offsets[home_slot] - visit_offsets[visit_slot]
    pair_total = lax.psum(1, "pair")
    chunk = cell_count // pair_total
    pair_me = lax.axis_index("pair")
    meta = jnp.concatenate(
        [
            delta.reshape(-1),
            live,
            home_slot,
            home_count + return_slot,
            jnp.reshape(pair_me, (1,)).astype(jnp.int32),
        ]
    )
    payload = pair_fields(meta, home_orb, part_orb, pair_total, chunk)
    got = jnp.stack(exchange(payload, "pair"))
    got_ids = got[:, :, chunk].astype(jnp.int32)
    all_rows = jnp.arange(home_count + slot_total, dtype=jnp.int32)
    picker = (got_ids[:, :, None] == all_rows[None, None, :]).astype(jnp.float32)
    totals = jnp.einsum("srk,srl->kl", picker, got[:, :, :chunk], precision=PRECISE)
    home_totals = totals[:home_count]
    back = (-jnp.arange(section_total, dtype=jnp.int32)) % section_total
    visit_totals = totals[home_count:].reshape(section_total, per_target, chunk)
    returned = jnp.stack(exchange(visit_totals, "home")).reshape(slot_total, chunk)
    owners = chosen[back].reshape(-1)
    chooser = (owners[:, None] == jnp.arange(home_count, dtype=jnp.int32)[None, :]).astype(
        jnp.float32
    )
    return home_totals + jnp.dot(chooser.T, returned, precision=PRECISE)


def solution(mesh):
    in_specs = (
        P("home", None),
        P("home", None),
        P("home", None, None),
        P("home", "pair", None),
        P("home", "pair", None),
        P("home", "pair"),
    )
    out_specs = P("home", "pair")
    return jax.shard_map(
        per_device, mesh=mesh, in_specs=in_specs, out_specs=out_specs, check_vma=False
    )
```

```python
import functools

import jax
import jax.numpy as jnp
import ml_dtypes
import numpy as np
from jax import lax
from jax.experimental import pallas as pl
from jax.experimental.pallas import tpu as pltpu
from jax.sharding import PartitionSpec as P

B = 32
PLANE = B * B


PRECISE = lax.Precision.HIGHEST


def sine_table():
    grid = jnp.arange(B, dtype=jnp.float32) + 1.0
    return jnp.sqrt(2.0 / (B + 1.0)) * jnp.sin(jnp.pi * grid[:, None] * grid[None, :] / (B + 1.0))


def eigen_sum():
    grid = jnp.arange(B, dtype=jnp.float32) + 1.0
    single = 2.0 - 2.0 * jnp.cos(jnp.pi * grid / (B + 1.0))
    return single[:, None, None] + single[None, :, None] + single[None, None, :]


def host_tables(slots):
    grid = np.arange(B, dtype=np.float32) + np.float32(1.0)
    angle = np.float32(np.pi) * grid[:, None] * grid[None, :] / np.float32(B + 1.0)
    table = (np.sqrt(np.float32(2.0 / (B + 1.0))) * np.sin(angle)).astype(np.float32)
    tiled = np.tile(table, (1, B))
    spread = np.repeat(table, B, axis=1)
    rows = np.kron(np.eye(slots, dtype=np.float32), table).astype(np.float32)
    rows_high = rows.astype(ml_dtypes.bfloat16)
    rows_low = (rows - rows_high.astype(np.float32)).astype(ml_dtypes.bfloat16)
    single = (np.float32(2.0) - np.float32(2.0) * np.cos(np.float32(np.pi) * grid / np.float32(B + 1.0))).astype(np.float32)
    eigen = (single[:, None, None] + single[None, :, None] + single[None, None, :]).reshape(B, PLANE)
    return tiled, spread, rows_high, rows_low, eigen.astype(np.float32)


def split(values):
    high = values.astype(jnp.bfloat16)
    low = (values - high.astype(jnp.float32)).astype(jnp.bfloat16)
    return high, low


def split_outside(values):
    high = lax.reduce_precision(values, exponent_bits=8, mantissa_bits=7)
    return high.astype(jnp.bfloat16), (values - high).astype(jnp.bfloat16)


def dot3(left, right_high, right_low):
    high, low = split(left)
    out = jnp.dot(high, right_high, preferred_element_type=jnp.float32)
    out = out + jnp.dot(low, right_high, preferred_element_type=jnp.float32)
    return out + jnp.dot(high, right_low, preferred_element_type=jnp.float32)


def dot3_left(left_high, left_low, right):
    high, low = split(right)
    out = jnp.dot(left_high, high, preferred_element_type=jnp.float32)
    out = out + jnp.dot(left_low, high, preferred_element_type=jnp.float32)
    return out + jnp.dot(left_high, low, preferred_element_type=jnp.float32)


def exact_rows(matrix, values):
    first = values.astype(jnp.bfloat16)
    rest = values - first.astype(jnp.float32)
    second = rest.astype(jnp.bfloat16)
    third = (rest - second.astype(jnp.float32)).astype(jnp.bfloat16)
    out = jnp.dot(matrix, first, preferred_element_type=jnp.float32)
    out = out + jnp.dot(matrix, second, preferred_element_type=jnp.float32)
    return out + jnp.dot(matrix, third, preferred_element_type=jnp.float32)


def emit(payload_refs, stage_ref, row, values, tag, me):
    count = len(payload_refs)
    chunk = payload_refs[0].shape[1] - 128
    stage_ref[...] = values
    for step in range(count):
        index = lax.rem(me + step, count)
        out = payload_refs[step]
        if chunk >= PLANE:
            per = chunk // PLANE
            for part in range(per):
                out[pl.ds(row, 1), pl.ds(part * PLANE, PLANE)] = stage_ref[
                    pl.ds(index * per + part, 1), :
                ]
        else:
            per = PLANE // chunk
            full = stage_ref[pl.ds(index // per, 1), :]
            piece = index % per
            pick = full[:, 0:chunk]
            for other in range(1, per):
                pick = jnp.where(piece == other, full[:, other * chunk : (other + 1) * chunk], pick)
            out[pl.ds(row, 1), pl.ds(0, chunk)] = pick
        out[pl.ds(row, 1), pl.ds(chunk, 128)] = tag


def pair_kernel(
    count,
    meta_ref,
    home_ref,
    part_ref,
    tiled_ref,
    spread_ref,
    rows_high_ref,
    rows_low_ref,
    eigen_ref,
    *rest,
):
    payload_ref = rest[:count]
    shifted_ref, work_ref, kron_high_ref, kron_low_ref, stage_ref = rest[count:]
    slots = home_ref.shape[0]
    me = meta_ref[6 * slots]
    tiled = tiled_ref[...]
    for block in range(B):
        values = tiled * spread_ref[block : block + 1, :]
        high = values.astype(jnp.bfloat16)
        kron_high_ref[block * B : (block + 1) * B, :] = high
        kron_low_ref[block * B : (block + 1) * B, :] = (
            values - high.astype(jnp.float32)
        ).astype(jnp.bfloat16)
    lane = lax.broadcasted_iota(jnp.int32, (B, PLANE), 1)
    lane_b = lane // B
    lane_c = lane % B
    row = lax.broadcasted_iota(jnp.int32, (B, B), 0)
    col = lax.broadcasted_iota(jnp.int32, (B, B), 1)
    for slot in range(slots):
        d_a = meta_ref[3 * slot]
        d_b = meta_ref[3 * slot + 1]
        d_c = meta_ref[3 * slot + 2]
        pick = (col == row + d_a).astype(jnp.bfloat16)
        moved = jnp.dot(pick, part_ref[slot], preferred_element_type=jnp.float32)
        step = d_b * B + d_c
        moved = pltpu.roll(moved, (PLANE - step) % PLANE, 1)
        inside = (
            (lane_b + d_b >= 0) & (lane_b + d_b < B) & (lane_c + d_c >= 0) & (lane_c + d_c < B)
        )
        moved = jnp.where(inside, moved, 0.0)
        shifted_ref[slot] = moved
        work_ref[slot * B : (slot + 1) * B, :] = home_ref[slot].astype(jnp.float32) * moved

    kron_high = kron_high_ref[...]
    kron_low = kron_low_ref[...]
    rows_high = rows_high_ref[...]
    rows_low = rows_low_ref[...]
    coef = dot3_left(rows_high, rows_low, dot3(work_ref[...], kron_high, kron_low))
    eigen = eigen_ref[...]
    for slot in range(slots):
        work_ref[slot * B : (slot + 1) * B, :] = coef[slot * B : (slot + 1) * B, :] / eigen
    potential = dot3_left(rows_high, rows_low, dot3(work_ref[...], kron_high, kron_low))

    for slot in range(slots):
        d_a = meta_ref[3 * slot]
        d_b = meta_ref[3 * slot + 1]
        d_c = meta_ref[3 * slot + 2]
        live = meta_ref[3 * slots + slot] > 0
        here = potential[slot * B : (slot + 1) * B, :]
        tag_home = jnp.full((1, 128), meta_ref[4 * slots + slot].astype(jnp.float32))
        tag_part = jnp.full((1, 128), meta_ref[5 * slots + slot].astype(jnp.float32))
        emit(payload_ref, stage_ref, slot, jnp.where(live, here * shifted_ref[slot], 0.0), tag_home, me)
        product = here * home_ref[slot].astype(jnp.float32)
        pick = (col == row - d_a).astype(jnp.bfloat16)
        moved = exact_rows(pick, product)
        step = d_b * B + d_c
        moved = pltpu.roll(moved, (PLANE + step) % PLANE, 1)
        inside = (
            (lane_b - d_b >= 0) & (lane_b - d_b < B) & (lane_c - d_c >= 0) & (lane_c - d_c < B)
        )
        emit(
            payload_ref, stage_ref, slots + slot, jnp.where(live & inside, moved, 0.0), tag_part, me
        )


def pair_fields(meta, home, part, count, chunk):
    slots = home.shape[0]
    tiled, spread, rows_high, rows_low, eigen = host_tables(slots)
    smem = pl.BlockSpec(memory_space=pltpu.SMEM)
    vmem = pl.BlockSpec(memory_space=pltpu.VMEM)
    box = jax.ShapeDtypeStruct((2 * slots, chunk + 128), jnp.float32)
    return pl.pallas_call(
        functools.partial(pair_kernel, count),
        out_shape=tuple([box] * count),
        in_specs=[smem] + [vmem] * 7,
        out_specs=tuple([vmem] * count),
        scratch_shapes=[
            pltpu.VMEM((slots, B, PLANE), jnp.float32),
            pltpu.VMEM((slots * B, PLANE), jnp.float32),
            pltpu.VMEM((PLANE, PLANE), jnp.bfloat16),
            pltpu.VMEM((PLANE, PLANE), jnp.bfloat16),
            pltpu.VMEM((B, PLANE), jnp.float32),
        ],
    )(meta, home, part, tiled, spread, rows_high, rows_low, eigen)


def exchange(blocks, axis):
    count = len(blocks)
    received = [blocks[0]]
    for step in range(1, count):
        pairs = [(source, (source + step) % count) for source in range(count)]
        received.append(lax.ppermute(blocks[step], axis, pairs))
    return received


def per_device(orbitals, offsets, sends, pair_home, pair_visit, pair_count):
    home_count = orbitals.shape[0]
    cell_count = orbitals.shape[1]
    section_total = sends.shape[1]
    per_target = sends.shape[2]
    slot_total = section_total * per_target
    slots = pair_home.shape[2]
    extra = 128
    me = lax.axis_index("home")
    chosen = lax.dynamic_slice_in_dim(jnp.concatenate([sends[0], sends[0]]), me, section_total)
    flat_chosen = chosen.reshape(-1)
    outgoing = jnp.concatenate(
        [
            orbitals[flat_chosen],
            jnp.pad(offsets[flat_chosen].astype(jnp.bfloat16), ((0, 0), (0, extra - 3))),
        ],
        axis=1,
    ).reshape(section_total, per_target, cell_count + extra)
    arrived = exchange(outgoing, "home")
    visitors = jnp.stack(
        [block[:, :cell_count].reshape(per_target, B, PLANE) for block in arrived]
    ).reshape(slot_total, B, PLANE)
    visit_offsets = jnp.stack(
        [block[:, cell_count : cell_count + 3] for block in arrived]
    ).reshape(slot_total, 3).astype(jnp.int32)

    home_slot = pair_home[0, 0]
    visit_code = pair_visit[0, 0]
    source = visit_code // per_target
    visit_slot = ((me - source) % section_total) * per_target + visit_code % per_target
    return_slot = ((source - me) % section_total) * per_target + visit_code % per_target
    live = (jnp.arange(slots, dtype=jnp.int32) < pair_count[0, 0]).astype(jnp.int32)
    home_orb = orbitals[home_slot].reshape(slots, B, PLANE)
    part_orb = visitors[visit_slot]
    delta = offsets[home_slot] - visit_offsets[visit_slot]
    pair_total = lax.psum(1, "pair")
    chunk = cell_count // pair_total
    pair_me = lax.axis_index("pair")
    meta = jnp.concatenate(
        [
            delta.reshape(-1),
            live,
            home_slot,
            home_count + return_slot,
            jnp.reshape(pair_me, (1,)).astype(jnp.int32),
        ]
    )
    payload = pair_fields(meta, home_orb, part_orb, pair_total, chunk)
    got = jnp.stack(exchange(payload, "pair"))
    got_ids = got[:, :, chunk].astype(jnp.int32)
    all_rows = jnp.arange(home_count + slot_total, dtype=jnp.int32)
    picker = (got_ids[:, :, None] == all_rows[None, None, :]).astype(jnp.float32)
    totals = jnp.einsum("srk,srl->kl", picker, got[:, :, :chunk], precision=lax.Precision.HIGH)
    home_totals = totals[:home_count]
    back = (-jnp.arange(section_total, dtype=jnp.int32)) % section_total
    visit_totals = totals[home_count:].reshape(section_total, per_target, chunk)
    returned = jnp.stack(exchange(visit_totals, "home")).reshape(slot_total, chunk)
    owners = chosen[back].reshape(-1)
    chooser = (owners[:, None] == jnp.arange(home_count, dtype=jnp.int32)[None, :]).astype(
        jnp.float32
    )
    return home_totals + jnp.dot(chooser.T, returned, precision=lax.Precision.HIGH)


def solution(mesh):
    in_specs = (
        P("home", None),
        P("home", None),
        P("home", None, None),
        P("home", "pair", None),
        P("home", "pair", None),
        P("home", "pair"),
    )
    out_specs = P("home", "pair")
    return jax.shard_map(
        per_device, mesh=mesh, in_specs=in_specs, out_specs=out_specs, check_vma=False
    )
```

```python
import functools

import jax
import jax.numpy as jnp
import ml_dtypes
import numpy as np
from jax import lax
from jax.experimental import pallas as pl
from jax.experimental.pallas import tpu as pltpu
from jax.sharding import PartitionSpec as P

B = 32
PLANE = B * B


PRECISE = lax.Precision.HIGHEST


def sine_table():
    grid = jnp.arange(B, dtype=jnp.float32) + 1.0
    return jnp.sqrt(2.0 / (B + 1.0)) * jnp.sin(jnp.pi * grid[:, None] * grid[None, :] / (B + 1.0))


def eigen_sum():
    grid = jnp.arange(B, dtype=jnp.float32) + 1.0
    single = 2.0 - 2.0 * jnp.cos(jnp.pi * grid / (B + 1.0))
    return single[:, None, None] + single[None, :, None] + single[None, None, :]


def host_tables(slots):
    grid = np.arange(B, dtype=np.float32) + np.float32(1.0)
    angle = np.float32(np.pi) * grid[:, None] * grid[None, :] / np.float32(B + 1.0)
    table = (np.sqrt(np.float32(2.0 / (B + 1.0))) * np.sin(angle)).astype(np.float32)
    tiled = np.tile(table, (1, B))
    spread = np.repeat(table, B, axis=1)
    rows = np.kron(np.eye(slots, dtype=np.float32), table).astype(np.float32)
    rows_high = rows.astype(ml_dtypes.bfloat16)
    rows_low = (rows - rows_high.astype(np.float32)).astype(ml_dtypes.bfloat16)
    single = (np.float32(2.0) - np.float32(2.0) * np.cos(np.float32(np.pi) * grid / np.float32(B + 1.0))).astype(np.float32)
    eigen = (single[:, None, None] + single[None, :, None] + single[None, None, :]).reshape(B, PLANE)
    return tiled, spread, rows_high, rows_low, eigen.astype(np.float32)


def split(values):
    high = values.astype(jnp.bfloat16)
    low = (values - high.astype(jnp.float32)).astype(jnp.bfloat16)
    return high, low


def split_outside(values):
    high = lax.reduce_precision(values, exponent_bits=8, mantissa_bits=7)
    return high.astype(jnp.bfloat16), (values - high).astype(jnp.bfloat16)


def dot3(left, right_high, right_low):
    high, low = split(left)
    out = jnp.dot(high, right_high, preferred_element_type=jnp.float32)
    out = out + jnp.dot(low, right_high, preferred_element_type=jnp.float32)
    return out + jnp.dot(high, right_low, preferred_element_type=jnp.float32)


def dot3_left(left_high, left_low, right):
    high, low = split(right)
    out = jnp.dot(left_high, high, preferred_element_type=jnp.float32)
    out = out + jnp.dot(left_low, high, preferred_element_type=jnp.float32)
    return out + jnp.dot(left_high, low, preferred_element_type=jnp.float32)


def exact_rows(matrix, values):
    first = values.astype(jnp.bfloat16)
    rest = values - first.astype(jnp.float32)
    second = rest.astype(jnp.bfloat16)
    third = (rest - second.astype(jnp.float32)).astype(jnp.bfloat16)
    out = jnp.dot(matrix, first, preferred_element_type=jnp.float32)
    out = out + jnp.dot(matrix, second, preferred_element_type=jnp.float32)
    return out + jnp.dot(matrix, third, preferred_element_type=jnp.float32)


def emit(payload_refs, stage_ref, row, values, tag, me):
    count = len(payload_refs)
    chunk = payload_refs[0].shape[1] - 128
    stage_ref[...] = values
    for step in range(count):
        index = lax.rem(me + step, count)
        out = payload_refs[step]
        if chunk >= PLANE:
            per = chunk // PLANE
            for part in range(per):
                out[pl.ds(row, 1), pl.ds(part * PLANE, PLANE)] = stage_ref[
                    pl.ds(index * per + part, 1), :
                ]
        else:
            per = PLANE // chunk
            full = stage_ref[pl.ds(index // per, 1), :]
            piece = index % per
            pick = full[:, 0:chunk]
            for other in range(1, per):
                pick = jnp.where(piece == other, full[:, other * chunk : (other + 1) * chunk], pick)
            out[pl.ds(row, 1), pl.ds(0, chunk)] = pick
        out[pl.ds(row, 1), pl.ds(chunk, 128)] = tag


def pair_kernel(
    count,
    meta_ref,
    home_ref,
    part_ref,
    tiled_ref,
    spread_ref,
    rows_high_ref,
    rows_low_ref,
    eigen_ref,
    *rest,
):
    payload_ref = rest[:count]
    shifted_ref, work_ref, kron_high_ref, kron_low_ref, stage_ref = rest[count:]
    slots = home_ref.shape[0]
    me = meta_ref[6 * slots]
    tiled = tiled_ref[...]
    for block in range(B):
        values = tiled * spread_ref[block : block + 1, :]
        high = values.astype(jnp.bfloat16)
        kron_high_ref[block * B : (block + 1) * B, :] = high
        kron_low_ref[block * B : (block + 1) * B, :] = (
            values - high.astype(jnp.float32)
        ).astype(jnp.bfloat16)
    lane = lax.broadcasted_iota(jnp.int32, (B, PLANE), 1)
    lane_b = lane // B
    lane_c = lane % B
    row = lax.broadcasted_iota(jnp.int32, (B, B), 0)
    col = lax.broadcasted_iota(jnp.int32, (B, B), 1)
    for slot in range(slots):
        d_a = meta_ref[3 * slot]
        d_b = meta_ref[3 * slot + 1]
        d_c = meta_ref[3 * slot + 2]
        pick = (col == row + d_a).astype(jnp.bfloat16)
        moved = jnp.dot(pick, part_ref[slot], preferred_element_type=jnp.float32)
        step = d_b * B + d_c
        moved = pltpu.roll(moved, (PLANE - step) % PLANE, 1)
        inside = (
            (lane_b + d_b >= 0) & (lane_b + d_b < B) & (lane_c + d_c >= 0) & (lane_c + d_c < B)
        )
        moved = jnp.where(inside, moved, 0.0)
        shifted_ref[slot] = moved
        work_ref[slot * B : (slot + 1) * B, :] = home_ref[slot].astype(jnp.float32) * moved

    kron_high = kron_high_ref[...]
    kron_low = kron_low_ref[...]
    rows_high = rows_high_ref[...]
    rows_low = rows_low_ref[...]
    coef = dot3_left(rows_high, rows_low, dot3(work_ref[...], kron_high, kron_low))
    eigen = eigen_ref[...]
    for slot in range(slots):
        work_ref[slot * B : (slot + 1) * B, :] = coef[slot * B : (slot + 1) * B, :] / eigen
    potential = dot3_left(rows_high, rows_low, dot3(work_ref[...], kron_high, kron_low))

    for slot in range(slots):
        d_a = meta_ref[3 * slot]
        d_b = meta_ref[3 * slot + 1]
        d_c = meta_ref[3 * slot + 2]
        live = meta_ref[3 * slots + slot] > 0
        here = potential[slot * B : (slot + 1) * B, :]
        tag_home = jnp.full((1, 128), meta_ref[4 * slots + slot].astype(jnp.float32))
        tag_part = jnp.full((1, 128), meta_ref[5 * slots + slot].astype(jnp.float32))
        emit(payload_ref, stage_ref, slot, jnp.where(live, here * shifted_ref[slot], 0.0), tag_home, me)
        product = here * home_ref[slot].astype(jnp.float32)
        pick = (col == row - d_a).astype(jnp.bfloat16)
        moved = exact_rows(pick, product)
        step = d_b * B + d_c
        moved = pltpu.roll(moved, (PLANE + step) % PLANE, 1)
        inside = (
            (lane_b - d_b >= 0) & (lane_b - d_b < B) & (lane_c - d_c >= 0) & (lane_c - d_c < B)
        )
        emit(
            payload_ref, stage_ref, slots + slot, jnp.where(live & inside, moved, 0.0), tag_part, me
        )


def pair_fields(meta, home, part, count, chunk):
    slots = home.shape[0]
    tiled, spread, rows_high, rows_low, eigen = host_tables(slots)
    smem = pl.BlockSpec(memory_space=pltpu.SMEM)
    vmem = pl.BlockSpec(memory_space=pltpu.VMEM)
    box = jax.ShapeDtypeStruct((2 * slots, chunk + 128), jnp.float32)
    return pl.pallas_call(
        functools.partial(pair_kernel, count),
        out_shape=tuple([box] * count),
        in_specs=[smem] + [vmem] * 7,
        out_specs=tuple([vmem] * count),
        scratch_shapes=[
            pltpu.VMEM((slots, B, PLANE), jnp.float32),
            pltpu.VMEM((slots * B, PLANE), jnp.float32),
            pltpu.VMEM((PLANE, PLANE), jnp.bfloat16),
            pltpu.VMEM((PLANE, PLANE), jnp.bfloat16),
            pltpu.VMEM((B, PLANE), jnp.float32),
        ],
    )(meta, home, part, tiled, spread, rows_high, rows_low, eigen)


def exchange(blocks, axis):
    count = len(blocks)
    received = [blocks[0]]
    for step in range(1, count):
        pairs = [(source, (source + step) % count) for source in range(count)]
        received.append(lax.ppermute(blocks[step], axis, pairs))
    return received


def pick_rows(indices, table):
    chooser = (indices[:, None] == jnp.arange(table.shape[0], dtype=jnp.int32)[None, :])
    return jnp.dot(chooser.astype(jnp.float32), table.astype(jnp.float32), precision=PRECISE)


def per_device(orbitals, offsets, sends, pair_home, pair_visit, pair_count):
    home_count = orbitals.shape[0]
    cell_count = orbitals.shape[1]
    section_total = sends.shape[1]
    per_target = sends.shape[2]
    slot_total = section_total * per_target
    slots = pair_home.shape[2]
    extra = 128
    me = lax.axis_index("home")
    chosen = lax.dynamic_slice_in_dim(jnp.concatenate([sends[0], sends[0]]), me, section_total)
    flat_chosen = chosen.reshape(-1)
    outgoing = jnp.concatenate(
        [
            orbitals[flat_chosen],
            jnp.pad(pick_rows(flat_chosen, offsets).astype(jnp.bfloat16), ((0, 0), (0, extra - 3))),
        ],
        axis=1,
    ).reshape(section_total, per_target, cell_count + extra)
    arrived = exchange(outgoing, "home")
    visitors = jnp.stack(
        [block[:, :cell_count].reshape(per_target, B, PLANE) for block in arrived]
    ).reshape(slot_total, B, PLANE)
    visit_offsets = jnp.stack(
        [block[:, cell_count : cell_count + 3] for block in arrived]
    ).reshape(slot_total, 3).astype(jnp.int32)

    home_slot = pair_home[0, 0]
    visit_code = pair_visit[0, 0]
    source = visit_code // per_target
    visit_slot = ((me - source) % section_total) * per_target + visit_code % per_target
    return_slot = ((source - me) % section_total) * per_target + visit_code % per_target
    live = (jnp.arange(slots, dtype=jnp.int32) < pair_count[0, 0]).astype(jnp.int32)
    home_orb = orbitals[home_slot].reshape(slots, B, PLANE)
    part_orb = visitors[visit_slot]
    delta = pick_rows(home_slot, offsets).astype(jnp.int32) - visit_offsets[visit_slot]
    pair_total = lax.psum(1, "pair")
    chunk = cell_count // pair_total
    pair_me = lax.axis_index("pair")
    meta = jnp.concatenate(
        [
            delta.reshape(-1),
            live,
            home_slot,
            home_count + return_slot,
            jnp.reshape(pair_me, (1,)).astype(jnp.int32),
        ]
    )
    payload = pair_fields(meta, home_orb, part_orb, pair_total, chunk)
    got = jnp.stack(exchange(payload, "pair"))
    got_ids = got[:, :, chunk].astype(jnp.int32)
    all_rows = jnp.arange(home_count + slot_total, dtype=jnp.int32)
    picker = (got_ids[:, :, None] == all_rows[None, None, :]).astype(jnp.float32)
    totals = jnp.einsum("srk,srl->kl", picker, got[:, :, :chunk], precision=lax.Precision.HIGH)
    home_totals = totals[:home_count]
    back = (-jnp.arange(section_total, dtype=jnp.int32)) % section_total
    visit_totals = totals[home_count:].reshape(section_total, per_target, chunk)
    returned = jnp.stack(exchange(visit_totals, "home")).reshape(slot_total, chunk)
    owners = chosen[back].reshape(-1)
    chooser = (owners[:, None] == jnp.arange(home_count, dtype=jnp.int32)[None, :]).astype(
        jnp.float32
    )
    return home_totals + jnp.dot(chooser.T, returned, precision=lax.Precision.HIGH)


def solution(mesh):
    in_specs = (
        P("home", None),
        P("home", None),
        P("home", None, None),
        P("home", "pair", None),
        P("home", "pair", None),
        P("home", "pair"),
    )
    out_specs = P("home", "pair")
    return jax.shard_map(
        per_device, mesh=mesh, in_specs=in_specs, out_specs=out_specs, check_vma=False
    )
```

```python
import functools

import jax
import jax.numpy as jnp
import ml_dtypes
import numpy as np
from jax import lax
from jax.experimental import pallas as pl
from jax.experimental.pallas import tpu as pltpu
from jax.sharding import PartitionSpec as P

B = 32
PLANE = B * B


PRECISE = lax.Precision.HIGHEST


def sine_table():
    grid = jnp.arange(B, dtype=jnp.float32) + 1.0
    return jnp.sqrt(2.0 / (B + 1.0)) * jnp.sin(jnp.pi * grid[:, None] * grid[None, :] / (B + 1.0))


def eigen_sum():
    grid = jnp.arange(B, dtype=jnp.float32) + 1.0
    single = 2.0 - 2.0 * jnp.cos(jnp.pi * grid / (B + 1.0))
    return single[:, None, None] + single[None, :, None] + single[None, None, :]


def host_tables(slots):
    grid = np.arange(B, dtype=np.float32) + np.float32(1.0)
    angle = np.float32(np.pi) * grid[:, None] * grid[None, :] / np.float32(B + 1.0)
    table = (np.sqrt(np.float32(2.0 / (B + 1.0))) * np.sin(angle)).astype(np.float32)
    tiled = np.tile(table, (1, B))
    spread = np.repeat(table, B, axis=1)
    rows = np.kron(np.eye(slots, dtype=np.float32), table).astype(np.float32)
    rows_high = rows.astype(ml_dtypes.bfloat16)
    rows_low = (rows - rows_high.astype(np.float32)).astype(ml_dtypes.bfloat16)
    single = (np.float32(2.0) - np.float32(2.0) * np.cos(np.float32(np.pi) * grid / np.float32(B + 1.0))).astype(np.float32)
    eigen = (single[:, None, None] + single[None, :, None] + single[None, None, :]).reshape(B, PLANE)
    return tiled, spread, rows_high, rows_low, eigen.astype(np.float32)


def split(values):
    high = values.astype(jnp.bfloat16)
    low = (values - high.astype(jnp.float32)).astype(jnp.bfloat16)
    return high, low


def split_outside(values):
    high = lax.reduce_precision(values, exponent_bits=8, mantissa_bits=7)
    return high.astype(jnp.bfloat16), (values - high).astype(jnp.bfloat16)


def dot3(left, right_high, right_low):
    high, low = split(left)
    out = jnp.dot(high, right_high, preferred_element_type=jnp.float32)
    out = out + jnp.dot(low, right_high, preferred_element_type=jnp.float32)
    return out + jnp.dot(high, right_low, preferred_element_type=jnp.float32)


def dot3_left(left_high, left_low, right):
    high, low = split(right)
    out = jnp.dot(left_high, high, preferred_element_type=jnp.float32)
    out = out + jnp.dot(left_low, high, preferred_element_type=jnp.float32)
    return out + jnp.dot(left_high, low, preferred_element_type=jnp.float32)


def exact_rows(matrix, values):
    first = values.astype(jnp.bfloat16)
    rest = values - first.astype(jnp.float32)
    second = rest.astype(jnp.bfloat16)
    third = (rest - second.astype(jnp.float32)).astype(jnp.bfloat16)
    out = jnp.dot(matrix, first, preferred_element_type=jnp.float32)
    out = out + jnp.dot(matrix, second, preferred_element_type=jnp.float32)
    return out + jnp.dot(matrix, third, preferred_element_type=jnp.float32)


def emit(payload_refs, stage_ref, row, values, tag, me):
    count = len(payload_refs)
    chunk = payload_refs[0].shape[1] - 128
    stage_ref[...] = values
    for step in range(count):
        index = lax.rem(me + step, count)
        out = payload_refs[step]
        if chunk >= PLANE:
            per = chunk // PLANE
            for part in range(per):
                out[pl.ds(row, 1), pl.ds(part * PLANE, PLANE)] = stage_ref[
                    pl.ds(index * per + part, 1), :
                ]
        else:
            per = PLANE // chunk
            full = stage_ref[pl.ds(index // per, 1), :]
            piece = index % per
            pick = full[:, 0:chunk]
            for other in range(1, per):
                pick = jnp.where(piece == other, full[:, other * chunk : (other + 1) * chunk], pick)
            out[pl.ds(row, 1), pl.ds(0, chunk)] = pick
        out[pl.ds(row, 1), pl.ds(chunk, 128)] = tag


def pair_kernel(
    count,
    boxes,
    meta_ref,
    home_ref,
    *rest,
):
    box_refs = rest[:boxes]
    pair_kernel_body(count, meta_ref, home_ref, box_refs, *rest[boxes:])


def pair_kernel_body(
    count,
    meta_ref,
    home_ref,
    box_refs,
    tiled_ref,
    spread_ref,
    rows_high_ref,
    rows_low_ref,
    eigen_ref,
    *rest,
):
    payload_ref = rest[:count]
    shifted_ref, work_ref, kron_high_ref, kron_low_ref, stage_ref = rest[count:]
    slots = home_ref.shape[0]
    me = meta_ref[6 * slots]
    tiled = tiled_ref[...]
    for block in range(B):
        values = tiled * spread_ref[block : block + 1, :]
        high = values.astype(jnp.bfloat16)
        kron_high_ref[block * B : (block + 1) * B, :] = high
        kron_low_ref[block * B : (block + 1) * B, :] = (
            values - high.astype(jnp.float32)
        ).astype(jnp.bfloat16)
    lane = lax.broadcasted_iota(jnp.int32, (B, PLANE), 1)
    lane_b = lane // B
    lane_c = lane % B
    row = lax.broadcasted_iota(jnp.int32, (B, B), 0)
    col = lax.broadcasted_iota(jnp.int32, (B, B), 1)
    for slot in range(slots):
        d_a = meta_ref[3 * slot]
        d_b = meta_ref[3 * slot + 1]
        d_c = meta_ref[3 * slot + 2]
        visit = meta_ref[6 * slots + 1 + slot]
        per_box = box_refs[0].shape[0]
        part = box_refs[0][0]
        for index in range(1, len(box_refs) * per_box):
            part = jnp.where(visit == index, box_refs[index // per_box][index % per_box], part)
        pick = (col == row + d_a).astype(jnp.bfloat16)
        moved = jnp.dot(pick, part, preferred_element_type=jnp.float32)
        step = d_b * B + d_c
        moved = pltpu.roll(moved, (PLANE - step) % PLANE, 1)
        inside = (
            (lane_b + d_b >= 0) & (lane_b + d_b < B) & (lane_c + d_c >= 0) & (lane_c + d_c < B)
        )
        moved = jnp.where(inside, moved, 0.0)
        shifted_ref[slot] = moved
        work_ref[slot * B : (slot + 1) * B, :] = home_ref[slot].astype(jnp.float32) * moved

    kron_high = kron_high_ref[...]
    kron_low = kron_low_ref[...]
    rows_high = rows_high_ref[...]
    rows_low = rows_low_ref[...]
    coef = dot3_left(rows_high, rows_low, dot3(work_ref[...], kron_high, kron_low))
    eigen = eigen_ref[...]
    for slot in range(slots):
        work_ref[slot * B : (slot + 1) * B, :] = coef[slot * B : (slot + 1) * B, :] / eigen
    potential = dot3_left(rows_high, rows_low, dot3(work_ref[...], kron_high, kron_low))

    for slot in range(slots):
        d_a = meta_ref[3 * slot]
        d_b = meta_ref[3 * slot + 1]
        d_c = meta_ref[3 * slot + 2]
        live = meta_ref[3 * slots + slot] > 0
        here = potential[slot * B : (slot + 1) * B, :]
        tag_home = jnp.full((1, 128), meta_ref[4 * slots + slot].astype(jnp.float32))
        tag_part = jnp.full((1, 128), meta_ref[5 * slots + slot].astype(jnp.float32))
        emit(payload_ref, stage_ref, slot, jnp.where(live, here * shifted_ref[slot], 0.0), tag_home, me)
        product = here * home_ref[slot].astype(jnp.float32)
        pick = (col == row - d_a).astype(jnp.bfloat16)
        moved = exact_rows(pick, product)
        step = d_b * B + d_c
        moved = pltpu.roll(moved, (PLANE + step) % PLANE, 1)
        inside = (
            (lane_b - d_b >= 0) & (lane_b - d_b < B) & (lane_c - d_c >= 0) & (lane_c - d_c < B)
        )
        emit(
            payload_ref, stage_ref, slots + slot, jnp.where(live & inside, moved, 0.0), tag_part, me
        )


def pair_fields(meta, home, boxes, count, chunk):
    slots = home.shape[0]
    tiled, spread, rows_high, rows_low, eigen = host_tables(slots)
    smem = pl.BlockSpec(memory_space=pltpu.SMEM)
    vmem = pl.BlockSpec(memory_space=pltpu.VMEM)
    box = jax.ShapeDtypeStruct((2 * slots, chunk + 128), jnp.float32)
    return pl.pallas_call(
        functools.partial(pair_kernel, count, len(boxes)),
        out_shape=tuple([box] * count),
        in_specs=[smem] + [vmem] * (6 + len(boxes)),
        out_specs=tuple([vmem] * count),
        scratch_shapes=[
            pltpu.VMEM((slots, B, PLANE), jnp.float32),
            pltpu.VMEM((slots * B, PLANE), jnp.float32),
            pltpu.VMEM((PLANE, PLANE), jnp.bfloat16),
            pltpu.VMEM((PLANE, PLANE), jnp.bfloat16),
            pltpu.VMEM((B, PLANE), jnp.float32),
        ],
    )(meta, home, *boxes, tiled, spread, rows_high, rows_low, eigen)


def exchange(blocks, axis):
    count = len(blocks)
    received = [blocks[0]]
    for step in range(1, count):
        pairs = [(source, (source + step) % count) for source in range(count)]
        received.append(lax.ppermute(blocks[step], axis, pairs))
    return received


def pick_rows(indices, table):
    chooser = (indices[:, None] == jnp.arange(table.shape[0], dtype=jnp.int32)[None, :])
    return jnp.dot(chooser.astype(jnp.float32), table.astype(jnp.float32), precision=PRECISE)


def per_device(orbitals, offsets, sends, pair_home, pair_visit, pair_count):
    home_count = orbitals.shape[0]
    cell_count = orbitals.shape[1]
    section_total = sends.shape[1]
    per_target = sends.shape[2]
    slot_total = section_total * per_target
    slots = pair_home.shape[2]
    extra = 128
    me = lax.axis_index("home")
    chosen = lax.dynamic_slice_in_dim(jnp.concatenate([sends[0], sends[0]]), me, section_total)
    flat_chosen = chosen.reshape(-1)
    outgoing = jnp.concatenate(
        [
            orbitals[flat_chosen],
            jnp.pad(pick_rows(flat_chosen, offsets).astype(jnp.bfloat16), ((0, 0), (0, extra - 3))),
        ],
        axis=1,
    ).reshape(section_total, per_target, cell_count + extra)
    arrived = exchange(outgoing, "home")
    visitors = [block[:, :cell_count].reshape(per_target, B, PLANE) for block in arrived]
    visit_offsets = jnp.stack(
        [block[:, cell_count : cell_count + 3] for block in arrived]
    ).reshape(slot_total, 3).astype(jnp.int32)

    home_slot = pair_home[0, 0]
    visit_code = pair_visit[0, 0]
    source = visit_code // per_target
    visit_slot = ((me - source) % section_total) * per_target + visit_code % per_target
    return_slot = ((source - me) % section_total) * per_target + visit_code % per_target
    live = (jnp.arange(slots, dtype=jnp.int32) < pair_count[0, 0]).astype(jnp.int32)
    home_orb = orbitals[home_slot].reshape(slots, B, PLANE)
    delta = pick_rows(home_slot, offsets).astype(jnp.int32) - visit_offsets[visit_slot]
    pair_total = lax.psum(1, "pair")
    chunk = cell_count // pair_total
    pair_me = lax.axis_index("pair")
    meta = jnp.concatenate(
        [
            delta.reshape(-1),
            live,
            home_slot,
            home_count + return_slot,
            jnp.reshape(pair_me, (1,)).astype(jnp.int32),
            visit_slot,
        ]
    )
    payload = pair_fields(meta, home_orb, visitors, pair_total, chunk)
    got = jnp.stack(exchange(payload, "pair"))
    got_ids = got[:, :, chunk].astype(jnp.int32)
    all_rows = jnp.arange(home_count + slot_total, dtype=jnp.int32)
    picker = (got_ids[:, :, None] == all_rows[None, None, :]).astype(jnp.float32)
    totals = jnp.einsum("srk,srl->kl", picker, got[:, :, :chunk], precision=lax.Precision.HIGH)
    home_totals = totals[:home_count]
    back = (-jnp.arange(section_total, dtype=jnp.int32)) % section_total
    visit_totals = totals[home_count:].reshape(section_total, per_target, chunk)
    returned = jnp.stack(exchange(visit_totals, "home")).reshape(slot_total, chunk)
    owners = chosen[back].reshape(-1)
    chooser = (owners[:, None] == jnp.arange(home_count, dtype=jnp.int32)[None, :]).astype(
        jnp.float32
    )
    return home_totals + jnp.dot(chooser.T, returned, precision=lax.Precision.HIGH)


def solution(mesh):
    in_specs = (
        P("home", None),
        P("home", None),
        P("home", None, None),
        P("home", "pair", None),
        P("home", "pair", None),
        P("home", "pair"),
    )
    out_specs = P("home", "pair")
    return jax.shard_map(
        per_device, mesh=mesh, in_specs=in_specs, out_specs=out_specs, check_vma=False
    )
```

```python
import functools

import jax
import jax.numpy as jnp
import ml_dtypes
import numpy as np
from jax import lax
from jax.experimental import pallas as pl
from jax.experimental.pallas import tpu as pltpu
from jax.sharding import PartitionSpec as P

B = 32
PLANE = B * B


PRECISE = lax.Precision.HIGHEST


def sine_table():
    grid = jnp.arange(B, dtype=jnp.float32) + 1.0
    return jnp.sqrt(2.0 / (B + 1.0)) * jnp.sin(jnp.pi * grid[:, None] * grid[None, :] / (B + 1.0))


def eigen_sum():
    grid = jnp.arange(B, dtype=jnp.float32) + 1.0
    single = 2.0 - 2.0 * jnp.cos(jnp.pi * grid / (B + 1.0))
    return single[:, None, None] + single[None, :, None] + single[None, None, :]


def host_tables(slots):
    grid = np.arange(B, dtype=np.float32) + np.float32(1.0)
    angle = np.float32(np.pi) * grid[:, None] * grid[None, :] / np.float32(B + 1.0)
    table = (np.sqrt(np.float32(2.0 / (B + 1.0))) * np.sin(angle)).astype(np.float32)
    tiled = np.tile(table, (1, B))
    spread = np.repeat(table, B, axis=1)
    rows = np.kron(np.eye(slots, dtype=np.float32), table).astype(np.float32)
    rows_high = rows.astype(ml_dtypes.bfloat16)
    rows_low = (rows - rows_high.astype(np.float32)).astype(ml_dtypes.bfloat16)
    single = (np.float32(2.0) - np.float32(2.0) * np.cos(np.float32(np.pi) * grid / np.float32(B + 1.0))).astype(np.float32)
    eigen = (single[:, None, None] + single[None, :, None] + single[None, None, :]).reshape(B, PLANE)
    return tiled, spread, rows_high, rows_low, eigen.astype(np.float32)


def split(values):
    high = values.astype(jnp.bfloat16)
    low = (values - high.astype(jnp.float32)).astype(jnp.bfloat16)
    return high, low


def split_outside(values):
    high = lax.reduce_precision(values, exponent_bits=8, mantissa_bits=7)
    return high.astype(jnp.bfloat16), (values - high).astype(jnp.bfloat16)


def dot3(left, right_high, right_low):
    high, low = split(left)
    out = jnp.dot(high, right_high, preferred_element_type=jnp.float32)
    out = out + jnp.dot(low, right_high, preferred_element_type=jnp.float32)
    return out + jnp.dot(high, right_low, preferred_element_type=jnp.float32)


def dot3_left(left_high, left_low, right):
    high, low = split(right)
    out = jnp.dot(left_high, high, preferred_element_type=jnp.float32)
    out = out + jnp.dot(left_low, high, preferred_element_type=jnp.float32)
    return out + jnp.dot(left_high, low, preferred_element_type=jnp.float32)


def exact_rows(matrix, values):
    first = values.astype(jnp.bfloat16)
    rest = values - first.astype(jnp.float32)
    second = rest.astype(jnp.bfloat16)
    third = (rest - second.astype(jnp.float32)).astype(jnp.bfloat16)
    out = jnp.dot(matrix, first, preferred_element_type=jnp.float32)
    out = out + jnp.dot(matrix, second, preferred_element_type=jnp.float32)
    return out + jnp.dot(matrix, third, preferred_element_type=jnp.float32)


def emit(payload_refs, stage_ref, row, values, tag, me):
    count = len(payload_refs)
    chunk = payload_refs[0].shape[1] - 128
    stage_ref[...] = values
    for step in range(count):
        index = lax.rem(me + step, count)
        out = payload_refs[step]
        if chunk >= PLANE:
            per = chunk // PLANE
            for part in range(per):
                out[pl.ds(row, 1), pl.ds(part * PLANE, PLANE)] = stage_ref[
                    pl.ds(index * per + part, 1), :
                ]
        else:
            per = PLANE // chunk
            full = stage_ref[pl.ds(index // per, 1), :]
            piece = index % per
            pick = full[:, 0:chunk]
            for other in range(1, per):
                pick = jnp.where(piece == other, full[:, other * chunk : (other + 1) * chunk], pick)
            out[pl.ds(row, 1), pl.ds(0, chunk)] = pick
        out[pl.ds(row, 1), pl.ds(chunk, 128)] = tag


def pair_kernel(
    count,
    boxes,
    meta_ref,
    home_ref,
    *rest,
):
    box_refs = rest[:boxes]
    pair_kernel_body(count, meta_ref, home_ref, box_refs, *rest[boxes:])


def pair_kernel_body(
    count,
    meta_ref,
    home_ref,
    box_refs,
    tiled_ref,
    spread_ref,
    rows_high_ref,
    rows_low_ref,
    eigen_ref,
    *rest,
):
    payload_ref = rest[:count]
    shifted_ref, work_ref, kron_high_ref, kron_low_ref, stage_ref = rest[count:]
    slots = home_ref.shape[0]
    me = meta_ref[6 * slots]
    tiled = tiled_ref[...]
    for block in range(B):
        values = tiled * spread_ref[block : block + 1, :]
        high = values.astype(jnp.bfloat16)
        kron_high_ref[block * B : (block + 1) * B, :] = high
        kron_low_ref[block * B : (block + 1) * B, :] = (
            values - high.astype(jnp.float32)
        ).astype(jnp.bfloat16)
    lane = lax.broadcasted_iota(jnp.int32, (B, PLANE), 1)
    lane_b = lane // B
    lane_c = lane % B
    row = lax.broadcasted_iota(jnp.int32, (B, B), 0)
    col = lax.broadcasted_iota(jnp.int32, (B, B), 1)
    for slot in range(slots):
        d_a = meta_ref[3 * slot]
        d_b = meta_ref[3 * slot + 1]
        d_c = meta_ref[3 * slot + 2]
        visit = meta_ref[6 * slots + 1 + slot]
        per_box = box_refs[0].shape[0]
        part = box_refs[0][0]
        for index in range(1, len(box_refs) * per_box):
            part = jnp.where(visit == index, box_refs[index // per_box][index % per_box], part)
        pick = (col == row + d_a).astype(jnp.bfloat16)
        moved = jnp.dot(pick, part, preferred_element_type=jnp.float32)
        step = d_b * B + d_c
        moved = pltpu.roll(moved, (PLANE - step) % PLANE, 1)
        inside = (
            (lane_b + d_b >= 0) & (lane_b + d_b < B) & (lane_c + d_c >= 0) & (lane_c + d_c < B)
        )
        moved = jnp.where(inside, moved, 0.0)
        shifted_ref[slot] = moved
        work_ref[slot * B : (slot + 1) * B, :] = home_ref[slot].astype(jnp.float32) * moved

    kron_high = kron_high_ref[...]
    kron_low = kron_low_ref[...]
    rows_high = rows_high_ref[...]
    rows_low = rows_low_ref[...]
    coef = dot3_left(rows_high, rows_low, dot3(work_ref[...], kron_high, kron_low))
    eigen = eigen_ref[...]
    for slot in range(slots):
        work_ref[slot * B : (slot + 1) * B, :] = coef[slot * B : (slot + 1) * B, :] / eigen
    potential = dot3_left(rows_high, rows_low, dot3(work_ref[...], kron_high, kron_low))

    for slot in range(slots):
        d_a = meta_ref[3 * slot]
        d_b = meta_ref[3 * slot + 1]
        d_c = meta_ref[3 * slot + 2]
        live = meta_ref[3 * slots + slot] > 0
        here = potential[slot * B : (slot + 1) * B, :]
        tag_home = jnp.full((1, 128), meta_ref[4 * slots + slot].astype(jnp.float32))
        tag_part = jnp.full((1, 128), meta_ref[5 * slots + slot].astype(jnp.float32))
        emit(payload_ref, stage_ref, slot, jnp.where(live, here * shifted_ref[slot], 0.0), tag_home, me)
        product = here * home_ref[slot].astype(jnp.float32)
        pick = (col == row - d_a).astype(jnp.bfloat16)
        moved = exact_rows(pick, product)
        step = d_b * B + d_c
        moved = pltpu.roll(moved, (PLANE + step) % PLANE, 1)
        inside = (
            (lane_b - d_b >= 0) & (lane_b - d_b < B) & (lane_c - d_c >= 0) & (lane_c - d_c < B)
        )
        emit(
            payload_ref, stage_ref, slots + slot, jnp.where(live & inside, moved, 0.0), tag_part, me
        )


def pair_fields(meta, home, boxes, count, chunk):
    slots = home.shape[0]
    tiled, spread, rows_high, rows_low, eigen = host_tables(slots)
    smem = pl.BlockSpec(memory_space=pltpu.SMEM)
    vmem = pl.BlockSpec(memory_space=pltpu.VMEM)
    box = jax.ShapeDtypeStruct((2 * slots, chunk + 128), jnp.float32)
    return pl.pallas_call(
        functools.partial(pair_kernel, count, len(boxes)),
        out_shape=tuple([box] * count),
        in_specs=[smem] + [vmem] * (6 + len(boxes)),
        out_specs=tuple([vmem] * count),
        scratch_shapes=[
            pltpu.VMEM((slots, B, PLANE), jnp.float32),
            pltpu.VMEM((slots * B, PLANE), jnp.float32),
            pltpu.VMEM((PLANE, PLANE), jnp.bfloat16),
            pltpu.VMEM((PLANE, PLANE), jnp.bfloat16),
            pltpu.VMEM((B, PLANE), jnp.float32),
        ],
    )(meta, home, *boxes, tiled, spread, rows_high, rows_low, eigen)


def exchange(blocks, axis):
    count = len(blocks)
    received = [blocks[0]]
    for step in range(1, count):
        pairs = [(source, (source + step) % count) for source in range(count)]
        received.append(lax.ppermute(blocks[step], axis, pairs))
    return received


def pick_rows(indices, table):
    chooser = (indices[:, None] == jnp.arange(table.shape[0], dtype=jnp.int32)[None, :])
    return jnp.dot(chooser.astype(jnp.float32), table.astype(jnp.float32), precision=PRECISE)


def per_device(orbitals, offsets, sends, pair_home, pair_visit, pair_count):
    home_count = orbitals.shape[0]
    cell_count = orbitals.shape[1]
    section_total = sends.shape[1]
    per_target = sends.shape[2]
    slot_total = section_total * per_target
    slots = pair_home.shape[2]
    extra = 128
    me = lax.axis_index("home")
    chosen = lax.dynamic_slice_in_dim(jnp.concatenate([sends[0], sends[0]]), me, section_total)
    flat_chosen = chosen.reshape(-1)
    outgoing = jnp.concatenate(
        [
            orbitals[flat_chosen],
            jnp.pad(pick_rows(flat_chosen, offsets).astype(jnp.bfloat16), ((0, 0), (0, extra - 3))),
        ],
        axis=1,
    ).reshape(section_total, per_target, cell_count + extra)
    arrived = exchange(outgoing, "home")
    visitors = [block[:, :cell_count].reshape(per_target, B, PLANE) for block in arrived]
    visit_offsets = jnp.stack(
        [block[:, cell_count : cell_count + 3] for block in arrived]
    ).reshape(slot_total, 3)

    home_slot = pair_home[0, 0]
    visit_code = pair_visit[0, 0]
    source = visit_code // per_target
    visit_slot = ((me - source) % section_total) * per_target + visit_code % per_target
    return_slot = ((source - me) % section_total) * per_target + visit_code % per_target
    live = (jnp.arange(slots, dtype=jnp.int32) < pair_count[0, 0]).astype(jnp.int32)
    home_orb = orbitals[home_slot].reshape(slots, B, PLANE)
    delta = (pick_rows(home_slot, offsets) - pick_rows(visit_slot, visit_offsets)).astype(jnp.int32)
    pair_total = lax.psum(1, "pair")
    chunk = cell_count // pair_total
    pair_me = lax.axis_index("pair")
    meta = jnp.concatenate(
        [
            delta.reshape(-1),
            live,
            home_slot,
            home_count + return_slot,
            jnp.reshape(pair_me, (1,)).astype(jnp.int32),
            visit_slot,
        ]
    )
    payload = pair_fields(meta, home_orb, visitors, pair_total, chunk)
    got = jnp.stack(exchange(payload, "pair"))
    got_ids = got[:, :, chunk].astype(jnp.int32)
    all_rows = jnp.arange(home_count + slot_total, dtype=jnp.int32)
    picker = (got_ids[:, :, None] == all_rows[None, None, :]).astype(jnp.float32)
    totals = jnp.einsum("srk,srl->kl", picker, got[:, :, :chunk], precision=lax.Precision.HIGH)
    home_totals = totals[:home_count]
    back = (-jnp.arange(section_total, dtype=jnp.int32)) % section_total
    visit_totals = totals[home_count:].reshape(section_total, per_target, chunk)
    returned = jnp.stack(exchange(visit_totals, "home")).reshape(slot_total, chunk)
    owners = chosen[back].reshape(-1)
    chooser = (owners[:, None] == jnp.arange(home_count, dtype=jnp.int32)[None, :]).astype(
        jnp.float32
    )
    return home_totals + jnp.dot(chooser.T, returned, precision=lax.Precision.HIGH)


def solution(mesh):
    in_specs = (
        P("home", None),
        P("home", None),
        P("home", None, None),
        P("home", "pair", None),
        P("home", "pair", None),
        P("home", "pair"),
    )
    out_specs = P("home", "pair")
    return jax.shard_map(
        per_device, mesh=mesh, in_specs=in_specs, out_specs=out_specs, check_vma=False
    )
```

```python
import functools

import jax
import jax.numpy as jnp
import ml_dtypes
import numpy as np
from jax import lax
from jax.experimental import pallas as pl
from jax.experimental.pallas import tpu as pltpu
from jax.sharding import PartitionSpec as P

B = 32
PLANE = B * B


PRECISE = lax.Precision.HIGHEST


def sine_table():
    grid = jnp.arange(B, dtype=jnp.float32) + 1.0
    return jnp.sqrt(2.0 / (B + 1.0)) * jnp.sin(jnp.pi * grid[:, None] * grid[None, :] / (B + 1.0))


def eigen_sum():
    grid = jnp.arange(B, dtype=jnp.float32) + 1.0
    single = 2.0 - 2.0 * jnp.cos(jnp.pi * grid / (B + 1.0))
    return single[:, None, None] + single[None, :, None] + single[None, None, :]


def host_tables(slots):
    grid = np.arange(B, dtype=np.float32) + np.float32(1.0)
    angle = np.float32(np.pi) * grid[:, None] * grid[None, :] / np.float32(B + 1.0)
    table = (np.sqrt(np.float32(2.0 / (B + 1.0))) * np.sin(angle)).astype(np.float32)
    tiled = np.tile(table, (1, B))
    spread = np.repeat(table, B, axis=1)
    rows = np.kron(np.eye(slots, dtype=np.float32), table).astype(np.float32)
    rows_high = rows.astype(ml_dtypes.bfloat16)
    rows_low = (rows - rows_high.astype(np.float32)).astype(ml_dtypes.bfloat16)
    single = (np.float32(2.0) - np.float32(2.0) * np.cos(np.float32(np.pi) * grid / np.float32(B + 1.0))).astype(np.float32)
    eigen = (single[:, None, None] + single[None, :, None] + single[None, None, :]).reshape(B, PLANE)
    return tiled, spread, rows_high, rows_low, eigen.astype(np.float32)


def split(values):
    high = values.astype(jnp.bfloat16)
    low = (values - high.astype(jnp.float32)).astype(jnp.bfloat16)
    return high, low


def split_outside(values):
    high = lax.reduce_precision(values, exponent_bits=8, mantissa_bits=7)
    return high.astype(jnp.bfloat16), (values - high).astype(jnp.bfloat16)


def dot3(left, right_high, right_low):
    high, low = split(left)
    out = jnp.dot(high, right_high, preferred_element_type=jnp.float32)
    out = out + jnp.dot(low, right_high, preferred_element_type=jnp.float32)
    return out + jnp.dot(high, right_low, preferred_element_type=jnp.float32)


def dot3_left(left_high, left_low, right):
    high, low = split(right)
    out = jnp.dot(left_high, high, preferred_element_type=jnp.float32)
    out = out + jnp.dot(left_low, high, preferred_element_type=jnp.float32)
    return out + jnp.dot(left_high, low, preferred_element_type=jnp.float32)


def exact_rows(matrix, values):
    first = values.astype(jnp.bfloat16)
    rest = values - first.astype(jnp.float32)
    second = rest.astype(jnp.bfloat16)
    third = (rest - second.astype(jnp.float32)).astype(jnp.bfloat16)
    out = jnp.dot(matrix, first, preferred_element_type=jnp.float32)
    out = out + jnp.dot(matrix, second, preferred_element_type=jnp.float32)
    return out + jnp.dot(matrix, third, preferred_element_type=jnp.float32)


def emit(payload_refs, stage_ref, row, values, tag, me):
    count = len(payload_refs)
    chunk = payload_refs[0].shape[1] - 128
    stage_ref[...] = values
    for step in range(count):
        index = lax.rem(me + step, count)
        out = payload_refs[step]
        if chunk >= PLANE:
            per = chunk // PLANE
            for part in range(per):
                out[pl.ds(row, 1), pl.ds(part * PLANE, PLANE)] = stage_ref[
                    pl.ds(index * per + part, 1), :
                ]
        else:
            per = PLANE // chunk
            full = stage_ref[pl.ds(index // per, 1), :]
            piece = index % per
            pick = full[:, 0:chunk]
            for other in range(1, per):
                pick = jnp.where(piece == other, full[:, other * chunk : (other + 1) * chunk], pick)
            out[pl.ds(row, 1), pl.ds(0, chunk)] = pick
        out[pl.ds(row, 1), pl.ds(chunk, 128)] = tag


def pair_kernel(
    count,
    boxes,
    meta_ref,
    home_ref,
    *rest,
):
    box_refs = rest[:boxes]
    pair_kernel_body(count, meta_ref, home_ref, box_refs, *rest[boxes:])


def pair_kernel_body(
    count,
    meta_ref,
    home_ref,
    box_refs,
    tiled_ref,
    spread_ref,
    rows_high_ref,
    rows_low_ref,
    eigen_ref,
    *rest,
):
    payload_ref = rest[:count]
    shifted_ref, work_ref, kron_high_ref, kron_low_ref, stage_ref = rest[count:]
    slots = home_ref.shape[0]
    me = meta_ref[6 * slots]
    tiled = tiled_ref[...]
    for block in range(B):
        values = tiled * spread_ref[block : block + 1, :]
        high = values.astype(jnp.bfloat16)
        kron_high_ref[block * B : (block + 1) * B, :] = high
        kron_low_ref[block * B : (block + 1) * B, :] = (
            values - high.astype(jnp.float32)
        ).astype(jnp.bfloat16)
    lane = lax.broadcasted_iota(jnp.int32, (B, PLANE), 1)
    lane_b = lane // B
    lane_c = lane % B
    row = lax.broadcasted_iota(jnp.int32, (B, B), 0)
    col = lax.broadcasted_iota(jnp.int32, (B, B), 1)
    for slot in range(slots):
        d_a = meta_ref[3 * slot]
        d_b = meta_ref[3 * slot + 1]
        d_c = meta_ref[3 * slot + 2]
        visit = meta_ref[6 * slots + 1 + slot]
        per_box = box_refs[0].shape[0]
        part = box_refs[0][0]
        for index in range(1, len(box_refs) * per_box):
            part = jnp.where(visit == index, box_refs[index // per_box][index % per_box], part)
        pick = (col == row + d_a).astype(jnp.bfloat16)
        moved = jnp.dot(pick, part, preferred_element_type=jnp.float32)
        step = d_b * B + d_c
        moved = pltpu.roll(moved, (PLANE - step) % PLANE, 1)
        inside = (
            (lane_b + d_b >= 0) & (lane_b + d_b < B) & (lane_c + d_c >= 0) & (lane_c + d_c < B)
        )
        moved = jnp.where(inside, moved, 0.0)
        shifted_ref[slot] = moved
        work_ref[slot * B : (slot + 1) * B, :] = home_ref[slot].astype(jnp.float32) * moved

    kron_high = kron_high_ref[...]
    kron_low = kron_low_ref[...]
    rows_high = rows_high_ref[...]
    rows_low = rows_low_ref[...]
    coef = dot3_left(rows_high, rows_low, dot3(work_ref[...], kron_high, kron_low))
    eigen = eigen_ref[...]
    for slot in range(slots):
        work_ref[slot * B : (slot + 1) * B, :] = coef[slot * B : (slot + 1) * B, :] / eigen
    potential = dot3_left(rows_high, rows_low, dot3(work_ref[...], kron_high, kron_low))

    for slot in range(slots):
        d_a = meta_ref[3 * slot]
        d_b = meta_ref[3 * slot + 1]
        d_c = meta_ref[3 * slot + 2]
        live = meta_ref[3 * slots + slot] > 0
        here = potential[slot * B : (slot + 1) * B, :]
        tag_home = jnp.full((1, 128), meta_ref[4 * slots + slot].astype(jnp.float32))
        tag_part = jnp.full((1, 128), meta_ref[5 * slots + slot].astype(jnp.float32))
        emit(payload_ref, stage_ref, slot, jnp.where(live, here * shifted_ref[slot], 0.0), tag_home, me)
        product = here * home_ref[slot].astype(jnp.float32)
        pick = (col == row - d_a).astype(jnp.bfloat16)
        moved = exact_rows(pick, product)
        step = d_b * B + d_c
        moved = pltpu.roll(moved, (PLANE + step) % PLANE, 1)
        inside = (
            (lane_b - d_b >= 0) & (lane_b - d_b < B) & (lane_c - d_c >= 0) & (lane_c - d_c < B)
        )
        emit(
            payload_ref, stage_ref, slots + slot, jnp.where(live & inside, moved, 0.0), tag_part, me
        )


def pair_fields(meta, home, boxes, count, chunk):
    slots = home.shape[0]
    tiled, spread, rows_high, rows_low, eigen = host_tables(slots)
    smem = pl.BlockSpec(memory_space=pltpu.SMEM)
    vmem = pl.BlockSpec(memory_space=pltpu.VMEM)
    box = jax.ShapeDtypeStruct((2 * slots, chunk + 128), jnp.float32)
    return pl.pallas_call(
        functools.partial(pair_kernel, count, len(boxes)),
        out_shape=tuple([box] * count),
        in_specs=[smem] + [vmem] * (6 + len(boxes)),
        out_specs=tuple([vmem] * count),
        scratch_shapes=[
            pltpu.VMEM((slots, B, PLANE), jnp.float32),
            pltpu.VMEM((slots * B, PLANE), jnp.float32),
            pltpu.VMEM((PLANE, PLANE), jnp.bfloat16),
            pltpu.VMEM((PLANE, PLANE), jnp.bfloat16),
            pltpu.VMEM((B, PLANE), jnp.float32),
        ],
    )(meta, home, *boxes, tiled, spread, rows_high, rows_low, eigen)


def exchange(blocks, axis):
    count = len(blocks)
    received = [blocks[0]]
    for step in range(1, count):
        pairs = [(source, (source + step) % count) for source in range(count)]
        received.append(lax.ppermute(blocks[step], axis, pairs))
    return received


def pick_rows(indices, table):
    chooser = (indices[:, None] == jnp.arange(table.shape[0], dtype=jnp.int32)[None, :])
    return jnp.dot(chooser.astype(jnp.float32), table.astype(jnp.float32), precision=PRECISE)


def per_device(orbitals, offsets, sends, pair_home, pair_visit, pair_count):
    home_count = orbitals.shape[0]
    cell_count = orbitals.shape[1]
    section_total = sends.shape[1]
    per_target = sends.shape[2]
    slot_total = section_total * per_target
    slots = pair_home.shape[2]
    extra = 128
    me = lax.axis_index("home")
    chosen = lax.dynamic_slice_in_dim(jnp.concatenate([sends[0], sends[0]]), me, section_total)
    flat_chosen = chosen.reshape(-1)
    outgoing = jnp.concatenate(
        [
            orbitals[flat_chosen],
            jnp.pad(pick_rows(flat_chosen, offsets).astype(jnp.bfloat16), ((0, 0), (0, extra - 3))),
        ],
        axis=1,
    ).reshape(section_total, per_target, cell_count + extra)
    arrived = exchange(outgoing, "home")
    visitors = [block[:, :cell_count].reshape(per_target, B, PLANE) for block in arrived]
    visit_offsets = jnp.stack(
        [block[:, cell_count : cell_count + 3] for block in arrived]
    ).reshape(slot_total, 3).astype(jnp.int32)

    home_slot = pair_home[0, 0]
    visit_code = pair_visit[0, 0]
    source = visit_code // per_target
    visit_slot = ((me - source) % section_total) * per_target + visit_code % per_target
    return_slot = ((source - me) % section_total) * per_target + visit_code % per_target
    live = (jnp.arange(slots, dtype=jnp.int32) < pair_count[0, 0]).astype(jnp.int32)
    home_orb = orbitals[home_slot].reshape(slots, B, PLANE)
    delta = pick_rows(home_slot, offsets).astype(jnp.int32) - visit_offsets[visit_slot]
    pair_total = lax.psum(1, "pair")
    chunk = cell_count // pair_total
    pair_me = lax.axis_index("pair")
    meta = jnp.concatenate(
        [
            delta.reshape(-1),
            live,
            home_slot,
            home_count + return_slot,
            jnp.reshape(pair_me, (1,)).astype(jnp.int32),
            visit_slot,
        ]
    )
    payload = pair_fields(meta, home_orb, visitors, pair_total, chunk)
    got = jnp.stack(exchange(payload, "pair"))
    got_ids = got[:, :, chunk].astype(jnp.int32)
    all_rows = jnp.arange(home_count + slot_total, dtype=jnp.int32)
    picker = (got_ids[:, :, None] == all_rows[None, None, :]).astype(jnp.float32)
    data = got[:, :, :chunk]
    visit_part = jnp.einsum(
        "srk,srl->kl", picker[:, :, home_count:], data, precision=lax.Precision.HIGH
    )
    home_totals = jnp.einsum(
        "srk,srl->kl", picker[:, :, :home_count], data, precision=lax.Precision.HIGH
    )
    back = (-jnp.arange(section_total, dtype=jnp.int32)) % section_total
    visit_totals = visit_part.reshape(section_total, per_target, chunk)
    returned = jnp.stack(exchange(visit_totals, "home")).reshape(slot_total, chunk)
    owners = chosen[back].reshape(-1)
    chooser = (owners[:, None] == jnp.arange(home_count, dtype=jnp.int32)[None, :]).astype(
        jnp.float32
    )
    return home_totals + jnp.dot(chooser.T, returned, precision=lax.Precision.HIGH)


def solution(mesh):
    in_specs = (
        P("home", None),
        P("home", None),
        P("home", None, None),
        P("home", "pair", None),
        P("home", "pair", None),
        P("home", "pair"),
    )
    out_specs = P("home", "pair")
    return jax.shard_map(
        per_device, mesh=mesh, in_specs=in_specs, out_specs=out_specs, check_vma=False
    )
```

```python
import functools

import jax
import jax.numpy as jnp
import ml_dtypes
import numpy as np
from jax import lax
from jax.experimental import pallas as pl
from jax.experimental.pallas import tpu as pltpu
from jax.sharding import PartitionSpec as P

B = 32
PLANE = B * B


PRECISE = lax.Precision.HIGHEST


def sine_table():
    grid = jnp.arange(B, dtype=jnp.float32) + 1.0
    return jnp.sqrt(2.0 / (B + 1.0)) * jnp.sin(jnp.pi * grid[:, None] * grid[None, :] / (B + 1.0))


def eigen_sum():
    grid = jnp.arange(B, dtype=jnp.float32) + 1.0
    single = 2.0 - 2.0 * jnp.cos(jnp.pi * grid / (B + 1.0))
    return single[:, None, None] + single[None, :, None] + single[None, None, :]


def host_tables(slots):
    grid = np.arange(B, dtype=np.float32) + np.float32(1.0)
    angle = np.float32(np.pi) * grid[:, None] * grid[None, :] / np.float32(B + 1.0)
    table = (np.sqrt(np.float32(2.0 / (B + 1.0))) * np.sin(angle)).astype(np.float32)
    tiled = np.tile(table, (1, B))
    spread = np.repeat(table, B, axis=1)
    rows = np.kron(np.eye(slots, dtype=np.float32), table).astype(np.float32)
    rows_high = rows.astype(ml_dtypes.bfloat16)
    rows_low = (rows - rows_high.astype(np.float32)).astype(ml_dtypes.bfloat16)
    single = (np.float32(2.0) - np.float32(2.0) * np.cos(np.float32(np.pi) * grid / np.float32(B + 1.0))).astype(np.float32)
    eigen = (single[:, None, None] + single[None, :, None] + single[None, None, :]).reshape(B, PLANE)
    return tiled, spread, rows_high, rows_low, eigen.astype(np.float32)


def split(values):
    high = values.astype(jnp.bfloat16)
    low = (values - high.astype(jnp.float32)).astype(jnp.bfloat16)
    return high, low


def split_outside(values):
    high = lax.reduce_precision(values, exponent_bits=8, mantissa_bits=7)
    return high.astype(jnp.bfloat16), (values - high).astype(jnp.bfloat16)


def dot3(left, right_high, right_low):
    high, low = split(left)
    out = jnp.dot(high, right_high, preferred_element_type=jnp.float32)
    out = out + jnp.dot(low, right_high, preferred_element_type=jnp.float32)
    return out + jnp.dot(high, right_low, preferred_element_type=jnp.float32)


def dot3_left(left_high, left_low, right):
    high, low = split(right)
    out = jnp.dot(left_high, high, preferred_element_type=jnp.float32)
    out = out + jnp.dot(left_low, high, preferred_element_type=jnp.float32)
    return out + jnp.dot(left_high, low, preferred_element_type=jnp.float32)


def exact_rows(matrix, values):
    first = values.astype(jnp.bfloat16)
    rest = values - first.astype(jnp.float32)
    second = rest.astype(jnp.bfloat16)
    third = (rest - second.astype(jnp.float32)).astype(jnp.bfloat16)
    out = jnp.dot(matrix, first, preferred_element_type=jnp.float32)
    out = out + jnp.dot(matrix, second, preferred_element_type=jnp.float32)
    return out + jnp.dot(matrix, third, preferred_element_type=jnp.float32)


def emit(payload_refs, stage_ref, row, values, tag, me):
    count = len(payload_refs)
    chunk = payload_refs[0].shape[1] - 128
    stage_ref[...] = values
    for step in range(count):
        index = lax.rem(me + step, count)
        out = payload_refs[step]
        if chunk >= PLANE:
            per = chunk // PLANE
            for part in range(per):
                out[pl.ds(row, 1), pl.ds(part * PLANE, PLANE)] = stage_ref[
                    pl.ds(index * per + part, 1), :
                ]
        else:
            per = PLANE // chunk
            full = stage_ref[pl.ds(index // per, 1), :]
            piece = index % per
            pick = full[:, 0:chunk]
            for other in range(1, per):
                pick = jnp.where(piece == other, full[:, other * chunk : (other + 1) * chunk], pick)
            out[pl.ds(row, 1), pl.ds(0, chunk)] = pick
        out[pl.ds(row, 1), pl.ds(chunk, 128)] = tag


def pair_kernel(
    count,
    boxes,
    meta_ref,
    home_ref,
    *rest,
):
    box_refs = rest[:boxes]
    pair_kernel_body(count, meta_ref, home_ref, box_refs, *rest[boxes:])


def pair_kernel_body(
    count,
    meta_ref,
    home_ref,
    box_refs,
    tiled_ref,
    spread_ref,
    rows_high_ref,
    rows_low_ref,
    eigen_ref,
    *rest,
):
    payload_ref = rest[:count]
    shifted_ref, work_ref, kron_high_ref, kron_low_ref, stage_ref = rest[count:]
    slots = home_ref.shape[0]
    me = meta_ref[6 * slots]
    tiled = tiled_ref[...]
    for block in range(B):
        values = tiled * spread_ref[block : block + 1, :]
        high = values.astype(jnp.bfloat16)
        kron_high_ref[block * B : (block + 1) * B, :] = high
        kron_low_ref[block * B : (block + 1) * B, :] = (
            values - high.astype(jnp.float32)
        ).astype(jnp.bfloat16)
    lane = lax.broadcasted_iota(jnp.int32, (B, PLANE), 1)
    lane_b = lane // B
    lane_c = lane % B
    row = lax.broadcasted_iota(jnp.int32, (B, B), 0)
    col = lax.broadcasted_iota(jnp.int32, (B, B), 1)
    for slot in range(slots):
        d_a = meta_ref[3 * slot]
        d_b = meta_ref[3 * slot + 1]
        d_c = meta_ref[3 * slot + 2]
        visit = meta_ref[6 * slots + 1 + slot]
        per_box = box_refs[0].shape[0]
        part = box_refs[0][0]
        for index in range(1, len(box_refs) * per_box):
            part = jnp.where(visit == index, box_refs[index // per_box][index % per_box], part)
        pick = (col == row + d_a).astype(jnp.bfloat16)
        moved = jnp.dot(pick, part, preferred_element_type=jnp.float32)
        step = d_b * B + d_c
        moved = pltpu.roll(moved, (PLANE - step) % PLANE, 1)
        inside = (
            (lane_b + d_b >= 0) & (lane_b + d_b < B) & (lane_c + d_c >= 0) & (lane_c + d_c < B)
        )
        moved = jnp.where(inside, moved, 0.0)
        shifted_ref[slot] = moved
        work_ref[slot * B : (slot + 1) * B, :] = home_ref[slot].astype(jnp.float32) * moved

    kron_high = kron_high_ref[...]
    kron_low = kron_low_ref[...]
    rows_high = rows_high_ref[...]
    rows_low = rows_low_ref[...]
    coef = dot3_left(rows_high, rows_low, dot3(work_ref[...], kron_high, kron_low))
    eigen = eigen_ref[...]
    for slot in range(slots):
        work_ref[slot * B : (slot + 1) * B, :] = coef[slot * B : (slot + 1) * B, :] / eigen
    potential = dot3_left(rows_high, rows_low, dot3(work_ref[...], kron_high, kron_low))

    for slot in range(slots):
        d_a = meta_ref[3 * slot]
        d_b = meta_ref[3 * slot + 1]
        d_c = meta_ref[3 * slot + 2]
        live = meta_ref[3 * slots + slot] > 0
        here = potential[slot * B : (slot + 1) * B, :]
        tag_home = jnp.full((1, 128), meta_ref[4 * slots + slot].astype(jnp.float32))
        tag_part = jnp.full((1, 128), meta_ref[5 * slots + slot].astype(jnp.float32))
        emit(payload_ref, stage_ref, slot, jnp.where(live, here * shifted_ref[slot], 0.0), tag_home, me)
        product = here * home_ref[slot].astype(jnp.float32)
        pick = (col == row - d_a).astype(jnp.bfloat16)
        moved = exact_rows(pick, product)
        step = d_b * B + d_c
        moved = pltpu.roll(moved, (PLANE + step) % PLANE, 1)
        inside = (
            (lane_b - d_b >= 0) & (lane_b - d_b < B) & (lane_c - d_c >= 0) & (lane_c - d_c < B)
        )
        emit(
            payload_ref, stage_ref, slots + slot, jnp.where(live & inside, moved, 0.0), tag_part, me
        )


def pair_fields(meta, home, boxes, count, chunk):
    slots = home.shape[0]
    tiled, spread, rows_high, rows_low, eigen = host_tables(slots)
    smem = pl.BlockSpec(memory_space=pltpu.SMEM)
    vmem = pl.BlockSpec(memory_space=pltpu.VMEM)
    box = jax.ShapeDtypeStruct((2 * slots, chunk + 128), jnp.float32)
    return pl.pallas_call(
        functools.partial(pair_kernel, count, len(boxes)),
        out_shape=tuple([box] * count),
        in_specs=[smem] + [vmem] * (6 + len(boxes)),
        out_specs=tuple([vmem] * count),
        scratch_shapes=[
            pltpu.VMEM((slots, B, PLANE), jnp.float32),
            pltpu.VMEM((slots * B, PLANE), jnp.float32),
            pltpu.VMEM((PLANE, PLANE), jnp.bfloat16),
            pltpu.VMEM((PLANE, PLANE), jnp.bfloat16),
            pltpu.VMEM((B, PLANE), jnp.float32),
        ],
    )(meta, home, *boxes, tiled, spread, rows_high, rows_low, eigen)


def exchange(blocks, axis):
    count = len(blocks)
    received = [blocks[0]]
    for step in range(1, count):
        pairs = [(source, (source + step) % count) for source in range(count)]
        received.append(lax.ppermute(blocks[step], axis, pairs))
    return received


def pick_rows(indices, table):
    chooser = (indices[:, None] == jnp.arange(table.shape[0], dtype=jnp.int32)[None, :])
    return jnp.dot(chooser.astype(jnp.float32), table.astype(jnp.float32), precision=PRECISE)


def per_device(orbitals, offsets, sends, pair_home, pair_visit, pair_count):
    home_count = orbitals.shape[0]
    cell_count = orbitals.shape[1]
    section_total = sends.shape[1]
    per_target = sends.shape[2]
    slot_total = section_total * per_target
    slots = pair_home.shape[2]
    extra = 128
    me = lax.axis_index("home")
    chosen = lax.dynamic_slice_in_dim(jnp.concatenate([sends[0], sends[0]]), me, section_total)
    flat_chosen = chosen.reshape(-1)
    outgoing = jnp.concatenate(
        [
            orbitals[flat_chosen],
            jnp.pad(pick_rows(flat_chosen, offsets).astype(jnp.bfloat16), ((0, 0), (0, extra - 3))),
        ],
        axis=1,
    ).reshape(section_total, per_target, cell_count + extra)
    arrived = exchange(outgoing, "home")
    visitors = [block[:, :cell_count].reshape(per_target, B, PLANE) for block in arrived]
    visit_offsets = jnp.stack(
        [block[:, cell_count : cell_count + 3] for block in arrived]
    ).reshape(slot_total, 3).astype(jnp.int32)

    home_slot = pair_home[0, 0]
    visit_code = pair_visit[0, 0]
    source = visit_code // per_target
    visit_slot = ((me - source) % section_total) * per_target + visit_code % per_target
    return_slot = ((source - me) % section_total) * per_target + visit_code % per_target
    live = (jnp.arange(slots, dtype=jnp.int32) < pair_count[0, 0]).astype(jnp.int32)
    home_orb = orbitals[home_slot].reshape(slots, B, PLANE)
    delta = pick_rows(home_slot, offsets).astype(jnp.int32) - visit_offsets[visit_slot]
    pair_total = lax.psum(1, "pair")
    chunk = cell_count // pair_total
    pair_me = lax.axis_index("pair")
    meta = jnp.concatenate(
        [
            delta.reshape(-1),
            live,
            home_slot,
            home_count + return_slot,
            jnp.reshape(pair_me, (1,)).astype(jnp.int32),
            visit_slot,
        ]
    )
    payload = pair_fields(meta, home_orb, visitors, pair_total, chunk)
    got = jnp.stack(exchange(payload, "pair"))
    got_ids = got[:, :, chunk].astype(jnp.int32)
    all_rows = jnp.arange(home_count + slot_total, dtype=jnp.int32)
    picker = (got_ids[:, :, None] == all_rows[None, None, :]).astype(jnp.float32)
    totals = jnp.einsum("srk,srl->kl", picker, got[:, :, :chunk], precision=lax.Precision.HIGH)
    home_totals = totals[:home_count]
    back = (-jnp.arange(section_total, dtype=jnp.int32)) % section_total
    visit_totals = totals[home_count:].reshape(section_total, per_target, chunk)
    returned = jnp.stack(exchange(visit_totals, "home")).reshape(slot_total, chunk)
    owners = chosen[back].reshape(-1)
    chooser = (owners[:, None] == jnp.arange(home_count, dtype=jnp.int32)[None, :]).astype(
        jnp.float32
    )
    return home_totals + jnp.sum(
        jnp.where(chooser.T[:, :, None] > 0, returned[None, :, :], 0.0), axis=1
    )


def solution(mesh):
    in_specs = (
        P("home", None),
        P("home", None),
        P("home", None, None),
        P("home", "pair", None),
        P("home", "pair", None),
        P("home", "pair"),
    )
    out_specs = P("home", "pair")
    return jax.shard_map(
        per_device, mesh=mesh, in_specs=in_specs, out_specs=out_specs, check_vma=False
    )
```

```python
import functools

import jax
import jax.numpy as jnp
import ml_dtypes
import numpy as np
from jax import lax
from jax.experimental import pallas as pl
from jax.experimental.pallas import tpu as pltpu
from jax.sharding import PartitionSpec as P

B = 32
PLANE = B * B


PRECISE = lax.Precision.HIGHEST


def sine_table():
    grid = jnp.arange(B, dtype=jnp.float32) + 1.0
    return jnp.sqrt(2.0 / (B + 1.0)) * jnp.sin(jnp.pi * grid[:, None] * grid[None, :] / (B + 1.0))


def eigen_sum():
    grid = jnp.arange(B, dtype=jnp.float32) + 1.0
    single = 2.0 - 2.0 * jnp.cos(jnp.pi * grid / (B + 1.0))
    return single[:, None, None] + single[None, :, None] + single[None, None, :]


def host_tables(slots):
    grid = np.arange(B, dtype=np.float32) + np.float32(1.0)
    angle = np.float32(np.pi) * grid[:, None] * grid[None, :] / np.float32(B + 1.0)
    table = (np.sqrt(np.float32(2.0 / (B + 1.0))) * np.sin(angle)).astype(np.float32)
    tiled = np.tile(table, (1, B))
    spread = np.repeat(table, B, axis=1)
    rows = np.kron(np.eye(slots, dtype=np.float32), table).astype(np.float32)
    rows_high = rows.astype(ml_dtypes.bfloat16)
    rows_low = (rows - rows_high.astype(np.float32)).astype(ml_dtypes.bfloat16)
    single = (np.float32(2.0) - np.float32(2.0) * np.cos(np.float32(np.pi) * grid / np.float32(B + 1.0))).astype(np.float32)
    eigen = (single[:, None, None] + single[None, :, None] + single[None, None, :]).reshape(B, PLANE)
    return tiled, spread, rows_high, rows_low, (np.float32(1.0) / eigen).astype(np.float32)


def split(values):
    high = values.astype(jnp.bfloat16)
    low = (values - high.astype(jnp.float32)).astype(jnp.bfloat16)
    return high, low


def split_outside(values):
    high = lax.reduce_precision(values, exponent_bits=8, mantissa_bits=7)
    return high.astype(jnp.bfloat16), (values - high).astype(jnp.bfloat16)


def dot3(left, right_high, right_low):
    high, low = split(left)
    out = jnp.dot(high, right_high, preferred_element_type=jnp.float32)
    out = out + jnp.dot(low, right_high, preferred_element_type=jnp.float32)
    return out + jnp.dot(high, right_low, preferred_element_type=jnp.float32)


def dot3_left(left_high, left_low, right):
    high, low = split(right)
    out = jnp.dot(left_high, high, preferred_element_type=jnp.float32)
    out = out + jnp.dot(left_low, high, preferred_element_type=jnp.float32)
    return out + jnp.dot(left_high, low, preferred_element_type=jnp.float32)


def exact_rows(matrix, values):
    first = values.astype(jnp.bfloat16)
    rest = values - first.astype(jnp.float32)
    second = rest.astype(jnp.bfloat16)
    third = (rest - second.astype(jnp.float32)).astype(jnp.bfloat16)
    out = jnp.dot(matrix, first, preferred_element_type=jnp.float32)
    out = out + jnp.dot(matrix, second, preferred_element_type=jnp.float32)
    return out + jnp.dot(matrix, third, preferred_element_type=jnp.float32)


def emit(payload_refs, stage_ref, row, values, tag, me):
    count = len(payload_refs)
    chunk = payload_refs[0].shape[1] - 128
    stage_ref[...] = values
    for step in range(count):
        index = lax.rem(me + step, count)
        out = payload_refs[step]
        if chunk >= PLANE:
            per = chunk // PLANE
            for part in range(per):
                out[pl.ds(row, 1), pl.ds(part * PLANE, PLANE)] = stage_ref[
                    pl.ds(index * per + part, 1), :
                ]
        else:
            per = PLANE // chunk
            full = stage_ref[pl.ds(index // per, 1), :]
            piece = index % per
            pick = full[:, 0:chunk]
            for other in range(1, per):
                pick = jnp.where(piece == other, full[:, other * chunk : (other + 1) * chunk], pick)
            out[pl.ds(row, 1), pl.ds(0, chunk)] = pick
        out[pl.ds(row, 1), pl.ds(chunk, 128)] = tag


def pair_kernel(
    count,
    boxes,
    meta_ref,
    home_ref,
    *rest,
):
    box_refs = rest[:boxes]
    pair_kernel_body(count, meta_ref, home_ref, box_refs, *rest[boxes:])


def pair_kernel_body(
    count,
    meta_ref,
    home_ref,
    box_refs,
    tiled_ref,
    spread_ref,
    rows_high_ref,
    rows_low_ref,
    eigen_ref,
    *rest,
):
    payload_ref = rest[:count]
    shifted_ref, work_ref, kron_high_ref, kron_low_ref, stage_ref = rest[count:]
    slots = home_ref.shape[0]
    me = meta_ref[6 * slots]
    tiled = tiled_ref[...]
    for block in range(B):
        values = tiled * spread_ref[block : block + 1, :]
        high = values.astype(jnp.bfloat16)
        kron_high_ref[block * B : (block + 1) * B, :] = high
        kron_low_ref[block * B : (block + 1) * B, :] = (
            values - high.astype(jnp.float32)
        ).astype(jnp.bfloat16)
    lane = lax.broadcasted_iota(jnp.int32, (B, PLANE), 1)
    lane_b = lane // B
    lane_c = lane % B
    row = lax.broadcasted_iota(jnp.int32, (B, B), 0)
    col = lax.broadcasted_iota(jnp.int32, (B, B), 1)
    for slot in range(slots):
        d_a = meta_ref[3 * slot]
        d_b = meta_ref[3 * slot + 1]
        d_c = meta_ref[3 * slot + 2]
        visit = meta_ref[6 * slots + 1 + slot]
        per_box = box_refs[0].shape[0]
        part = box_refs[0][0]
        for index in range(1, len(box_refs) * per_box):
            part = jnp.where(visit == index, box_refs[index // per_box][index % per_box], part)
        pick = (col == row + d_a).astype(jnp.bfloat16)
        moved = jnp.dot(pick, part, preferred_element_type=jnp.float32)
        step = d_b * B + d_c
        moved = pltpu.roll(moved, (PLANE - step) % PLANE, 1)
        inside = (
            (lane_b + d_b >= 0) & (lane_b + d_b < B) & (lane_c + d_c >= 0) & (lane_c + d_c < B)
        )
        moved = jnp.where(inside, moved, 0.0)
        shifted_ref[slot] = moved
        work_ref[slot * B : (slot + 1) * B, :] = home_ref[slot].astype(jnp.float32) * moved

    kron_high = kron_high_ref[...]
    kron_low = kron_low_ref[...]
    rows_high = rows_high_ref[...]
    rows_low = rows_low_ref[...]
    coef = dot3_left(rows_high, rows_low, dot3(work_ref[...], kron_high, kron_low))
    eigen = eigen_ref[...]
    for slot in range(slots):
        work_ref[slot * B : (slot + 1) * B, :] = coef[slot * B : (slot + 1) * B, :] * eigen
    potential = dot3_left(rows_high, rows_low, dot3(work_ref[...], kron_high, kron_low))

    for slot in range(slots):
        d_a = meta_ref[3 * slot]
        d_b = meta_ref[3 * slot + 1]
        d_c = meta_ref[3 * slot + 2]
        live = meta_ref[3 * slots + slot] > 0
        here = potential[slot * B : (slot + 1) * B, :]
        tag_home = jnp.full((1, 128), meta_ref[4 * slots + slot].astype(jnp.float32))
        tag_part = jnp.full((1, 128), meta_ref[5 * slots + slot].astype(jnp.float32))
        emit(payload_ref, stage_ref, slot, jnp.where(live, here * shifted_ref[slot], 0.0), tag_home, me)
        product = here * home_ref[slot].astype(jnp.float32)
        pick = (col == row - d_a).astype(jnp.bfloat16)
        moved = exact_rows(pick, product)
        step = d_b * B + d_c
        moved = pltpu.roll(moved, (PLANE + step) % PLANE, 1)
        inside = (
            (lane_b - d_b >= 0) & (lane_b - d_b < B) & (lane_c - d_c >= 0) & (lane_c - d_c < B)
        )
        emit(
            payload_ref, stage_ref, slots + slot, jnp.where(live & inside, moved, 0.0), tag_part, me
        )


def pair_fields(meta, home, boxes, count, chunk):
    slots = home.shape[0]
    tiled, spread, rows_high, rows_low, eigen = host_tables(slots)
    smem = pl.BlockSpec(memory_space=pltpu.SMEM)
    vmem = pl.BlockSpec(memory_space=pltpu.VMEM)
    box = jax.ShapeDtypeStruct((2 * slots, chunk + 128), jnp.float32)
    return pl.pallas_call(
        functools.partial(pair_kernel, count, len(boxes)),
        out_shape=tuple([box] * count),
        in_specs=[smem] + [vmem] * (6 + len(boxes)),
        out_specs=tuple([vmem] * count),
        scratch_shapes=[
            pltpu.VMEM((slots, B, PLANE), jnp.float32),
            pltpu.VMEM((slots * B, PLANE), jnp.float32),
            pltpu.VMEM((PLANE, PLANE), jnp.bfloat16),
            pltpu.VMEM((PLANE, PLANE), jnp.bfloat16),
            pltpu.VMEM((B, PLANE), jnp.float32),
        ],
    )(meta, home, *boxes, tiled, spread, rows_high, rows_low, eigen)


def exchange(blocks, axis):
    count = len(blocks)
    received = [blocks[0]]
    for step in range(1, count):
        pairs = [(source, (source + step) % count) for source in range(count)]
        received.append(lax.ppermute(blocks[step], axis, pairs))
    return received


def pick_rows(indices, table):
    chooser = (indices[:, None] == jnp.arange(table.shape[0], dtype=jnp.int32)[None, :])
    return jnp.dot(chooser.astype(jnp.float32), table.astype(jnp.float32), precision=PRECISE)


def per_device(orbitals, offsets, sends, pair_home, pair_visit, pair_count):
    home_count = orbitals.shape[0]
    cell_count = orbitals.shape[1]
    section_total = sends.shape[1]
    per_target = sends.shape[2]
    slot_total = section_total * per_target
    slots = pair_home.shape[2]
    extra = 128
    me = lax.axis_index("home")
    chosen = lax.dynamic_slice_in_dim(jnp.concatenate([sends[0], sends[0]]), me, section_total)
    flat_chosen = chosen.reshape(-1)
    outgoing = jnp.concatenate(
        [
            orbitals[flat_chosen],
            jnp.pad(pick_rows(flat_chosen, offsets).astype(jnp.bfloat16), ((0, 0), (0, extra - 3))),
        ],
        axis=1,
    ).reshape(section_total, per_target, cell_count + extra)
    arrived = exchange(outgoing, "home")
    visitors = [block[:, :cell_count].reshape(per_target, B, PLANE) for block in arrived]
    visit_offsets = jnp.stack(
        [block[:, cell_count : cell_count + 3] for block in arrived]
    ).reshape(slot_total, 3).astype(jnp.int32)

    home_slot = pair_home[0, 0]
    visit_code = pair_visit[0, 0]
    source = visit_code // per_target
    visit_slot = ((me - source) % section_total) * per_target + visit_code % per_target
    return_slot = ((source - me) % section_total) * per_target + visit_code % per_target
    live = (jnp.arange(slots, dtype=jnp.int32) < pair_count[0, 0]).astype(jnp.int32)
    home_orb = orbitals[home_slot].reshape(slots, B, PLANE)
    delta = pick_rows(home_slot, offsets).astype(jnp.int32) - visit_offsets[visit_slot]
    pair_total = lax.psum(1, "pair")
    chunk = cell_count // pair_total
    pair_me = lax.axis_index("pair")
    meta = jnp.concatenate(
        [
            delta.reshape(-1),
            live,
            home_slot,
            home_count + return_slot,
            jnp.reshape(pair_me, (1,)).astype(jnp.int32),
            visit_slot,
        ]
    )
    payload = pair_fields(meta, home_orb, visitors, pair_total, chunk)
    got = jnp.stack(exchange(payload, "pair"))
    got_ids = got[:, :, chunk].astype(jnp.int32)
    all_rows = jnp.arange(home_count + slot_total, dtype=jnp.int32)
    picker = (got_ids[:, :, None] == all_rows[None, None, :]).astype(jnp.float32)
    totals = jnp.einsum("srk,srl->kl", picker, got[:, :, :chunk], precision=lax.Precision.HIGH)
    home_totals = totals[:home_count]
    back = (-jnp.arange(section_total, dtype=jnp.int32)) % section_total
    visit_totals = totals[home_count:].reshape(section_total, per_target, chunk)
    returned = jnp.stack(exchange(visit_totals, "home")).reshape(slot_total, chunk)
    owners = chosen[back].reshape(-1)
    chooser = (owners[:, None] == jnp.arange(home_count, dtype=jnp.int32)[None, :]).astype(
        jnp.float32
    )
    return home_totals + jnp.dot(chooser.T, returned, precision=lax.Precision.HIGH)


def solution(mesh):
    in_specs = (
        P("home", None),
        P("home", None),
        P("home", None, None),
        P("home", "pair", None),
        P("home", "pair", None),
        P("home", "pair"),
    )
    out_specs = P("home", "pair")
    return jax.shard_map(
        per_device, mesh=mesh, in_specs=in_specs, out_specs=out_specs, check_vma=False
    )
```

```python
import functools

import jax
import jax.numpy as jnp
import ml_dtypes
import numpy as np
from jax import lax
from jax.experimental import pallas as pl
from jax.experimental.pallas import tpu as pltpu
from jax.sharding import PartitionSpec as P

B = 32
PLANE = B * B


PRECISE = lax.Precision.HIGHEST


def sine_table():
    grid = jnp.arange(B, dtype=jnp.float32) + 1.0
    return jnp.sqrt(2.0 / (B + 1.0)) * jnp.sin(jnp.pi * grid[:, None] * grid[None, :] / (B + 1.0))


def eigen_sum():
    grid = jnp.arange(B, dtype=jnp.float32) + 1.0
    single = 2.0 - 2.0 * jnp.cos(jnp.pi * grid / (B + 1.0))
    return single[:, None, None] + single[None, :, None] + single[None, None, :]


def host_tables(slots):
    grid = np.arange(B, dtype=np.float32) + np.float32(1.0)
    angle = np.float32(np.pi) * grid[:, None] * grid[None, :] / np.float32(B + 1.0)
    table = (np.sqrt(np.float32(2.0 / (B + 1.0))) * np.sin(angle)).astype(np.float32)
    tiled = np.tile(table, (1, B))
    spread = np.repeat(table, B, axis=1)
    rows = np.kron(np.eye(slots, dtype=np.float32), table).astype(np.float32)
    rows_high = rows.astype(ml_dtypes.bfloat16)
    rows_low = (rows - rows_high.astype(np.float32)).astype(ml_dtypes.bfloat16)
    single = (np.float32(2.0) - np.float32(2.0) * np.cos(np.float32(np.pi) * grid / np.float32(B + 1.0))).astype(np.float32)
    eigen = (single[:, None, None] + single[None, :, None] + single[None, None, :]).reshape(B, PLANE)
    return tiled, spread, rows_high, rows_low, eigen.astype(np.float32)


def split(values):
    high = values.astype(jnp.bfloat16)
    low = (values - high.astype(jnp.float32)).astype(jnp.bfloat16)
    return high, low


def split_outside(values):
    high = lax.reduce_precision(values, exponent_bits=8, mantissa_bits=7)
    return high.astype(jnp.bfloat16), (values - high).astype(jnp.bfloat16)


def dot3(left, right_high, right_low):
    high, low = split(left)
    out = jnp.dot(high, right_high, preferred_element_type=jnp.float32)
    out = out + jnp.dot(low, right_high, preferred_element_type=jnp.float32)
    return out + jnp.dot(high, right_low, preferred_element_type=jnp.float32)


def dot3_left(left_high, left_low, right):
    high, low = split(right)
    out = jnp.dot(left_high, high, preferred_element_type=jnp.float32)
    out = out + jnp.dot(left_low, high, preferred_element_type=jnp.float32)
    return out + jnp.dot(left_high, low, preferred_element_type=jnp.float32)


def exact_rows(matrix, values):
    first = values.astype(jnp.bfloat16)
    rest = values - first.astype(jnp.float32)
    second = rest.astype(jnp.bfloat16)
    third = (rest - second.astype(jnp.float32)).astype(jnp.bfloat16)
    out = jnp.dot(matrix, first, preferred_element_type=jnp.float32)
    out = out + jnp.dot(matrix, second, preferred_element_type=jnp.float32)
    return out + jnp.dot(matrix, third, preferred_element_type=jnp.float32)


def emit(payload_refs, stage_ref, row, values, tag, me):
    count = len(payload_refs)
    chunk = payload_refs[0].shape[1] - 128
    stage_ref[...] = values
    for step in range(count):
        index = lax.rem(me + step, count)
        out = payload_refs[step]
        if chunk >= PLANE:
            per = chunk // PLANE
            for part in range(per):
                out[pl.ds(row, 1), pl.ds(part * PLANE, PLANE)] = stage_ref[
                    pl.ds(index * per + part, 1), :
                ]
        else:
            per = PLANE // chunk
            full = stage_ref[pl.ds(index // per, 1), :]
            piece = index % per
            pick = full[:, 0:chunk]
            for other in range(1, per):
                pick = jnp.where(piece == other, full[:, other * chunk : (other + 1) * chunk], pick)
            out[pl.ds(row, 1), pl.ds(0, chunk)] = pick
        out[pl.ds(row, 1), pl.ds(chunk, 128)] = tag


def pair_kernel(
    count,
    boxes,
    meta_ref,
    home_ref,
    *rest,
):
    box_refs = rest[:boxes]
    pair_kernel_body(count, meta_ref, home_ref, box_refs, *rest[boxes:])


def pair_kernel_body(
    count,
    meta_ref,
    home_ref,
    box_refs,
    tiled_ref,
    spread_ref,
    rows_high_ref,
    rows_low_ref,
    eigen_ref,
    *rest,
):
    payload_ref = rest[:count]
    shifted_ref, work_ref, kron_high_ref, kron_low_ref, stage_ref = rest[count:]
    slots = home_ref.shape[0]
    me = meta_ref[6 * slots]
    tiled = tiled_ref[...]
    for block in range(B):
        values = tiled * spread_ref[block : block + 1, :]
        high = values.astype(jnp.bfloat16)
        kron_high_ref[block * B : (block + 1) * B, :] = high
        kron_low_ref[block * B : (block + 1) * B, :] = (
            values - high.astype(jnp.float32)
        ).astype(jnp.bfloat16)
    lane = lax.broadcasted_iota(jnp.int32, (B, PLANE), 1)
    lane_b = lane // B
    lane_c = lane % B
    row = lax.broadcasted_iota(jnp.int32, (B, B), 0)
    col = lax.broadcasted_iota(jnp.int32, (B, B), 1)
    for slot in range(slots):
        d_a = meta_ref[3 * slot]
        d_b = meta_ref[3 * slot + 1]
        d_c = meta_ref[3 * slot + 2]
        visit = meta_ref[6 * slots + 1 + slot]
        per_box = box_refs[0].shape[0]
        part = box_refs[0][0, 0:B, :]
        for index in range(1, len(box_refs) * per_box):
            part = jnp.where(
                visit == index, box_refs[index // per_box][index % per_box, 0:B, :], part
            )
        pick = (col == row + d_a).astype(jnp.bfloat16)
        moved = jnp.dot(pick, part, preferred_element_type=jnp.float32)
        step = d_b * B + d_c
        moved = pltpu.roll(moved, (PLANE - step) % PLANE, 1)
        inside = (
            (lane_b + d_b >= 0) & (lane_b + d_b < B) & (lane_c + d_c >= 0) & (lane_c + d_c < B)
        )
        moved = jnp.where(inside, moved, 0.0)
        shifted_ref[slot] = moved
        work_ref[slot * B : (slot + 1) * B, :] = home_ref[slot].astype(jnp.float32) * moved

    kron_high = kron_high_ref[...]
    kron_low = kron_low_ref[...]
    rows_high = rows_high_ref[...]
    rows_low = rows_low_ref[...]
    coef = dot3_left(rows_high, rows_low, dot3(work_ref[...], kron_high, kron_low))
    eigen = eigen_ref[...]
    for slot in range(slots):
        work_ref[slot * B : (slot + 1) * B, :] = coef[slot * B : (slot + 1) * B, :] / eigen
    potential = dot3_left(rows_high, rows_low, dot3(work_ref[...], kron_high, kron_low))

    for slot in range(slots):
        d_a = meta_ref[3 * slot]
        d_b = meta_ref[3 * slot + 1]
        d_c = meta_ref[3 * slot + 2]
        live = meta_ref[3 * slots + slot] > 0
        here = potential[slot * B : (slot + 1) * B, :]
        tag_home = jnp.full((1, 128), meta_ref[4 * slots + slot].astype(jnp.float32))
        tag_part = jnp.full((1, 128), meta_ref[5 * slots + slot].astype(jnp.float32))
        emit(payload_ref, stage_ref, slot, jnp.where(live, here * shifted_ref[slot], 0.0), tag_home, me)
        product = here * home_ref[slot].astype(jnp.float32)
        pick = (col == row - d_a).astype(jnp.bfloat16)
        moved = exact_rows(pick, product)
        step = d_b * B + d_c
        moved = pltpu.roll(moved, (PLANE + step) % PLANE, 1)
        inside = (
            (lane_b - d_b >= 0) & (lane_b - d_b < B) & (lane_c - d_c >= 0) & (lane_c - d_c < B)
        )
        emit(
            payload_ref, stage_ref, slots + slot, jnp.where(live & inside, moved, 0.0), tag_part, me
        )


def pair_fields(meta, home, boxes, count, chunk):
    slots = home.shape[0]
    tiled, spread, rows_high, rows_low, eigen = host_tables(slots)
    smem = pl.BlockSpec(memory_space=pltpu.SMEM)
    vmem = pl.BlockSpec(memory_space=pltpu.VMEM)
    box = jax.ShapeDtypeStruct((2 * slots, chunk + 128), jnp.float32)
    return pl.pallas_call(
        functools.partial(pair_kernel, count, len(boxes)),
        out_shape=tuple([box] * count),
        in_specs=[smem] + [vmem] * (6 + len(boxes)),
        out_specs=tuple([vmem] * count),
        scratch_shapes=[
            pltpu.VMEM((slots, B, PLANE), jnp.float32),
            pltpu.VMEM((slots * B, PLANE), jnp.float32),
            pltpu.VMEM((PLANE, PLANE), jnp.bfloat16),
            pltpu.VMEM((PLANE, PLANE), jnp.bfloat16),
            pltpu.VMEM((B, PLANE), jnp.float32),
        ],
    )(meta, home, *boxes, tiled, spread, rows_high, rows_low, eigen)


def exchange(blocks, axis):
    count = len(blocks)
    received = [blocks[0]]
    for step in range(1, count):
        pairs = [(source, (source + step) % count) for source in range(count)]
        received.append(lax.ppermute(blocks[step], axis, pairs))
    return received


def pick_rows(indices, table):
    chooser = (indices[:, None] == jnp.arange(table.shape[0], dtype=jnp.int32)[None, :])
    return jnp.dot(chooser.astype(jnp.float32), table.astype(jnp.float32), precision=PRECISE)


def per_device(orbitals, offsets, sends, pair_home, pair_visit, pair_count):
    home_count = orbitals.shape[0]
    cell_count = orbitals.shape[1]
    section_total = sends.shape[1]
    per_target = sends.shape[2]
    slot_total = section_total * per_target
    slots = pair_home.shape[2]
    extra = 128
    me = lax.axis_index("home")
    chosen = lax.dynamic_slice_in_dim(jnp.concatenate([sends[0], sends[0]]), me, section_total)
    flat_chosen = chosen.reshape(-1)
    outgoing = jnp.concatenate(
        [
            orbitals[flat_chosen].reshape(slot_total, B, PLANE),
            jnp.pad(
                pick_rows(flat_chosen, offsets).astype(jnp.bfloat16), ((0, 0), (0, PLANE - 3))
            )[:, None, :],
        ],
        axis=1,
    ).reshape(section_total, per_target, B + 1, PLANE)
    visitors = exchange(outgoing, "home")
    visit_offsets = jnp.stack([block[:, B, 0:3] for block in visitors]).reshape(
        slot_total, 3
    ).astype(jnp.int32)

    home_slot = pair_home[0, 0]
    visit_code = pair_visit[0, 0]
    source = visit_code // per_target
    visit_slot = ((me - source) % section_total) * per_target + visit_code % per_target
    return_slot = ((source - me) % section_total) * per_target + visit_code % per_target
    live = (jnp.arange(slots, dtype=jnp.int32) < pair_count[0, 0]).astype(jnp.int32)
    home_orb = orbitals[home_slot].reshape(slots, B, PLANE)
    delta = pick_rows(home_slot, offsets).astype(jnp.int32) - visit_offsets[visit_slot]
    pair_total = lax.psum(1, "pair")
    chunk = cell_count // pair_total
    pair_me = lax.axis_index("pair")
    meta = jnp.concatenate(
        [
            delta.reshape(-1),
            live,
            home_slot,
            home_count + return_slot,
            jnp.reshape(pair_me, (1,)).astype(jnp.int32),
            visit_slot,
        ]
    )
    payload = pair_fields(meta, home_orb, visitors, pair_total, chunk)
    got = jnp.stack(exchange(payload, "pair"))
    got_ids = got[:, :, chunk].astype(jnp.int32)
    all_rows = jnp.arange(home_count + slot_total, dtype=jnp.int32)
    picker = (got_ids[:, :, None] == all_rows[None, None, :]).astype(jnp.float32)
    totals = jnp.einsum("srk,srl->kl", picker, got[:, :, :chunk], precision=lax.Precision.HIGH)
    home_totals = totals[:home_count]
    back = (-jnp.arange(section_total, dtype=jnp.int32)) % section_total
    visit_totals = totals[home_count:].reshape(section_total, per_target, chunk)
    returned = jnp.stack(exchange(visit_totals, "home")).reshape(slot_total, chunk)
    owners = chosen[back].reshape(-1)
    chooser = (owners[:, None] == jnp.arange(home_count, dtype=jnp.int32)[None, :]).astype(
        jnp.float32
    )
    return home_totals + jnp.dot(chooser.T, returned, precision=lax.Precision.HIGH)


def solution(mesh):
    in_specs = (
        P("home", None),
        P("home", None),
        P("home", None, None),
        P("home", "pair", None),
        P("home", "pair", None),
        P("home", "pair"),
    )
    out_specs = P("home", "pair")
    return jax.shard_map(
        per_device, mesh=mesh, in_specs=in_specs, out_specs=out_specs, check_vma=False
    )
```

```python
import functools

import jax
import jax.numpy as jnp
import ml_dtypes
import numpy as np
from jax import lax
from jax.experimental import pallas as pl
from jax.experimental.pallas import tpu as pltpu
from jax.sharding import PartitionSpec as P

B = 32
PLANE = B * B


PRECISE = lax.Precision.HIGHEST


def sine_table():
    grid = jnp.arange(B, dtype=jnp.float32) + 1.0
    return jnp.sqrt(2.0 / (B + 1.0)) * jnp.sin(jnp.pi * grid[:, None] * grid[None, :] / (B + 1.0))


def eigen_sum():
    grid = jnp.arange(B, dtype=jnp.float32) + 1.0
    single = 2.0 - 2.0 * jnp.cos(jnp.pi * grid / (B + 1.0))
    return single[:, None, None] + single[None, :, None] + single[None, None, :]


def host_tables(slots):
    grid = np.arange(B, dtype=np.float32) + np.float32(1.0)
    angle = np.float32(np.pi) * grid[:, None] * grid[None, :] / np.float32(B + 1.0)
    table = (np.sqrt(np.float32(2.0 / (B + 1.0))) * np.sin(angle)).astype(np.float32)
    tiled = np.tile(table, (1, B))
    spread = np.repeat(table, B, axis=1)
    rows = np.kron(np.eye(slots, dtype=np.float32), table).astype(np.float32)
    rows_high = rows.astype(ml_dtypes.bfloat16)
    rows_low = (rows - rows_high.astype(np.float32)).astype(ml_dtypes.bfloat16)
    single = (np.float32(2.0) - np.float32(2.0) * np.cos(np.float32(np.pi) * grid / np.float32(B + 1.0))).astype(np.float32)
    eigen = (single[:, None, None] + single[None, :, None] + single[None, None, :]).reshape(B, PLANE)
    return tiled, spread, rows_high, rows_low, eigen.astype(np.float32)


def split(values):
    high = values.astype(jnp.bfloat16)
    low = (values - high.astype(jnp.float32)).astype(jnp.bfloat16)
    return high, low


def split_outside(values):
    high = lax.reduce_precision(values, exponent_bits=8, mantissa_bits=7)
    return high.astype(jnp.bfloat16), (values - high).astype(jnp.bfloat16)


def dot3(left, right_high, right_low):
    high, low = split(left)
    out = jnp.dot(high, right_high, preferred_element_type=jnp.float32)
    out = out + jnp.dot(low, right_high, preferred_element_type=jnp.float32)
    return out + jnp.dot(high, right_low, preferred_element_type=jnp.float32)


def dot3_left(left_high, left_low, right):
    high, low = split(right)
    out = jnp.dot(left_high, high, preferred_element_type=jnp.float32)
    out = out + jnp.dot(left_low, high, preferred_element_type=jnp.float32)
    return out + jnp.dot(left_high, low, preferred_element_type=jnp.float32)


def exact_rows(matrix, values):
    first = values.astype(jnp.bfloat16)
    rest = values - first.astype(jnp.float32)
    second = rest.astype(jnp.bfloat16)
    third = (rest - second.astype(jnp.float32)).astype(jnp.bfloat16)
    out = jnp.dot(matrix, first, preferred_element_type=jnp.float32)
    out = out + jnp.dot(matrix, second, preferred_element_type=jnp.float32)
    return out + jnp.dot(matrix, third, preferred_element_type=jnp.float32)


def emit(payload_refs, stage_ref, row, values, tag, me):
    count = len(payload_refs)
    chunk = payload_refs[0].shape[1] - 128
    stage_ref[...] = values
    for step in range(count):
        index = lax.rem(me + step, count)
        out = payload_refs[step]
        if chunk >= PLANE:
            per = chunk // PLANE
            for part in range(per):
                out[pl.ds(row, 1), pl.ds(part * PLANE, PLANE)] = stage_ref[
                    pl.ds(index * per + part, 1), :
                ]
        else:
            per = PLANE // chunk
            full = stage_ref[pl.ds(index // per, 1), :]
            piece = index % per
            pick = full[:, 0:chunk]
            for other in range(1, per):
                pick = jnp.where(piece == other, full[:, other * chunk : (other + 1) * chunk], pick)
            out[pl.ds(row, 1), pl.ds(0, chunk)] = pick
        out[pl.ds(row, 1), pl.ds(chunk, 128)] = tag


def pair_kernel(
    count,
    boxes,
    meta_ref,
    home_ref,
    *rest,
):
    box_refs = rest[:boxes]
    pair_kernel_body(count, meta_ref, home_ref, box_refs, *rest[boxes:])


def pair_kernel_body(
    count,
    meta_ref,
    home_ref,
    box_refs,
    tiled_ref,
    spread_ref,
    rows_high_ref,
    rows_low_ref,
    eigen_ref,
    *rest,
):
    payload_ref = rest[:count]
    shifted_ref, work_ref, kron_high_ref, kron_low_ref, stage_ref = rest[count:]
    slots = home_ref.shape[0]
    me = meta_ref[6 * slots]
    tiled = tiled_ref[...]
    for block in range(B):
        values = tiled * spread_ref[block : block + 1, :]
        high = values.astype(jnp.bfloat16)
        kron_high_ref[block * B : (block + 1) * B, :] = high
        kron_low_ref[block * B : (block + 1) * B, :] = (
            values - high.astype(jnp.float32)
        ).astype(jnp.bfloat16)
    lane = lax.broadcasted_iota(jnp.int32, (B, PLANE), 1)
    lane_b = lane // B
    lane_c = lane % B
    row = lax.broadcasted_iota(jnp.int32, (B, B), 0)
    col = lax.broadcasted_iota(jnp.int32, (B, B), 1)
    for slot in range(slots):
        d_a = meta_ref[3 * slot]
        d_b = meta_ref[3 * slot + 1]
        d_c = meta_ref[3 * slot + 2]
        visit = meta_ref[6 * slots + 1 + slot]
        per_box = box_refs[0].shape[0]
        part = box_refs[0][0, 0:B, :]
        for index in range(1, len(box_refs) * per_box):
            part = jnp.where(
                visit == index, box_refs[index // per_box][index % per_box, 0:B, :], part
            )
        pick = (col == row + d_a).astype(jnp.bfloat16)
        moved = jnp.dot(pick, part, preferred_element_type=jnp.float32)
        step = d_b * B + d_c
        moved = pltpu.roll(moved, (PLANE - step) % PLANE, 1)
        inside = (
            (lane_b + d_b >= 0) & (lane_b + d_b < B) & (lane_c + d_c >= 0) & (lane_c + d_c < B)
        )
        moved = jnp.where(inside, moved, 0.0)
        shifted_ref[slot] = moved
        work_ref[slot * B : (slot + 1) * B, :] = home_ref[slot].astype(jnp.float32) * moved

    kron_high = kron_high_ref[...]
    kron_low = kron_low_ref[...]
    rows_high = rows_high_ref[...]
    rows_low = rows_low_ref[...]
    coef = dot3_left(rows_high, rows_low, dot3(work_ref[...], kron_high, kron_low))
    eigen = eigen_ref[...]
    for slot in range(slots):
        work_ref[slot * B : (slot + 1) * B, :] = coef[slot * B : (slot + 1) * B, :] / eigen
    potential = dot3_left(rows_high, rows_low, dot3(work_ref[...], kron_high, kron_low))

    for slot in range(slots):
        d_a = meta_ref[3 * slot]
        d_b = meta_ref[3 * slot + 1]
        d_c = meta_ref[3 * slot + 2]
        live = meta_ref[3 * slots + slot] > 0
        here = potential[slot * B : (slot + 1) * B, :]
        tag_home = jnp.full((1, 128), meta_ref[4 * slots + slot].astype(jnp.float32))
        tag_part = jnp.full((1, 128), meta_ref[5 * slots + slot].astype(jnp.float32))
        emit(payload_ref, stage_ref, slot, jnp.where(live, here * shifted_ref[slot], 0.0), tag_home, me)
        product = here * home_ref[slot].astype(jnp.float32)
        pick = (col == row - d_a).astype(jnp.bfloat16)
        moved = exact_rows(pick, product)
        step = d_b * B + d_c
        moved = pltpu.roll(moved, (PLANE + step) % PLANE, 1)
        inside = (
            (lane_b - d_b >= 0) & (lane_b - d_b < B) & (lane_c - d_c >= 0) & (lane_c - d_c < B)
        )
        emit(
            payload_ref, stage_ref, slots + slot, jnp.where(live & inside, moved, 0.0), tag_part, me
        )


def pair_fields(meta, home, boxes, count, chunk):
    slots = home.shape[0]
    tiled, spread, rows_high, rows_low, eigen = host_tables(slots)
    smem = pl.BlockSpec(memory_space=pltpu.SMEM)
    vmem = pl.BlockSpec(memory_space=pltpu.VMEM)
    box = jax.ShapeDtypeStruct((2 * slots, chunk + 128), jnp.float32)
    return pl.pallas_call(
        functools.partial(pair_kernel, count, len(boxes)),
        out_shape=tuple([box] * count),
        in_specs=[smem] + [vmem] * (6 + len(boxes)),
        out_specs=tuple([vmem] * count),
        scratch_shapes=[
            pltpu.VMEM((slots, B, PLANE), jnp.float32),
            pltpu.VMEM((slots * B, PLANE), jnp.float32),
            pltpu.VMEM((PLANE, PLANE), jnp.bfloat16),
            pltpu.VMEM((PLANE, PLANE), jnp.bfloat16),
            pltpu.VMEM((B, PLANE), jnp.float32),
        ],
    )(meta, home, *boxes, tiled, spread, rows_high, rows_low, eigen)


def exchange(blocks, axis):
    count = len(blocks)
    received = [blocks[0]]
    for step in range(1, count):
        pairs = [(source, (source + step) % count) for source in range(count)]
        received.append(lax.ppermute(blocks[step], axis, pairs))
    return received


def pick_rows(indices, table):
    chooser = (indices[:, None] == jnp.arange(table.shape[0], dtype=jnp.int32)[None, :])
    return jnp.dot(chooser.astype(jnp.float32), table.astype(jnp.float32), precision=PRECISE)


def per_device(orbitals, offsets, sends, pair_home, pair_visit, pair_count):
    home_count = orbitals.shape[0]
    cell_count = orbitals.shape[1]
    section_total = sends.shape[1]
    per_target = sends.shape[2]
    slot_total = section_total * per_target
    slots = pair_home.shape[2]
    extra = 128
    me = lax.axis_index("home")
    chosen = lax.dynamic_slice_in_dim(jnp.concatenate([sends[0], sends[0]]), me, section_total)
    flat_chosen = chosen.reshape(-1)
    outgoing = jnp.concatenate(
        [
            orbitals[flat_chosen].reshape(slot_total, B, PLANE),
            jnp.pad(
                pick_rows(flat_chosen, offsets).astype(jnp.bfloat16), ((0, 0), (0, PLANE - 3))
            )[:, None, :],
        ],
        axis=1,
    ).reshape(section_total, per_target, B + 1, PLANE)
    visitors = exchange(outgoing, "home")
    visit_offsets = jnp.stack([block[:, B, 0:3] for block in visitors]).reshape(slot_total, 3)

    home_slot = pair_home[0, 0]
    visit_code = pair_visit[0, 0]
    source = visit_code // per_target
    visit_slot = ((me - source) % section_total) * per_target + visit_code % per_target
    return_slot = ((source - me) % section_total) * per_target + visit_code % per_target
    live = (jnp.arange(slots, dtype=jnp.int32) < pair_count[0, 0]).astype(jnp.int32)
    home_orb = orbitals[home_slot].reshape(slots, B, PLANE)
    delta = (pick_rows(home_slot, offsets) - pick_rows(visit_slot, visit_offsets)).astype(jnp.int32)
    pair_total = lax.psum(1, "pair")
    chunk = cell_count // pair_total
    pair_me = lax.axis_index("pair")
    meta = jnp.concatenate(
        [
            delta.reshape(-1),
            live,
            home_slot,
            home_count + return_slot,
            jnp.reshape(pair_me, (1,)).astype(jnp.int32),
            visit_slot,
        ]
    )
    payload = pair_fields(meta, home_orb, visitors, pair_total, chunk)
    got = jnp.stack(exchange(payload, "pair"))
    got_ids = got[:, :, chunk].astype(jnp.int32)
    all_rows = jnp.arange(home_count + slot_total, dtype=jnp.int32)
    picker = (got_ids[:, :, None] == all_rows[None, None, :]).astype(jnp.float32)
    totals = jnp.einsum("srk,srl->kl", picker, got[:, :, :chunk], precision=lax.Precision.HIGH)
    home_totals = totals[:home_count]
    back = (-jnp.arange(section_total, dtype=jnp.int32)) % section_total
    visit_totals = totals[home_count:].reshape(section_total, per_target, chunk)
    returned = jnp.stack(exchange(visit_totals, "home")).reshape(slot_total, chunk)
    owners = chosen[back].reshape(-1)
    chooser = (owners[:, None] == jnp.arange(home_count, dtype=jnp.int32)[None, :]).astype(
        jnp.float32
    )
    return home_totals + jnp.dot(chooser.T, returned, precision=lax.Precision.HIGH)


def solution(mesh):
    in_specs = (
        P("home", None),
        P("home", None),
        P("home", None, None),
        P("home", "pair", None),
        P("home", "pair", None),
        P("home", "pair"),
    )
    out_specs = P("home", "pair")
    return jax.shard_map(
        per_device, mesh=mesh, in_specs=in_specs, out_specs=out_specs, check_vma=False
    )
```
